128 devices in a mesh: row: 16 (over y_lo, x, core), col: 8 (over z, y_hi).
Axes of the slice: x: 4, y: 4 (y_hi: 2, y_lo: 2; y = y_hi * 2 + y_lo), z: 4, core: 2. Of those that a mesh axis runs over, the one named last changes fastest.
Arguments:
- gate_feats: bfloat16 [16, 8, 1024, 256], P('row', 'col'), may hold values from -6 to 6
- adjacency: int32 [16, 8, 8, 5, 128, 128], P('row', 'col'), may hold values 0 or 1
- gate_count: int32 [16, 8], P('row', 'col'), may hold values from 128 to 1024, as said below
- membership: int32 [16, 8, 512, 1024], P('row', 'col'), may hold values 0 or 1
- tok_count: int32 [16, 8], P('row', 'col'), may hold values from 64 to 512, as said below
- w_msg: bfloat16 [256, 256], replicated, may hold values from -0.375 to 0.375
- w_query: bfloat16 [256, 256], replicated, may hold values from -0.375 to 0.375
- w_key: bfloat16 [256, 256], replicated, may hold values from -0.375 to 0.375
- w_value: bfloat16 [256, 256], replicated, may hold values from -0.375 to 0.375
- w_out: bfloat16 [256, 256], replicated, may hold values from -0.375 to 0.375
- w_score: bfloat16 [256], replicated, may hold values from -0.375 to 0.375
- cotangent: float32 [16, 8, 512], P('row', 'col'), may hold values from -6 to 6
Outputs:
- value_out: float32 [16, 8, 512], P('row', 'col')
- g_msg: float32 [256, 256], replicated
- g_query: float32 [256, 256], replicated
- g_key: float32 [256, 256], replicated
- g_value: float32 [256, 256], replicated
- g_out: float32 [256, 256], replicated
- g_score: float32 [256], replicated
The draws below stay inside these ranges and needn't reach their ends.
Inputs may be any that keep to these rules, and one draw needn't show every extreme that they name: `gate_count`: some tile is full in every draw. `tok_count`: some tile is full in every draw.
All inputs are finite; a program needn't handle non-finite values. No bound on the sum of `adjacency` or of `membership` on one device may be relied on, other than what follows from the above.
Results may differ from the reference program's by a relative error of at most 0.017.
Values may be sent and summed in bfloat16 or wider, within the bound.
No kernel may reach another device: no remote copies, remote signals or barrier semaphores. Data moves between devices by JAX's collectives and lax.ppermute only.
A program may use at most 128 MiB of HBM per device.

```python
import math
import jax
import jax.numpy as jnp
from jax import lax

H = 256
HEADS = 2
HD = 128
BLK = 128
NB = 8
NT = 512
G = 1024
TROWS = 16
TCOLS = 8


def full_counts(key, most):
    counts = jax.random.randint(key, (TROWS * TCOLS,), most // 8, most + 1)
    chosen = jax.random.randint(jax.random.fold_in(key, 7), (), 0, TROWS * TCOLS)
    counts = counts.at[chosen].set(most)
    return counts.reshape(TROWS, TCOLS).astype(jnp.int32)


def draw_gate_count(key, part):
    return full_counts(jax.random.fold_in(key, 11), G)


def draw_tok_count(key, part):
    return full_counts(jax.random.fold_in(key, 23), NT)


def with_ends(array, own_key, low, top_value):
    spot = [jax.random.randint(jax.random.fold_in(own_key, axis), (), 0, length) for axis, length in enumerate(array.shape)]
    main_axis = array.shape.index(max(array.shape))
    beside = spot[:main_axis] + [(spot[main_axis] + 1) % array.shape[main_axis]] + spot[main_axis + 1:]
    return array.at[tuple(spot)].set(low).at[tuple(beside)].set(top_value)


def levels(rng, shape, shards, low, high):
    def one(axis_at, parts):
        heights = jax.random.uniform(jax.random.fold_in(jax.random.fold_in(rng, 6), axis_at), (parts,), jnp.float32, low / len(shards), high / len(shards))
        return jnp.repeat(jnp.exp(heights), shape[axis_at] // parts).reshape((-1,) + (1,) * (len(shape) - axis_at - 1))

    factor_of = one(*shards[0])
    for cut in shards[1:]:
        factor_of = factor_of * one(*cut)
    return factor_of


def normal_values(stream_key, shape, scale, most, split=(), held_as=jnp.bfloat16):
    gain = levels(stream_key, shape, split, -0.22, 0.18) if split else 1.0
    array = jax.random.normal(stream_key, shape, jnp.float32) * scale * gain
    return jnp.minimum(jnp.maximum(array, -most), most).astype(held_as)


def setup_inputs(seed: int = 0) -> dict:
    key_of = jax.random.split(jax.random.key(seed), 13)
    gate_feats = normal_values(key_of[0], (TROWS, TCOLS, G, H), 1.0, 6.0, ((0, 16), (1, 8)))
    adjacency = with_ends((jax.random.randint(key_of[1], (TROWS, TCOLS, NB, 5, BLK, BLK), 0, 16) < 1).astype(jnp.int32), jax.random.fold_in(key_of[1], 1), 0, 1)
    gate_count = draw_gate_count(jax.random.fold_in(key_of[12], 71), 0)
    membership = with_ends((jax.random.randint(key_of[3], (TROWS, TCOLS, NT, G), 0, 32) < 1).astype(jnp.int32), jax.random.fold_in(key_of[3], 1), 0, 1)
    tok_count = draw_tok_count(jax.random.fold_in(key_of[12], 71), 0)
    w_msg = normal_values(key_of[5], (H, H), H ** -0.5, 0.375)
    w_query = normal_values(key_of[6], (H, H), H ** -0.5, 0.375)
    w_key = normal_values(key_of[7], (H, H), H ** -0.5, 0.375)
    w_value = normal_values(key_of[8], (H, H), H ** -0.5, 0.375)
    w_out = normal_values(key_of[9], (H, H), H ** -0.5, 0.375)
    w_score = normal_values(key_of[10], (H,), H ** -0.5, 0.375)
    cotangent = normal_values(key_of[11], (TROWS, TCOLS, NT), 1.0, 6.0, ((0, 16), (1, 8)), jnp.float32)
    return dict(gate_feats=gate_feats, adjacency=adjacency, gate_count=gate_count, membership=membership, tok_count=tok_count, w_msg=w_msg, w_query=w_query, w_key=w_key, w_value=w_value, w_out=w_out, w_score=w_score, cotangent=cotangent)


EPS = 1e-06

def silu_grad(preact):
    sigmoid_val = jax.nn.sigmoid(preact)
    return sigmoid_val * (1.0 + preact * (1.0 - sigmoid_val))

def rms_forward(values_in):
    rscale = lax.rsqrt(lax.optimization_barrier(jnp.mean(values_in * values_in, axis=-1, keepdims=True)) + EPS)
    return (values_in * rscale, rscale)

def rms_backward(grad_in, normed, rscale):
    return rscale * (grad_in - normed * lax.optimization_barrier(jnp.mean(grad_in * normed, axis=-1, keepdims=True)))

def split_heads(rows_in):
    return rows_in.astype(jnp.float32).reshape(rows_in.shape[0], HEADS, HD)

def score_probs(query_rows, key_rows):
    scores = jnp.einsum('qhd,khd->hqk', split_heads(query_rows), split_heads(key_rows))
    return jax.nn.sigmoid(scores / math.sqrt(HD) - math.log(NT))

def attend(query_rows, key_rows, value_rows):
    weights = lax.optimization_barrier(score_probs(query_rows, key_rows).astype(jnp.bfloat16)).astype(jnp.float32)
    output = jnp.einsum('hqk,khd->qhd', weights, split_heads(value_rows))
    return output.reshape(query_rows.shape[0], H).astype(jnp.bfloat16)

def attend_grads(query_rows, grad_rows, key_rows, value_rows):
    probs_val = score_probs(query_rows, key_rows)
    weights = lax.optimization_barrier(probs_val.astype(jnp.bfloat16)).astype(jnp.float32)
    grad_prob = jnp.einsum('qhd,khd->hqk', split_heads(grad_rows), split_heads(value_rows))
    grad_score = grad_prob * probs_val * (1.0 - probs_val) / math.sqrt(HD)
    grad_score = lax.optimization_barrier(grad_score.astype(jnp.bfloat16)).astype(jnp.float32)
    grad_query = jnp.einsum('hqk,khd->qhd', grad_score, split_heads(key_rows)).reshape(query_rows.shape[0], H)
    grad_key = jnp.einsum('hqk,qhd->khd', grad_score, split_heads(query_rows)).reshape(key_rows.shape[0], H)
    grad_val = jnp.einsum('hqk,qhd->khd', weights, split_heads(grad_rows)).reshape(key_rows.shape[0], H)
    return (grad_query, grad_key, grad_val)

def reference(gate_feats, adjacency, gate_count, membership, tok_count, w_msg, w_query, w_key, w_value, w_out, w_score, cotangent):
    gate_live = (jnp.arange(G)[None, None, :] < gate_count[:, :, None]).astype(jnp.float32)
    live_feats = (gate_feats.astype(jnp.float32) * gate_live[..., None]).astype(jnp.bfloat16)
    padded = jnp.pad(live_feats, ((1, 1), (1, 1), (0, 0), (0, 0)))

    def tile_row(row_idx):
        near = lax.dynamic_slice_in_dim(padded, row_idx, 3, 0)
        sources = jnp.stack([near[1, 1:-1], near[0, 1:-1], near[2, 1:-1], near[1, :-2], near[1, 2:]], axis=1)
        sources = sources.reshape(TCOLS, 5, NB, BLK, H).astype(jnp.float32)
        adj_tiles = lax.dynamic_index_in_dim(adjacency, row_idx, 0, keepdims=False).astype(jnp.float32)
        aggregate = jnp.einsum('cbkij,ckbjh->cbih', adj_tiles, sources)
        degree = lax.optimization_barrier(jnp.sum(adj_tiles, axis=(2, 4)))
        message = (aggregate / (degree[..., None] + 1.0)).astype(jnp.bfloat16).reshape(TCOLS, G, H)
        preact = jnp.dot(message, w_msg, preferred_element_type=jnp.float32)
        live_row = lax.dynamic_index_in_dim(gate_live, row_idx, 0, keepdims=False)
        feat_row = lax.dynamic_index_in_dim(live_feats, row_idx, 0, keepdims=False)
        hidden = (live_row[..., None] * (feat_row.astype(jnp.float32) + jax.nn.silu(preact))).astype(jnp.bfloat16)
        member_rows = lax.dynamic_index_in_dim(membership, row_idx, 0, keepdims=False).astype(jnp.float32)
        member_count = lax.optimization_barrier(jnp.sum(member_rows, axis=-1, keepdims=True))
        pooled = jnp.einsum('cng,cgh->cnh', member_rows, hidden.astype(jnp.float32)) / (member_count + 1.0)
        return (message, preact, pooled, member_count)
    message, preact, pooled, member_count = lax.map(tile_row, jnp.arange(TROWS))
    normed, rscale = rms_forward(pooled)
    token_live = (jnp.arange(NT)[None, None, :] < tok_count[:, :, None]).astype(jnp.float32)
    tokens = (token_live[..., None] * normed).astype(jnp.bfloat16)
    query = jnp.dot(tokens, w_query, preferred_element_type=jnp.float32).astype(jnp.bfloat16)
    key = jnp.dot(tokens, w_key, preferred_element_type=jnp.float32).astype(jnp.bfloat16)
    value = jnp.dot(tokens, w_value, preferred_element_type=jnp.float32).astype(jnp.bfloat16)

    def attend_row(row_idx):
        key_all = lax.dynamic_index_in_dim(key, row_idx, 0, keepdims=False).reshape(TCOLS * NT, H)
        value_all = lax.dynamic_index_in_dim(value, row_idx, 0, keepdims=False).reshape(TCOLS * NT, H)
        query_row = lax.dynamic_index_in_dim(query, row_idx, 0, keepdims=False)
        return lax.map(lambda query_rows: attend(query_rows, key_all, value_all), query_row)
    attended = lax.map(attend_row, jnp.arange(TROWS))
    proj = jnp.dot(attended, w_out, preferred_element_type=jnp.float32)
    pnormed, pscale = rms_forward(proj)
    mixed = tokens.astype(jnp.float32) + pnormed
    score_w = w_score.astype(jnp.float32)
    value_out = token_live * lax.optimization_barrier(jnp.sum(mixed * score_w, axis=-1))
    grad_value = token_live * cotangent / math.sqrt(TROWS * TCOLS * NT)
    g_score = jnp.einsum('rcn,rcnh->h', grad_value, mixed)
    grad_mixed = grad_value[..., None] * score_w
    grad_proj = rms_backward(grad_mixed, pnormed, pscale).astype(jnp.bfloat16)
    g_out = jnp.einsum('rcnh,rcne->he', attended.astype(jnp.float32), grad_proj.astype(jnp.float32))
    grad_attn = jnp.dot(grad_proj, w_out.T, preferred_element_type=jnp.float32).astype(jnp.bfloat16)

    def grads_row(row_idx):
        key_all = lax.dynamic_index_in_dim(key, row_idx, 0, keepdims=False).reshape(TCOLS * NT, H)
        value_all = lax.dynamic_index_in_dim(value, row_idx, 0, keepdims=False).reshape(TCOLS * NT, H)
        query_row = lax.dynamic_index_in_dim(query, row_idx, 0, keepdims=False)
        grad_row = lax.dynamic_index_in_dim(grad_attn, row_idx, 0, keepdims=False)

        def per_tile(totals, tile_pair):
            grad_q, grad_k, grad_v = attend_grads(tile_pair[0], tile_pair[1], key_all, value_all)
            return ((totals[0] + grad_k, totals[1] + grad_v), grad_q)
        zero_rows = jnp.zeros((TCOLS * NT, H), jnp.float32)
        sums, grad_q_row = lax.scan(per_tile, (zero_rows, zero_rows), (query_row, grad_row))
        return (grad_q_row, sums[0].reshape(TCOLS, NT, H), sums[1].reshape(TCOLS, NT, H))
    grad_query, grad_key, grad_val = lax.map(grads_row, jnp.arange(TROWS))
    grad_query = grad_query.astype(jnp.bfloat16)
    grad_key = grad_key.astype(jnp.bfloat16)
    grad_val = grad_val.astype(jnp.bfloat16)
    tokens_f = tokens.astype(jnp.float32)
    g_query = jnp.einsum('rcnh,rcne->he', tokens_f, grad_query.astype(jnp.float32))
    g_key = jnp.einsum('rcnh,rcne->he', tokens_f, grad_key.astype(jnp.float32))
    g_value = jnp.einsum('rcnh,rcne->he', tokens_f, grad_val.astype(jnp.float32))
    grad_tokens = grad_mixed + jnp.dot(grad_query, w_query.T, preferred_element_type=jnp.float32)
    grad_tokens = grad_tokens + jnp.dot(grad_key, w_key.T, preferred_element_type=jnp.float32)
    grad_tokens = grad_tokens + jnp.dot(grad_val, w_value.T, preferred_element_type=jnp.float32)
    grad_pooled = rms_backward(token_live[..., None] * grad_tokens, normed, rscale)
    grad_scaled = (grad_pooled / (member_count + 1.0)).astype(jnp.bfloat16)

    def msg_row(row_idx):
        member_rows = lax.dynamic_index_in_dim(membership, row_idx, 0, keepdims=False).astype(jnp.float32)
        scaled_row = lax.dynamic_index_in_dim(grad_scaled, row_idx, 0, keepdims=False).astype(jnp.float32)
        grad_hidden = jnp.einsum('cng,cnh->cgh', member_rows, scaled_row)
        live_row = lax.dynamic_index_in_dim(gate_live, row_idx, 0, keepdims=False)
        pre_row = lax.dynamic_index_in_dim(preact, row_idx, 0, keepdims=False)
        grad_pre = (live_row[..., None] * grad_hidden * silu_grad(pre_row)).astype(jnp.bfloat16)
        msg_row_vals = lax.dynamic_index_in_dim(message, row_idx, 0, keepdims=False)
        return jnp.einsum('cgh,cge->he', msg_row_vals.astype(jnp.float32), grad_pre.astype(jnp.float32))
    g_msg = lax.optimization_barrier(jnp.sum(lax.map(msg_row, jnp.arange(TROWS)), axis=0))
    return (value_out, g_msg, g_query, g_key, g_value, g_out, g_score)
```

```python
import math

import jax
import jax.numpy as jnp
from jax import lax
from jax.sharding import PartitionSpec as P

H = 256
HEADS = 2
HD = 128
BLK = 128
NB = 8
NT = 512


EPS = 1e-06


def with_halo(array, sides, width):
    for axis, dim in sides:
        size, length = (lax.axis_size(axis), array.shape[dim])
        up = [(i, (i + 1) % size) for i in range(size - 1)]
        down = [(j, i) for i, j in up]
        last = lax.slice_in_dim(array, length - width, length, axis=dim)
        first = lax.slice_in_dim(array, 0, width, axis=dim)
        before = lax.ppermute(last, axis, up)
        after = lax.ppermute(first, axis, down)
        array = jnp.concatenate([before, array, after], axis=dim)
    return array


def gather_shifted(rows_in, axis):
    size = lax.axis_size(axis)
    parts = [rows_in]
    for shift in range(1, size):
        parts.append(lax.ppermute(rows_in, axis, [(i, (i + shift) % size) for i in range(size)]))
    return jnp.stack(parts)


def reduce_scatter_direct(flat, axis):
    size = lax.axis_size(axis)
    own = lax.axis_index(axis)
    chunks = flat.reshape(size, -1)
    total = lax.dynamic_index_in_dim(chunks, own, 0, keepdims=False)
    for shift in range(1, size):
        piece = lax.dynamic_index_in_dim(chunks, (own + shift) % size, 0, keepdims=False)
        total = total + lax.ppermute(piece, axis, [(i, (i + shift) % size) for i in range(size)])
    return total


def all_gather_direct(chunk, axis):
    size = lax.axis_size(axis)
    own = lax.axis_index(axis)
    stacked = gather_shifted(chunk, axis)
    order = (own - jnp.arange(size)) % size
    return jnp.take(stacked, order, axis=0).reshape(-1)


def all_reduce_direct(flat):
    part = reduce_scatter_direct(flat, "col")
    part = reduce_scatter_direct(part, "row")
    part = all_gather_direct(part, "row")
    return all_gather_direct(part, "col")


def silu_grad(preact):
    sigmoid_val = jax.nn.sigmoid(preact)
    return sigmoid_val * (1.0 + preact * (1.0 - sigmoid_val))


def rms_forward(values_in):
    rscale = lax.rsqrt(jnp.mean(values_in * values_in, axis=-1, keepdims=True) + EPS)
    return (values_in * rscale, rscale)


def rms_backward(grad_in, normed, rscale):
    return rscale * (grad_in - normed * jnp.mean(grad_in * normed, axis=-1, keepdims=True))


def split_heads(rows_in):
    return rows_in.reshape(rows_in.shape[0], HEADS, HD)


def score_probs(query_rows, key_rows):
    scores = jnp.einsum(
        "qhd,khd->hqk",
        split_heads(query_rows),
        split_heads(key_rows),
        preferred_element_type=jnp.float32,
    )
    return jax.nn.sigmoid(scores / math.sqrt(HD) - math.log(NT))


def project(rows_in, weight_mat):
    return jnp.dot(rows_in, weight_mat, preferred_element_type=jnp.float32).astype(jnp.bfloat16)


def body(
    gate_feats,
    adjacency,
    gate_count,
    membership,
    tok_count,
    w_msg,
    w_query,
    w_key,
    w_value,
    w_out,
    w_score,
    cotangent,
):
    gate_total = gate_feats.shape[2]
    gate_live = (jnp.arange(gate_total) < gate_count[0, 0]).astype(jnp.float32)
    live_feats = (gate_feats[0, 0].astype(jnp.float32) * gate_live[:, None]).astype(jnp.bfloat16)
    padded = with_halo(live_feats[None, None], (("row", 0), ("col", 1)), 1)
    sources = jnp.stack(
        [padded[1, 1], padded[0, 1], padded[2, 1], padded[1, 0], padded[1, 2]], axis=0
    )
    sources = sources.reshape(5, NB, BLK, H)
    adj_tiles = adjacency[0, 0]
    aggregate = jnp.einsum(
        "bkij,kbjh->bih",
        adj_tiles.astype(jnp.bfloat16),
        sources,
        preferred_element_type=jnp.float32,
    )
    degree = jnp.sum(adj_tiles, axis=(1, 3)).astype(jnp.float32)
    message = (aggregate / (degree[:, :, None] + 1.0)).astype(jnp.bfloat16).reshape(gate_total, H)
    preact = jnp.dot(message, w_msg, preferred_element_type=jnp.float32)
    hidden = (gate_live[:, None] * (live_feats.astype(jnp.float32) + jax.nn.silu(preact))).astype(
        jnp.bfloat16
    )
    member_rows = membership[0, 0].astype(jnp.bfloat16)
    member_count = jnp.sum(membership[0, 0], axis=1).astype(jnp.float32)[:, None]
    pooled = jnp.dot(member_rows, hidden, preferred_element_type=jnp.float32) / (member_count + 1.0)
    normed, rscale = rms_forward(pooled)
    token_live = (jnp.arange(NT) < tok_count[0, 0]).astype(jnp.float32)[:, None]
    tokens = (token_live * normed).astype(jnp.bfloat16)

    tokens_all = gather_shifted(tokens, "col").reshape(-1, H)
    query_all = project(tokens_all, w_query)
    key_all = project(tokens_all, w_key)
    value_all = project(tokens_all, w_value)
    query_own = query_all[:NT]
    key_own = key_all[:NT]
    value_own = value_all[:NT]

    probs_own = score_probs(query_own, key_all)
    weights_own = probs_own.astype(jnp.bfloat16)
    attended = jnp.einsum(
        "hqk,khd->qhd", weights_own, split_heads(value_all), preferred_element_type=jnp.float32
    )
    attended = attended.reshape(NT, H).astype(jnp.bfloat16)
    proj = jnp.dot(attended, w_out, preferred_element_type=jnp.float32)
    pnormed, pscale = rms_forward(proj)
    mixed = tokens.astype(jnp.float32) + pnormed
    score_w = w_score.astype(jnp.float32)
    value_out = token_live[:, 0] * jnp.sum(mixed * score_w, axis=1)
    loss_weight = 1.0 / math.sqrt(lax.axis_size("row") * lax.axis_size("col") * NT)
    grad_value = token_live[:, 0] * cotangent[0, 0] * loss_weight
    g_score = jnp.sum(mixed * grad_value[:, None], axis=0)
    grad_mixed = grad_value[:, None] * score_w
    grad_proj = rms_backward(grad_mixed, pnormed, pscale).astype(jnp.bfloat16)
    g_out = jnp.einsum("nh,ne->he", attended, grad_proj, preferred_element_type=jnp.float32)
    grad_attn = jnp.dot(grad_proj, w_out.T, preferred_element_type=jnp.float32).astype(jnp.bfloat16)

    grad_attn_all = gather_shifted(grad_attn, "col").reshape(-1, H)

    grad_prob_q = jnp.einsum(
        "qhd,khd->hqk", split_heads(grad_attn), split_heads(value_all),
        preferred_element_type=jnp.float32,
    )
    grad_score_q = (grad_prob_q * probs_own * (1.0 - probs_own) / math.sqrt(HD)).astype(jnp.bfloat16)
    grad_query = jnp.einsum(
        "hqk,khd->qhd", grad_score_q, split_heads(key_all), preferred_element_type=jnp.float32
    ).reshape(NT, H).astype(jnp.bfloat16)

    probs_key = score_probs(query_all, key_own)
    weights_key = probs_key.astype(jnp.bfloat16)
    grad_prob_k = jnp.einsum(
        "qhd,khd->hqk", split_heads(grad_attn_all), split_heads(value_own),
        preferred_element_type=jnp.float32,
    )
    grad_score_k = (grad_prob_k * probs_key * (1.0 - probs_key) / math.sqrt(HD)).astype(jnp.bfloat16)
    grad_key = jnp.einsum(
        "hqk,qhd->khd", grad_score_k, split_heads(query_all), preferred_element_type=jnp.float32
    ).reshape(NT, H).astype(jnp.bfloat16)
    grad_val = jnp.einsum(
        "hqk,qhd->khd", weights_key, split_heads(grad_attn_all), preferred_element_type=jnp.float32
    ).reshape(NT, H).astype(jnp.bfloat16)

    g_query = jnp.einsum("nh,ne->he", tokens, grad_query, preferred_element_type=jnp.float32)
    g_key = jnp.einsum("nh,ne->he", tokens, grad_key, preferred_element_type=jnp.float32)
    g_value = jnp.einsum("nh,ne->he", tokens, grad_val, preferred_element_type=jnp.float32)
    grad_tokens = grad_mixed + jnp.dot(grad_query, w_query.T, preferred_element_type=jnp.float32)
    grad_tokens = grad_tokens + jnp.dot(grad_key, w_key.T, preferred_element_type=jnp.float32)
    grad_tokens = grad_tokens + jnp.dot(grad_val, w_value.T, preferred_element_type=jnp.float32)
    grad_pooled = rms_backward(token_live * grad_tokens, normed, rscale)
    grad_scaled = (grad_pooled / (member_count + 1.0)).astype(jnp.bfloat16)
    grad_hidden = jnp.einsum(
        "ng,nh->gh", member_rows, grad_scaled, preferred_element_type=jnp.float32
    )
    grad_pre = (gate_live[:, None] * grad_hidden * silu_grad(preact)).astype(jnp.bfloat16)
    g_msg = jnp.einsum("gh,ge->he", message, grad_pre, preferred_element_type=jnp.float32)

    flat = jnp.concatenate(
        [g.reshape(-1) for g in (g_msg, g_query, g_key, g_value, g_out, g_score)]
    )
    devices = lax.axis_size("row") * lax.axis_size("col")
    pad = (-flat.shape[0]) % devices
    summed = all_reduce_direct(jnp.pad(flat, (0, pad)))
    sq = H * H
    outs = [summed[i * sq:(i + 1) * sq].reshape(H, H) for i in range(5)]
    g_score_sum = summed[5 * sq:5 * sq + H]
    return (value_out[None, None], *outs, g_score_sum)


def solution(mesh):
    placed = (
        P("row", "col", None, None),
        P("row", "col", None, None, None, None),
        P("row", "col"),
        P("row", "col", None, None),
        P("row", "col"),
        P(),
        P(),
        P(),
        P(),
        P(),
        P(),
        P("row", "col", None),
    )
    return jax.shard_map(
        body,
        mesh=mesh,
        in_specs=placed,
        out_specs=(P("row", "col", None), P(), P(), P(), P(), P(), P()),
        check_vma=False,
    )
```

```python
import math

import jax
import jax.numpy as jnp
from jax import lax
from jax.sharding import PartitionSpec as P

H = 256
HEADS = 2
HD = 128
BLK = 128
NB = 8
NT = 512


EPS = 1e-06


def with_halo(array, sides, width):
    for axis, dim in sides:
        size, length = (lax.axis_size(axis), array.shape[dim])
        up = [(i, (i + 1) % size) for i in range(size - 1)]
        down = [(j, i) for i, j in up]
        last = lax.slice_in_dim(array, length - width, length, axis=dim)
        first = lax.slice_in_dim(array, 0, width, axis=dim)
        before = lax.ppermute(last, axis, up)
        after = lax.ppermute(first, axis, down)
        array = jnp.concatenate([before, array, after], axis=dim)
    return array


def gather_tiles(rows_in, axis):
    size = lax.axis_size(axis)
    copies = jnp.broadcast_to(rows_in[None], (size,) + rows_in.shape)
    return lax.all_to_all(copies, axis, 0, 0, tiled=True)


def all_reduce_a2a(flat, axes):
    size = 1
    for axis in axes:
        size *= lax.axis_size(axis)
    chunks = lax.all_to_all(flat.reshape(size, -1), axes, 0, 0, tiled=True)
    total = jnp.sum(chunks, axis=0, keepdims=True)
    copies = jnp.broadcast_to(total, chunks.shape)
    return lax.all_to_all(copies, axes, 0, 0, tiled=True).reshape(-1)


def silu_grad(preact):
    sigmoid_val = jax.nn.sigmoid(preact)
    return sigmoid_val * (1.0 + preact * (1.0 - sigmoid_val))


def rms_forward(values_in):
    rscale = lax.rsqrt(jnp.mean(values_in * values_in, axis=-1, keepdims=True) + EPS)
    return (values_in * rscale, rscale)


def rms_backward(grad_in, normed, rscale):
    return rscale * (grad_in - normed * jnp.mean(grad_in * normed, axis=-1, keepdims=True))


def split_heads(rows_in):
    return rows_in.reshape(rows_in.shape[0], HEADS, HD)


def score_probs(query_rows, key_rows):
    scores = jnp.einsum(
        "qhd,khd->hqk",
        split_heads(query_rows),
        split_heads(key_rows),
        preferred_element_type=jnp.float32,
    )
    return jax.nn.sigmoid(scores / math.sqrt(HD) - math.log(NT))


def project(rows_in, weight_mat):
    return jnp.dot(rows_in, weight_mat, preferred_element_type=jnp.float32).astype(jnp.bfloat16)


def body(
    gate_feats,
    adjacency,
    gate_count,
    membership,
    tok_count,
    w_msg,
    w_query,
    w_key,
    w_value,
    w_out,
    w_score,
    cotangent,
):
    gate_total = gate_feats.shape[2]
    gate_live = (jnp.arange(gate_total) < gate_count[0, 0]).astype(jnp.float32)
    live_feats = (gate_feats[0, 0].astype(jnp.float32) * gate_live[:, None]).astype(jnp.bfloat16)
    by_row = with_halo(live_feats[None], (("row", 0),), 1)
    by_col = with_halo(live_feats[None], (("col", 0),), 1)
    sources = jnp.stack([live_feats, by_row[0], by_row[2], by_col[0], by_col[2]], axis=0)
    sources = sources.reshape(5, NB, BLK, H)
    adj_tiles = adjacency[0, 0]
    aggregate = jnp.einsum(
        "bkij,kbjh->bih",
        adj_tiles.astype(jnp.bfloat16),
        sources,
        preferred_element_type=jnp.float32,
    )
    degree = jnp.sum(adj_tiles, axis=(1, 3)).astype(jnp.float32)
    message = (aggregate / (degree[:, :, None] + 1.0)).astype(jnp.bfloat16).reshape(gate_total, H)
    preact = jnp.dot(message, w_msg, preferred_element_type=jnp.float32)
    hidden = (gate_live[:, None] * (live_feats.astype(jnp.float32) + jax.nn.silu(preact))).astype(
        jnp.bfloat16
    )
    member_rows = membership[0, 0].astype(jnp.bfloat16)
    member_count = jnp.sum(membership[0, 0], axis=1).astype(jnp.float32)[:, None]
    pooled = jnp.dot(member_rows, hidden, preferred_element_type=jnp.float32) / (member_count + 1.0)
    normed, rscale = rms_forward(pooled)
    token_live = (jnp.arange(NT) < tok_count[0, 0]).astype(jnp.float32)[:, None]
    tokens = (token_live * normed).astype(jnp.bfloat16)

    tokens_all = gather_tiles(tokens, "col").reshape(-1, H)
    query_all = project(tokens_all, w_query)
    key_all = project(tokens_all, w_key)
    value_all = project(tokens_all, w_value)
    query_own = project(tokens, w_query)
    key_own = project(tokens, w_key)
    value_own = project(tokens, w_value)

    probs_own = score_probs(query_own, key_all)
    weights_own = probs_own.astype(jnp.bfloat16)
    attended = jnp.einsum(
        "hqk,khd->qhd", weights_own, split_heads(value_all), preferred_element_type=jnp.float32
    )
    attended = attended.reshape(NT, H).astype(jnp.bfloat16)
    proj = jnp.dot(attended, w_out, preferred_element_type=jnp.float32)
    pnormed, pscale = rms_forward(proj)
    mixed = tokens.astype(jnp.float32) + pnormed
    score_w = w_score.astype(jnp.float32)
    value_out = token_live[:, 0] * jnp.sum(mixed * score_w, axis=1)
    loss_weight = 1.0 / math.sqrt(lax.axis_size("row") * lax.axis_size("col") * NT)
    grad_value = token_live[:, 0] * cotangent[0, 0] * loss_weight
    g_score = jnp.sum(mixed * grad_value[:, None], axis=0)
    grad_mixed = grad_value[:, None] * score_w
    grad_proj = rms_backward(grad_mixed, pnormed, pscale).astype(jnp.bfloat16)
    g_out = jnp.einsum("nh,ne->he", attended, grad_proj, preferred_element_type=jnp.float32)
    grad_attn = jnp.dot(grad_proj, w_out.T, preferred_element_type=jnp.float32).astype(jnp.bfloat16)

    grad_attn_all = gather_tiles(grad_attn, "col").reshape(-1, H)

    grad_prob_q = jnp.einsum(
        "qhd,khd->hqk", split_heads(grad_attn), split_heads(value_all),
        preferred_element_type=jnp.float32,
    )
    grad_score_q = (grad_prob_q * probs_own * (1.0 - probs_own) / math.sqrt(HD)).astype(jnp.bfloat16)
    grad_query = jnp.einsum(
        "hqk,khd->qhd", grad_score_q, split_heads(key_all), preferred_element_type=jnp.float32
    ).reshape(NT, H).astype(jnp.bfloat16)

    probs_key = score_probs(query_all, key_own)
    weights_key = probs_key.astype(jnp.bfloat16)
    grad_prob_k = jnp.einsum(
        "qhd,khd->hqk", split_heads(grad_attn_all), split_heads(value_own),
        preferred_element_type=jnp.float32,
    )
    grad_score_k = (grad_prob_k * probs_key * (1.0 - probs_key) / math.sqrt(HD)).astype(jnp.bfloat16)
    grad_key = jnp.einsum(
        "hqk,qhd->khd", grad_score_k, split_heads(query_all), preferred_element_type=jnp.float32
    ).reshape(NT, H).astype(jnp.bfloat16)
    grad_val = jnp.einsum(
        "hqk,qhd->khd", weights_key, split_heads(grad_attn_all), preferred_element_type=jnp.float32
    ).reshape(NT, H).astype(jnp.bfloat16)

    g_query = jnp.einsum("nh,ne->he", tokens, grad_query, preferred_element_type=jnp.float32)
    g_key = jnp.einsum("nh,ne->he", tokens, grad_key, preferred_element_type=jnp.float32)
    g_value = jnp.einsum("nh,ne->he", tokens, grad_val, preferred_element_type=jnp.float32)
    grad_tokens = grad_mixed + jnp.dot(grad_query, w_query.T, preferred_element_type=jnp.float32)
    grad_tokens = grad_tokens + jnp.dot(grad_key, w_key.T, preferred_element_type=jnp.float32)
    grad_tokens = grad_tokens + jnp.dot(grad_val, w_value.T, preferred_element_type=jnp.float32)
    grad_pooled = rms_backward(token_live * grad_tokens, normed, rscale)
    grad_scaled = (grad_pooled / (member_count + 1.0)).astype(jnp.bfloat16)
    grad_hidden = jnp.einsum(
        "ng,nh->gh", member_rows, grad_scaled, preferred_element_type=jnp.float32
    )
    grad_pre = (gate_live[:, None] * grad_hidden * silu_grad(preact)).astype(jnp.bfloat16)
    g_msg = jnp.einsum("gh,ge->he", message, grad_pre, preferred_element_type=jnp.float32)

    flat = jnp.concatenate(
        [g.reshape(-1) for g in (g_msg, g_query, g_key, g_value, g_out, g_score)]
    )
    devices = lax.axis_size("row") * lax.axis_size("col")
    pad = (-flat.shape[0]) % devices
    summed = all_reduce_a2a(jnp.pad(flat, (0, pad)), ("row", "col"))
    sq = H * H
    outs = [summed[i * sq:(i + 1) * sq].reshape(H, H) for i in range(5)]
    g_score_sum = summed[5 * sq:5 * sq + H]
    return (value_out[None, None], *outs, g_score_sum)


def solution(mesh):
    placed = (
        P("row", "col", None, None),
        P("row", "col", None, None, None, None),
        P("row", "col"),
        P("row", "col", None, None),
        P("row", "col"),
        P(),
        P(),
        P(),
        P(),
        P(),
        P(),
        P("row", "col", None),
    )
    return jax.shard_map(
        body,
        mesh=mesh,
        in_specs=placed,
        out_specs=(P("row", "col", None), P(), P(), P(), P(), P(), P()),
        check_vma=False,
    )
```

```python
import math

import jax
import jax.numpy as jnp
from jax import lax
from jax.experimental import pallas as pl
from jax.experimental.pallas import tpu as pltpu
from jax.sharding import PartitionSpec as P

H = 256
HEADS = 2
HD = 128
BLK = 128
NB = 8
NT = 512


EPS = 1e-06
SHIFT = math.log(NT)

def _nt(a, b):
    return lax.dot_general(a, b, (((1,), (1,)), ((), ())), preferred_element_type=jnp.float32)

def _nn(a, b):
    return jnp.dot(a, b, preferred_element_type=jnp.float32)

def _probs(q, k):
    return jax.nn.sigmoid(_nt(q, k) / math.sqrt(HD) - SHIFT)

def _fwd_kernel(q_ref, k_ref, v_ref, o_ref, acc_ref):
    blocks = k_ref.shape[0] // NT
    acc_ref[...] = jnp.zeros_like(acc_ref)
    def step(j, carry):
        rows = pl.ds(pl.multiple_of(j * NT, NT), NT)
        for h in range(HEADS):
            cols = slice(h * HD, (h + 1) * HD)
            w = _probs(q_ref[:, cols], k_ref[rows, cols]).astype(jnp.bfloat16)
            acc_ref[:, cols] += _nn(w, v_ref[rows, cols])
        return carry
    lax.fori_loop(0, blocks, step, 0)
    o_ref[...] = acc_ref[...].astype(o_ref.dtype)

def _gq_kernel(q_ref, g_ref, k_ref, v_ref, o_ref, acc_ref):
    blocks = k_ref.shape[0] // NT
    acc_ref[...] = jnp.zeros_like(acc_ref)
    def step(j, carry):
        rows = pl.ds(pl.multiple_of(j * NT, NT), NT)
        for h in range(HEADS):
            cols = slice(h * HD, (h + 1) * HD)
            k = k_ref[rows, cols]
            p = _probs(q_ref[:, cols], k)
            dp = _nt(g_ref[:, cols], v_ref[rows, cols])
            ds = (dp * p * (1.0 - p) / math.sqrt(HD)).astype(jnp.bfloat16)
            acc_ref[:, cols] += _nn(ds, k)
        return carry
    lax.fori_loop(0, blocks, step, 0)
    o_ref[...] = acc_ref[...].astype(o_ref.dtype)

def _gkv_kernel(q_ref, g_ref, k_ref, v_ref, dk_ref, dv_ref, acck_ref, accv_ref):
    blocks = q_ref.shape[0] // NT
    acck_ref[...] = jnp.zeros_like(acck_ref)
    accv_ref[...] = jnp.zeros_like(accv_ref)
    def step(i, carry):
        rows = pl.ds(pl.multiple_of(i * NT, NT), NT)
        for h in range(HEADS):
            cols = slice(h * HD, (h + 1) * HD)
            q = q_ref[rows, cols]
            g = g_ref[rows, cols]
            p = _probs(k_ref[:, cols], q)
            w = p.astype(jnp.bfloat16)
            dp = _nt(v_ref[:, cols], g)
            ds = (dp * p * (1.0 - p) / math.sqrt(HD)).astype(jnp.bfloat16)
            acck_ref[:, cols] += _nn(ds, q)
            accv_ref[:, cols] += _nn(w, g)
        return carry
    lax.fori_loop(0, blocks, step, 0)
    dk_ref[...] = acck_ref[...].astype(dk_ref.dtype)
    dv_ref[...] = accv_ref[...].astype(dv_ref.dtype)

def attend_fwd(q, k_all, v_all):
    return pl.pallas_call(_fwd_kernel, out_shape=jax.ShapeDtypeStruct(q.shape, jnp.bfloat16),
        scratch_shapes=[pltpu.VMEM(q.shape, jnp.float32)])(q, k_all, v_all)

def attend_gq(q, g, k_all, v_all):
    return pl.pallas_call(_gq_kernel, out_shape=jax.ShapeDtypeStruct(q.shape, jnp.bfloat16),
        scratch_shapes=[pltpu.VMEM(q.shape, jnp.float32)])(q, g, k_all, v_all)

def attend_gkv(q_all, g_all, k, v):
    sh = jax.ShapeDtypeStruct(k.shape, jnp.bfloat16)
    return pl.pallas_call(_gkv_kernel, out_shape=(sh, sh),
        scratch_shapes=[pltpu.VMEM(k.shape, jnp.float32), pltpu.VMEM(k.shape, jnp.float32)],)(q_all, g_all, k, v)


def with_halo(array, sides, width):
    for axis, dim in sides:
        size, length = (lax.axis_size(axis), array.shape[dim])
        up = [(i, (i + 1) % size) for i in range(size - 1)]
        down = [(j, i) for i, j in up]
        last = lax.slice_in_dim(array, length - width, length, axis=dim)
        first = lax.slice_in_dim(array, 0, width, axis=dim)
        before = lax.ppermute(last, axis, up)
        after = lax.ppermute(first, axis, down)
        array = jnp.concatenate([before, array, after], axis=dim)
    return array


def gather_tiles(rows_in, axis):
    size = lax.axis_size(axis)
    copies = jnp.broadcast_to(rows_in[None], (size,) + rows_in.shape)
    return lax.all_to_all(copies, axis, 0, 0, tiled=True)


def all_reduce_a2a(flat, axes):
    size = 1
    for axis in axes:
        size *= lax.axis_size(axis)
    chunks = lax.all_to_all(flat.reshape(size, -1), axes, 0, 0, tiled=True)
    total = jnp.sum(chunks, axis=0, keepdims=True)
    copies = jnp.broadcast_to(total, chunks.shape)
    return lax.all_to_all(copies, axes, 0, 0, tiled=True).reshape(-1)


def silu_grad(preact):
    sigmoid_val = jax.nn.sigmoid(preact)
    return sigmoid_val * (1.0 + preact * (1.0 - sigmoid_val))


def rms_forward(values_in):
    rscale = lax.rsqrt(jnp.mean(values_in * values_in, axis=-1, keepdims=True) + EPS)
    return (values_in * rscale, rscale)


def rms_backward(grad_in, normed, rscale):
    return rscale * (grad_in - normed * jnp.mean(grad_in * normed, axis=-1, keepdims=True))


def split_heads(rows_in):
    return rows_in.reshape(rows_in.shape[0], HEADS, HD)


def score_probs(query_rows, key_rows):
    scores = jnp.einsum(
        "qhd,khd->hqk",
        split_heads(query_rows),
        split_heads(key_rows),
        preferred_element_type=jnp.float32,
    )
    return jax.nn.sigmoid(scores / math.sqrt(HD) - math.log(NT))


def project(rows_in, weight_mat):
    return jnp.dot(rows_in, weight_mat, preferred_element_type=jnp.float32).astype(jnp.bfloat16)


def body(
    gate_feats,
    adjacency,
    gate_count,
    membership,
    tok_count,
    w_msg,
    w_query,
    w_key,
    w_value,
    w_out,
    w_score,
    cotangent,
):
    gate_total = gate_feats.shape[2]
    gate_live = (jnp.arange(gate_total) < gate_count[0, 0]).astype(jnp.float32)
    live_feats = (gate_feats[0, 0].astype(jnp.float32) * gate_live[:, None]).astype(jnp.bfloat16)
    by_row = with_halo(live_feats[None], (("row", 0),), 1)
    by_col = with_halo(live_feats[None], (("col", 0),), 1)
    sources = jnp.stack([live_feats, by_row[0], by_row[2], by_col[0], by_col[2]], axis=0)
    sources = sources.reshape(5, NB, BLK, H)
    adj_tiles = adjacency[0, 0]
    aggregate = jnp.einsum(
        "bkij,kbjh->bih",
        adj_tiles.astype(jnp.bfloat16),
        sources,
        preferred_element_type=jnp.float32,
    )
    degree = jnp.sum(adj_tiles, axis=(1, 3)).astype(jnp.float32)
    message = (aggregate / (degree[:, :, None] + 1.0)).astype(jnp.bfloat16).reshape(gate_total, H)
    preact = jnp.dot(message, w_msg, preferred_element_type=jnp.float32)
    hidden = (gate_live[:, None] * (live_feats.astype(jnp.float32) + jax.nn.silu(preact))).astype(
        jnp.bfloat16
    )
    member_rows = membership[0, 0].astype(jnp.bfloat16)
    member_count = jnp.sum(membership[0, 0], axis=1).astype(jnp.float32)[:, None]
    pooled = jnp.dot(member_rows, hidden, preferred_element_type=jnp.float32) / (member_count + 1.0)
    normed, rscale = rms_forward(pooled)
    token_live = (jnp.arange(NT) < tok_count[0, 0]).astype(jnp.float32)[:, None]
    tokens = (token_live * normed).astype(jnp.bfloat16)

    tokens_all = gather_tiles(tokens, "col").reshape(-1, H)
    query_all = project(tokens_all, w_query)
    key_all = project(tokens_all, w_key)
    value_all = project(tokens_all, w_value)
    query_own = project(tokens, w_query)
    key_own = project(tokens, w_key)
    value_own = project(tokens, w_value)

    attended = attend_fwd(query_own, key_all, value_all)
    proj = jnp.dot(attended, w_out, preferred_element_type=jnp.float32)
    pnormed, pscale = rms_forward(proj)
    mixed = tokens.astype(jnp.float32) + pnormed
    score_w = w_score.astype(jnp.float32)
    value_out = token_live[:, 0] * jnp.sum(mixed * score_w, axis=1)
    loss_weight = 1.0 / math.sqrt(lax.axis_size("row") * lax.axis_size("col") * NT)
    grad_value = token_live[:, 0] * cotangent[0, 0] * loss_weight
    g_score = jnp.sum(mixed * grad_value[:, None], axis=0)
    grad_mixed = grad_value[:, None] * score_w
    grad_proj = rms_backward(grad_mixed, pnormed, pscale).astype(jnp.bfloat16)
    g_out = jnp.einsum("nh,ne->he", attended, grad_proj, preferred_element_type=jnp.float32)
    grad_attn = jnp.dot(grad_proj, w_out.T, preferred_element_type=jnp.float32).astype(jnp.bfloat16)

    grad_attn_all = gather_tiles(grad_attn, "col").reshape(-1, H)

    grad_query = attend_gq(query_own, grad_attn, key_all, value_all)
    grad_key, grad_val = attend_gkv(query_all, grad_attn_all, key_own, value_own)

    g_query = jnp.einsum("nh,ne->he", tokens, grad_query, preferred_element_type=jnp.float32)
    g_key = jnp.einsum("nh,ne->he", tokens, grad_key, preferred_element_type=jnp.float32)
    g_value = jnp.einsum("nh,ne->he", tokens, grad_val, preferred_element_type=jnp.float32)
    grad_tokens = grad_mixed + jnp.dot(grad_query, w_query.T, preferred_element_type=jnp.float32)
    grad_tokens = grad_tokens + jnp.dot(grad_key, w_key.T, preferred_element_type=jnp.float32)
    grad_tokens = grad_tokens + jnp.dot(grad_val, w_value.T, preferred_element_type=jnp.float32)
    grad_pooled = rms_backward(token_live * grad_tokens, normed, rscale)
    grad_scaled = (grad_pooled / (member_count + 1.0)).astype(jnp.bfloat16)
    grad_hidden = jnp.einsum(
        "ng,nh->gh", member_rows, grad_scaled, preferred_element_type=jnp.float32
    )
    grad_pre = (gate_live[:, None] * grad_hidden * silu_grad(preact)).astype(jnp.bfloat16)
    g_msg = jnp.einsum("gh,ge->he", message, grad_pre, preferred_element_type=jnp.float32)

    flat = jnp.concatenate(
        [g.reshape(-1) for g in (g_msg, g_query, g_key, g_value, g_out, g_score)]
    )
    devices = lax.axis_size("row") * lax.axis_size("col")
    pad = (-flat.shape[0]) % devices
    summed = all_reduce_a2a(jnp.pad(flat, (0, pad)), ("row", "col"))
    sq = H * H
    outs = [summed[i * sq:(i + 1) * sq].reshape(H, H) for i in range(5)]
    g_score_sum = summed[5 * sq:5 * sq + H]
    return (value_out[None, None], *outs, g_score_sum)


def solution(mesh):
    placed = (
        P("row", "col", None, None),
        P("row", "col", None, None, None, None),
        P("row", "col"),
        P("row", "col", None, None),
        P("row", "col"),
        P(),
        P(),
        P(),
        P(),
        P(),
        P(),
        P("row", "col", None),
    )
    return jax.shard_map(
        body,
        mesh=mesh,
        in_specs=placed,
        out_specs=(P("row", "col", None), P(), P(), P(), P(), P(), P()),
        check_vma=False,
    )
```

```python
import math

import jax
import jax.numpy as jnp
from jax import lax
from jax.experimental import pallas as pl
from jax.experimental.pallas import tpu as pltpu
from jax.sharding import PartitionSpec as P

H = 256
HEADS = 2
HD = 128
BLK = 128
NB = 8
NT = 512


EPS = 1e-06
SHIFT = math.log(NT)

def _nt(a, b):
    return lax.dot_general(a, b, (((1,), (1,)), ((), ())), preferred_element_type=jnp.float32)

def _nn(a, b):
    return jnp.dot(a, b, preferred_element_type=jnp.float32)

def _half_tanh(q, k):
    return jnp.tanh(_nt(q, k) * (0.5 / math.sqrt(HD)) - 0.5 * SHIFT)

def _fwd_kernel(q_ref, k_ref, v_ref, o_ref, acc_ref):
    blocks = k_ref.shape[0] // NT
    acc_ref[...] = jnp.zeros_like(acc_ref)
    def step(j, carry):
        rows = pl.ds(pl.multiple_of(j * NT, NT), NT)
        for h in range(HEADS):
            cols = slice(h * HD, (h + 1) * HD)
            t = _half_tanh(q_ref[:, cols], k_ref[rows, cols])
            w = (0.5 * t + 0.5).astype(jnp.bfloat16)
            acc_ref[:, cols] += _nn(w, v_ref[rows, cols])
        return carry
    lax.fori_loop(0, blocks, step, 0)
    o_ref[...] = acc_ref[...].astype(o_ref.dtype)

def _gq_kernel(q_ref, g_ref, k_ref, v_ref, o_ref, acc_ref):
    blocks = k_ref.shape[0] // NT
    acc_ref[...] = jnp.zeros_like(acc_ref)
    def step(j, carry):
        rows = pl.ds(pl.multiple_of(j * NT, NT), NT)
        for h in range(HEADS):
            cols = slice(h * HD, (h + 1) * HD)
            k = k_ref[rows, cols]
            t = _half_tanh(q_ref[:, cols], k)
            dp = _nt(g_ref[:, cols], v_ref[rows, cols])
            ds = (dp * (1.0 - t * t) * (0.25 / math.sqrt(HD))).astype(jnp.bfloat16)
            acc_ref[:, cols] += _nn(ds, k)
        return carry
    lax.fori_loop(0, blocks, step, 0)
    o_ref[...] = acc_ref[...].astype(o_ref.dtype)

def _gkv_kernel(q_ref, g_ref, k_ref, v_ref, dk_ref, dv_ref, acck_ref, accv_ref):
    blocks = q_ref.shape[0] // NT
    acck_ref[...] = jnp.zeros_like(acck_ref)
    accv_ref[...] = jnp.zeros_like(accv_ref)
    def step(i, carry):
        rows = pl.ds(pl.multiple_of(i * NT, NT), NT)
        for h in range(HEADS):
            cols = slice(h * HD, (h + 1) * HD)
            q = q_ref[rows, cols]
            g = g_ref[rows, cols]
            t = _half_tanh(k_ref[:, cols], q)
            w = (0.5 * t + 0.5).astype(jnp.bfloat16)
            dp = _nt(v_ref[:, cols], g)
            ds = (dp * (1.0 - t * t) * (0.25 / math.sqrt(HD))).astype(jnp.bfloat16)
            acck_ref[:, cols] += _nn(ds, q)
            accv_ref[:, cols] += _nn(w, g)
        return carry
    lax.fori_loop(0, blocks, step, 0)
    dk_ref[...] = acck_ref[...].astype(dk_ref.dtype)
    dv_ref[...] = accv_ref[...].astype(dv_ref.dtype)

def attend_fwd(q, k_all, v_all):
    return pl.pallas_call(_fwd_kernel, out_shape=jax.ShapeDtypeStruct(q.shape, jnp.bfloat16),
        scratch_shapes=[pltpu.VMEM(q.shape, jnp.float32)])(q, k_all, v_all)

def attend_gq(q, g, k_all, v_all):
    return pl.pallas_call(_gq_kernel, out_shape=jax.ShapeDtypeStruct(q.shape, jnp.bfloat16),
        scratch_shapes=[pltpu.VMEM(q.shape, jnp.float32)])(q, g, k_all, v_all)

def attend_gkv(q_all, g_all, k, v):
    sh = jax.ShapeDtypeStruct(k.shape, jnp.bfloat16)
    return pl.pallas_call(_gkv_kernel, out_shape=(sh, sh),
        scratch_shapes=[pltpu.VMEM(k.shape, jnp.float32), pltpu.VMEM(k.shape, jnp.float32)],)(q_all, g_all, k, v)


def from_neighbour(array, axis, step):
    size = lax.axis_size(axis)
    pairs = [(i, i + step) for i in range(size) if 0 <= i + step < size]
    return lax.ppermute(array, axis, pairs)


def gather_tiles(rows_in, axis):
    size = lax.axis_size(axis)
    copies = jnp.broadcast_to(rows_in[None], (size,) + rows_in.shape)
    return lax.all_to_all(copies, axis, 0, 0, tiled=True)


def all_reduce_a2a(rows_in, axes):
    size = 1
    for axis in axes:
        size *= lax.axis_size(axis)
    chunks = lax.all_to_all(rows_in.reshape(size, -1, rows_in.shape[1]), axes, 0, 0, tiled=True)
    total = jnp.sum(chunks, axis=0, keepdims=True)
    copies = jnp.broadcast_to(total, chunks.shape)
    return lax.all_to_all(copies, axes, 0, 0, tiled=True).reshape(rows_in.shape)


def silu_grad(preact):
    sigmoid_val = jax.nn.sigmoid(preact)
    return sigmoid_val * (1.0 + preact * (1.0 - sigmoid_val))


def rms_forward(values_in):
    rscale = lax.rsqrt(jnp.mean(values_in * values_in, axis=-1, keepdims=True) + EPS)
    return (values_in * rscale, rscale)


def rms_backward(grad_in, normed, rscale):
    return rscale * (grad_in - normed * jnp.mean(grad_in * normed, axis=-1, keepdims=True))


def split_heads(rows_in):
    return rows_in.reshape(rows_in.shape[0], HEADS, HD)


def score_probs(query_rows, key_rows):
    scores = jnp.einsum(
        "qhd,khd->hqk",
        split_heads(query_rows),
        split_heads(key_rows),
        preferred_element_type=jnp.float32,
    )
    return jax.nn.sigmoid(scores / math.sqrt(HD) - math.log(NT))


def project(rows_in, weight_mat):
    return jnp.dot(rows_in, weight_mat, preferred_element_type=jnp.float32).astype(jnp.bfloat16)


def body(
    gate_feats,
    adjacency,
    gate_count,
    membership,
    tok_count,
    w_msg,
    w_query,
    w_key,
    w_value,
    w_out,
    w_score,
    cotangent,
):
    gate_total = gate_feats.shape[2]
    gate_live = (jnp.arange(gate_total) < gate_count[0, 0]).astype(jnp.float32)
    live_feats = (gate_feats[0, 0].astype(jnp.float32) * gate_live[:, None]).astype(jnp.bfloat16)
    sources = (
        live_feats,
        from_neighbour(live_feats, "row", 1),
        from_neighbour(live_feats, "row", -1),
        from_neighbour(live_feats, "col", 1),
        from_neighbour(live_feats, "col", -1),
    )
    adj_tiles = adjacency[0, 0]
    aggregate = sum(
        jnp.einsum(
            "bij,bjh->bih",
            adj_tiles[:, k].astype(jnp.bfloat16),
            src.reshape(NB, BLK, H),
            preferred_element_type=jnp.float32,
        )
        for k, src in enumerate(sources)
    )
    degree = jnp.sum(adj_tiles, axis=(1, 3)).astype(jnp.float32)
    message = (aggregate / (degree[:, :, None] + 1.0)).astype(jnp.bfloat16).reshape(gate_total, H)
    preact = jnp.dot(message, w_msg, preferred_element_type=jnp.float32)
    hidden = (gate_live[:, None] * (live_feats.astype(jnp.float32) + jax.nn.silu(preact))).astype(
        jnp.bfloat16
    )
    member_rows = membership[0, 0].astype(jnp.bfloat16)
    member_count = jnp.sum(membership[0, 0], axis=1).astype(jnp.float32)[:, None]
    pooled = jnp.dot(member_rows, hidden, preferred_element_type=jnp.float32) / (member_count + 1.0)
    normed, rscale = rms_forward(pooled)
    token_live = (jnp.arange(NT) < tok_count[0, 0]).astype(jnp.float32)[:, None]
    tokens = (token_live * normed).astype(jnp.bfloat16)

    tokens_all = gather_tiles(tokens, "col").reshape(-1, H)
    query_all = project(tokens_all, w_query)
    key_all = project(tokens_all, w_key)
    value_all = project(tokens_all, w_value)
    query_own = project(tokens, w_query)
    key_own = project(tokens, w_key)
    value_own = project(tokens, w_value)

    attended = attend_fwd(query_own, key_all, value_all)
    proj = jnp.dot(attended, w_out, preferred_element_type=jnp.float32)
    pnormed, pscale = rms_forward(proj)
    mixed = tokens.astype(jnp.float32) + pnormed
    score_w = w_score.astype(jnp.float32)
    value_out = token_live[:, 0] * jnp.sum(mixed * score_w, axis=1)
    loss_weight = 1.0 / math.sqrt(lax.axis_size("row") * lax.axis_size("col") * NT)
    grad_value = token_live[:, 0] * cotangent[0, 0] * loss_weight
    g_score = jnp.sum(mixed * grad_value[:, None], axis=0)
    grad_mixed = grad_value[:, None] * score_w
    grad_proj = rms_backward(grad_mixed, pnormed, pscale).astype(jnp.bfloat16)
    g_out = jnp.einsum("nh,ne->he", attended, grad_proj, preferred_element_type=jnp.float32)
    grad_attn = jnp.dot(grad_proj, w_out.T, preferred_element_type=jnp.float32).astype(jnp.bfloat16)

    grad_attn_all = gather_tiles(grad_attn, "col").reshape(-1, H)

    grad_query = attend_gq(query_own, grad_attn, key_all, value_all)
    grad_key, grad_val = attend_gkv(query_all, grad_attn_all, key_own, value_own)

    g_query = jnp.einsum("nh,ne->he", tokens, grad_query, preferred_element_type=jnp.float32)
    g_key = jnp.einsum("nh,ne->he", tokens, grad_key, preferred_element_type=jnp.float32)
    g_value = jnp.einsum("nh,ne->he", tokens, grad_val, preferred_element_type=jnp.float32)
    grad_tokens = grad_mixed + jnp.dot(grad_query, w_query.T, preferred_element_type=jnp.float32)
    grad_tokens = grad_tokens + jnp.dot(grad_key, w_key.T, preferred_element_type=jnp.float32)
    grad_tokens = grad_tokens + jnp.dot(grad_val, w_value.T, preferred_element_type=jnp.float32)
    grad_pooled = rms_backward(token_live * grad_tokens, normed, rscale)
    grad_scaled = (grad_pooled / (member_count + 1.0)).astype(jnp.bfloat16)
    grad_hidden = jnp.einsum(
        "ng,nh->gh", member_rows, grad_scaled, preferred_element_type=jnp.float32
    )
    grad_pre = (gate_live[:, None] * grad_hidden * silu_grad(preact)).astype(jnp.bfloat16)
    g_msg = jnp.einsum("gh,ge->he", message, grad_pre, preferred_element_type=jnp.float32)

    devices = lax.axis_size("row") * lax.axis_size("col")
    grads = [g_msg, g_query, g_key, g_value, g_out, g_score[None]]
    used = 5 * H + 1
    per_device = -(-used // devices)
    per_device = -(-per_device // 8) * 8
    grads.append(jnp.zeros((per_device * devices - used, H), jnp.float32))
    summed = all_reduce_a2a(jnp.concatenate(grads, axis=0), ("row", "col"))
    outs = [summed[i * H:(i + 1) * H] for i in range(5)]
    g_score_sum = summed[5 * H]
    return (value_out[None, None], *outs, g_score_sum)


def solution(mesh):
    placed = (
        P("row", "col", None, None),
        P("row", "col", None, None, None, None),
        P("row", "col"),
        P("row", "col", None, None),
        P("row", "col"),
        P(),
        P(),
        P(),
        P(),
        P(),
        P(),
        P("row", "col", None),
    )
    return jax.shard_map(
        body,
        mesh=mesh,
        in_specs=placed,
        out_specs=(P("row", "col", None), P(), P(), P(), P(), P(), P()),
        check_vma=False,
    )
```

```python
import math

import jax
import jax.numpy as jnp
from jax import lax
from jax.experimental import pallas as pl
from jax.experimental.pallas import tpu as pltpu
from jax.sharding import PartitionSpec as P

H = 256
HEADS = 2
HD = 128
BLK = 128
NB = 8
NT = 512


EPS = 1e-06
SHIFT = math.log(NT)

def _nt(a, b):
    return lax.dot_general(a, b, (((1,), (1,)), ((), ())), preferred_element_type=jnp.float32)

def _nn(a, b):
    return jnp.dot(a, b, preferred_element_type=jnp.float32)

def _half_tanh(q, k):
    return jnp.tanh(_nt(q, k) * (0.5 / math.sqrt(HD)) - 0.5 * SHIFT)

def _fwd_kernel(q_ref, k_ref, v_ref, o_ref, acc_ref):
    blocks = k_ref.shape[0] // NT
    acc_ref[...] = jnp.zeros_like(acc_ref)
    def step(j, carry):
        rows = pl.ds(pl.multiple_of(j * NT, NT), NT)
        for h in range(HEADS):
            cols = slice(h * HD, (h + 1) * HD)
            t = _half_tanh(q_ref[:, cols], k_ref[rows, cols])
            w = (0.5 * t + 0.5).astype(jnp.bfloat16)
            acc_ref[:, cols] += _nn(w, v_ref[rows, cols])
        return carry
    lax.fori_loop(0, blocks, step, 0)
    o_ref[...] = acc_ref[...].astype(o_ref.dtype)

def _gq_kernel(q_ref, g_ref, k_ref, v_ref, o_ref, acc_ref):
    blocks = k_ref.shape[0] // NT
    acc_ref[...] = jnp.zeros_like(acc_ref)
    def step(j, carry):
        rows = pl.ds(pl.multiple_of(j * NT, NT), NT)
        for h in range(HEADS):
            cols = slice(h * HD, (h + 1) * HD)
            k = k_ref[rows, cols]
            t = _half_tanh(q_ref[:, cols], k)
            dp = _nt(g_ref[:, cols], v_ref[rows, cols])
            ds = (dp * (1.0 - t * t) * (0.25 / math.sqrt(HD))).astype(jnp.bfloat16)
            acc_ref[:, cols] += _nn(ds, k)
        return carry
    lax.fori_loop(0, blocks, step, 0)
    o_ref[...] = acc_ref[...].astype(o_ref.dtype)

def _gkv_kernel(q_ref, g_ref, k_ref, v_ref, dk_ref, dv_ref, acck_ref, accv_ref):
    blocks = q_ref.shape[0] // NT
    acck_ref[...] = jnp.zeros_like(acck_ref)
    accv_ref[...] = jnp.zeros_like(accv_ref)
    def step(i, carry):
        rows = pl.ds(pl.multiple_of(i * NT, NT), NT)
        for h in range(HEADS):
            cols = slice(h * HD, (h + 1) * HD)
            q = q_ref[rows, cols]
            g = g_ref[rows, cols]
            t = _half_tanh(k_ref[:, cols], q)
            w = (0.5 * t + 0.5).astype(jnp.bfloat16)
            dp = _nt(v_ref[:, cols], g)
            ds = (dp * (1.0 - t * t) * (0.25 / math.sqrt(HD))).astype(jnp.bfloat16)
            acck_ref[:, cols] += _nn(ds, q)
            accv_ref[:, cols] += _nn(w, g)
        return carry
    lax.fori_loop(0, blocks, step, 0)
    dk_ref[...] = acck_ref[...].astype(dk_ref.dtype)
    dv_ref[...] = accv_ref[...].astype(dv_ref.dtype)

def attend_fwd(q, k_all, v_all):
    return pl.pallas_call(_fwd_kernel, out_shape=jax.ShapeDtypeStruct(q.shape, jnp.bfloat16),
        scratch_shapes=[pltpu.VMEM(q.shape, jnp.float32)])(q, k_all, v_all)

def attend_gq(q, g, k_all, v_all):
    return pl.pallas_call(_gq_kernel, out_shape=jax.ShapeDtypeStruct(q.shape, jnp.bfloat16),
        scratch_shapes=[pltpu.VMEM(q.shape, jnp.float32)])(q, g, k_all, v_all)

def attend_gkv(q_all, g_all, k, v):
    sh = jax.ShapeDtypeStruct(k.shape, jnp.bfloat16)
    return pl.pallas_call(_gkv_kernel, out_shape=(sh, sh),
        scratch_shapes=[pltpu.VMEM(k.shape, jnp.float32), pltpu.VMEM(k.shape, jnp.float32)],)(q_all, g_all, k, v)


def from_neighbour(array, axis, step):
    size = lax.axis_size(axis)
    pairs = [(i, i + step) for i in range(size) if 0 <= i + step < size]
    return lax.ppermute(array, axis, pairs)


def gather_tiles(rows_in, axis):
    size = lax.axis_size(axis)
    copies = jnp.broadcast_to(rows_in[None], (size,) + rows_in.shape)
    return lax.all_to_all(copies, axis, 0, 0, tiled=True)


def all_reduce_a2a(rows_in, axes):
    size = 1
    for axis in axes:
        size *= lax.axis_size(axis)
    if rows_in.shape[0] != size:
        rows_in = rows_in.reshape(size, -1, rows_in.shape[-1])
    chunks = lax.all_to_all(rows_in, axes, 0, 0, tiled=True)
    total = jnp.sum(chunks, axis=0, keepdims=True)
    copies = jnp.broadcast_to(total, chunks.shape)
    return lax.all_to_all(copies, axes, 0, 0, tiled=True)


def silu_grad(preact):
    sigmoid_val = jax.nn.sigmoid(preact)
    return sigmoid_val * (1.0 + preact * (1.0 - sigmoid_val))


def rms_forward(values_in):
    rscale = lax.rsqrt(jnp.mean(values_in * values_in, axis=-1, keepdims=True) + EPS)
    return (values_in * rscale, rscale)


def rms_backward(grad_in, normed, rscale):
    return rscale * (grad_in - normed * jnp.mean(grad_in * normed, axis=-1, keepdims=True))


def split_heads(rows_in):
    return rows_in.reshape(rows_in.shape[0], HEADS, HD)


def score_probs(query_rows, key_rows):
    scores = jnp.einsum(
        "qhd,khd->hqk",
        split_heads(query_rows),
        split_heads(key_rows),
        preferred_element_type=jnp.float32,
    )
    return jax.nn.sigmoid(scores / math.sqrt(HD) - math.log(NT))


def project(rows_in, weight_mat):
    return jnp.dot(rows_in, weight_mat, preferred_element_type=jnp.float32).astype(jnp.bfloat16)


def body(
    gate_feats,
    adjacency,
    gate_count,
    membership,
    tok_count,
    w_msg,
    w_query,
    w_key,
    w_value,
    w_out,
    w_score,
    cotangent,
):
    gate_total = gate_feats.shape[2]
    gate_live = (jnp.arange(gate_total) < gate_count[0, 0]).astype(jnp.float32)
    live_feats = (gate_feats[0, 0].astype(jnp.float32) * gate_live[:, None]).astype(jnp.bfloat16)
    sources = (
        live_feats,
        from_neighbour(live_feats, "row", 1),
        from_neighbour(live_feats, "row", -1),
        from_neighbour(live_feats, "col", 1),
        from_neighbour(live_feats, "col", -1),
    )
    adj_tiles = adjacency[0, 0]
    aggregate = sum(
        jnp.einsum(
            "bij,bjh->bih",
            adj_tiles[:, k].astype(jnp.bfloat16),
            src.reshape(NB, BLK, H),
            preferred_element_type=jnp.float32,
        )
        for k, src in enumerate(sources)
    )
    degree = jnp.sum(adj_tiles, axis=(1, 3)).astype(jnp.float32)
    message = (aggregate / (degree[:, :, None] + 1.0)).astype(jnp.bfloat16).reshape(gate_total, H)
    preact = jnp.dot(message, w_msg, preferred_element_type=jnp.float32)
    hidden = (gate_live[:, None] * (live_feats.astype(jnp.float32) + jax.nn.silu(preact))).astype(
        jnp.bfloat16
    )
    member_rows = membership[0, 0].astype(jnp.bfloat16)
    member_count = jnp.sum(membership[0, 0], axis=1).astype(jnp.float32)[:, None]
    pooled = jnp.dot(member_rows, hidden, preferred_element_type=jnp.float32) / (member_count + 1.0)
    normed, rscale = rms_forward(pooled)
    token_live = (jnp.arange(NT) < tok_count[0, 0]).astype(jnp.float32)[:, None]
    tokens = (token_live * normed).astype(jnp.bfloat16)

    tokens_all = gather_tiles(tokens, "col").reshape(-1, H)
    w_qkv = jnp.concatenate([w_query, w_key, w_value], axis=1)
    qkv_all = project(tokens_all, w_qkv)
    query_all = qkv_all[:, :H]
    key_all = qkv_all[:, H:2 * H]
    value_all = qkv_all[:, 2 * H:]
    qkv_own = project(tokens, w_qkv)
    query_own = qkv_own[:, :H]
    key_own = qkv_own[:, H:2 * H]
    value_own = qkv_own[:, 2 * H:]

    attended = attend_fwd(query_own, key_all, value_all)
    proj = jnp.dot(attended, w_out, preferred_element_type=jnp.float32)
    pnormed, pscale = rms_forward(proj)
    mixed = tokens.astype(jnp.float32) + pnormed
    score_w = w_score.astype(jnp.float32)
    value_out = token_live[:, 0] * jnp.sum(mixed * score_w, axis=1)
    loss_weight = 1.0 / math.sqrt(lax.axis_size("row") * lax.axis_size("col") * NT)
    grad_value = token_live[:, 0] * cotangent[0, 0] * loss_weight
    g_score = jnp.sum(mixed * grad_value[:, None], axis=0)
    grad_mixed = grad_value[:, None] * score_w
    grad_proj = rms_backward(grad_mixed, pnormed, pscale).astype(jnp.bfloat16)
    g_out = jnp.einsum("nh,ne->he", attended, grad_proj, preferred_element_type=jnp.float32)
    grad_attn = jnp.dot(grad_proj, w_out.T, preferred_element_type=jnp.float32).astype(jnp.bfloat16)
    devices = lax.axis_size("row") * lax.axis_size("col")
    early = jnp.concatenate([g_out, g_score[None], jnp.zeros((3 * devices - H - 1, H), jnp.float32)])
    early = all_reduce_a2a(early.reshape(devices, -1), ("row", "col")).reshape(-1, H)

    grad_attn_all = gather_tiles(grad_attn, "col").reshape(-1, H)

    grad_query = attend_gq(query_own, grad_attn, key_all, value_all)
    grad_key, grad_val = attend_gkv(query_all, grad_attn_all, key_own, value_own)

    g_query = jnp.einsum("nh,ne->he", tokens, grad_query, preferred_element_type=jnp.float32)
    g_key = jnp.einsum("nh,ne->he", tokens, grad_key, preferred_element_type=jnp.float32)
    g_value = jnp.einsum("nh,ne->he", tokens, grad_val, preferred_element_type=jnp.float32)
    grad_tokens = grad_mixed + jnp.dot(grad_query, w_query.T, preferred_element_type=jnp.float32)
    grad_tokens = grad_tokens + jnp.dot(grad_key, w_key.T, preferred_element_type=jnp.float32)
    grad_tokens = grad_tokens + jnp.dot(grad_val, w_value.T, preferred_element_type=jnp.float32)
    grad_pooled = rms_backward(token_live * grad_tokens, normed, rscale)
    grad_scaled = (grad_pooled / (member_count + 1.0)).astype(jnp.bfloat16)
    grad_hidden = jnp.einsum(
        "ng,nh->gh", member_rows, grad_scaled, preferred_element_type=jnp.float32
    )
    grad_pre = (gate_live[:, None] * grad_hidden * silu_grad(preact)).astype(jnp.bfloat16)
    g_msg = jnp.einsum("gh,ge->he", message, grad_pre, preferred_element_type=jnp.float32)

    late = jnp.concatenate([g_msg, g_query, g_key, g_value], axis=0)
    late = all_reduce_a2a(late, ("row", "col")).reshape(-1, H)
    outs = [late[i * H:(i + 1) * H] for i in range(4)] + [early[:H]]
    g_score_sum = early[H]
    return (value_out[None, None], *outs, g_score_sum)


def solution(mesh):
    placed = (
        P("row", "col", None, None),
        P("row", "col", None, None, None, None),
        P("row", "col"),
        P("row", "col", None, None),
        P("row", "col"),
        P(),
        P(),
        P(),
        P(),
        P(),
        P(),
        P("row", "col", None),
    )
    return jax.shard_map(
        body,
        mesh=mesh,
        in_specs=placed,
        out_specs=(P("row", "col", None), P(), P(), P(), P(), P(), P()),
        check_vma=False,
    )
```

```python
import math

import jax
import jax.numpy as jnp
from jax import lax
from jax.experimental import pallas as pl
from jax.experimental.pallas import tpu as pltpu
from jax.sharding import PartitionSpec as P

H = 256
HEADS = 2
HD = 128
BLK = 128
NB = 8
NT = 512


EPS = 1e-06
SHIFT = math.log(NT)

def _nt(a, b):
    return lax.dot_general(a, b, (((1,), (1,)), ((), ())), preferred_element_type=jnp.float32)

def _nn(a, b):
    return jnp.dot(a, b, preferred_element_type=jnp.float32)

def _half_tanh(q, k):
    return jnp.tanh(_nt(q, k) * (0.5 / math.sqrt(HD)) - 0.5 * SHIFT)

def _fwd_kernel(q_ref, k_ref, v_ref, o_ref, acc_ref):
    blocks = k_ref.shape[0] // NT
    acc_ref[...] = jnp.zeros_like(acc_ref)
    def step(j, carry):
        rows = pl.ds(pl.multiple_of(j * NT, NT), NT)
        for h in range(HEADS):
            cols = slice(h * HD, (h + 1) * HD)
            t = _half_tanh(q_ref[:, cols], k_ref[rows, cols])
            w = (0.5 * t + 0.5).astype(jnp.bfloat16)
            acc_ref[:, cols] += _nn(w, v_ref[rows, cols])
        return carry
    lax.fori_loop(0, blocks, step, 0)
    o_ref[...] = acc_ref[...].astype(o_ref.dtype)

def _gq_kernel(q_ref, g_ref, k_ref, v_ref, o_ref, acc_ref):
    blocks = k_ref.shape[0] // NT
    acc_ref[...] = jnp.zeros_like(acc_ref)
    def step(j, carry):
        rows = pl.ds(pl.multiple_of(j * NT, NT), NT)
        for h in range(HEADS):
            cols = slice(h * HD, (h + 1) * HD)
            k = k_ref[rows, cols]
            t = _half_tanh(q_ref[:, cols], k)
            dp = _nt(g_ref[:, cols], v_ref[rows, cols])
            ds = (dp * (1.0 - t * t) * (0.25 / math.sqrt(HD))).astype(jnp.bfloat16)
            acc_ref[:, cols] += _nn(ds, k)
        return carry
    lax.fori_loop(0, blocks, step, 0)
    o_ref[...] = acc_ref[...].astype(o_ref.dtype)

def _gkv_kernel(q_ref, g_ref, k_ref, v_ref, dk_ref, dv_ref, acck_ref, accv_ref):
    blocks = q_ref.shape[0] // NT
    acck_ref[...] = jnp.zeros_like(acck_ref)
    accv_ref[...] = jnp.zeros_like(accv_ref)
    def step(i, carry):
        rows = pl.ds(pl.multiple_of(i * NT, NT), NT)
        for h in range(HEADS):
            cols = slice(h * HD, (h + 1) * HD)
            q = q_ref[rows, cols]
            g = g_ref[rows, cols]
            t = _half_tanh(k_ref[:, cols], q)
            w = (0.5 * t + 0.5).astype(jnp.bfloat16)
            dp = _nt(v_ref[:, cols], g)
            ds = (dp * (1.0 - t * t) * (0.25 / math.sqrt(HD))).astype(jnp.bfloat16)
            acck_ref[:, cols] += _nn(ds, q)
            accv_ref[:, cols] += _nn(w, g)
        return carry
    lax.fori_loop(0, blocks, step, 0)
    dk_ref[...] = acck_ref[...].astype(dk_ref.dtype)
    dv_ref[...] = accv_ref[...].astype(dv_ref.dtype)

def attend_fwd(q, k_all, v_all):
    return pl.pallas_call(_fwd_kernel, out_shape=jax.ShapeDtypeStruct(q.shape, jnp.bfloat16),
        scratch_shapes=[pltpu.VMEM(q.shape, jnp.float32)])(q, k_all, v_all)

def attend_gq(q, g, k_all, v_all):
    return pl.pallas_call(_gq_kernel, out_shape=jax.ShapeDtypeStruct(q.shape, jnp.bfloat16),
        scratch_shapes=[pltpu.VMEM(q.shape, jnp.float32)])(q, g, k_all, v_all)

def attend_gkv(q_all, g_all, k, v):
    sh = jax.ShapeDtypeStruct(k.shape, jnp.bfloat16)
    return pl.pallas_call(_gkv_kernel, out_shape=(sh, sh),
        scratch_shapes=[pltpu.VMEM(k.shape, jnp.float32), pltpu.VMEM(k.shape, jnp.float32)],)(q_all, g_all, k, v)


def from_neighbour(array, axis, step):
    size = lax.axis_size(axis)
    pairs = [(i, i + step) for i in range(size) if 0 <= i + step < size]
    return lax.ppermute(array, axis, pairs)


def gather_tiles(rows_in, axis):
    size = lax.axis_size(axis)
    copies = jnp.broadcast_to(rows_in[None], (size,) + rows_in.shape)
    return lax.all_to_all(copies, axis, 0, 0, tiled=True)


def all_reduce_a2a(rows_in, axes):
    size = 1
    for axis in axes:
        size *= lax.axis_size(axis)
    if rows_in.shape[0] != size:
        rows_in = rows_in.reshape(size, -1, rows_in.shape[-1])
    chunks = lax.all_to_all(rows_in, axes, 0, 0, tiled=True)
    total = jnp.sum(chunks, axis=0, keepdims=True).astype(jnp.bfloat16)
    copies = jnp.broadcast_to(total, chunks.shape)
    return lax.all_to_all(copies, axes, 0, 0, tiled=True).astype(jnp.float32)


def silu_grad(preact):
    sigmoid_val = jax.nn.sigmoid(preact)
    return sigmoid_val * (1.0 + preact * (1.0 - sigmoid_val))


def rms_forward(values_in):
    rscale = lax.rsqrt(jnp.mean(values_in * values_in, axis=-1, keepdims=True) + EPS)
    return (values_in * rscale, rscale)


def rms_backward(grad_in, normed, rscale):
    return rscale * (grad_in - normed * jnp.mean(grad_in * normed, axis=-1, keepdims=True))


def split_heads(rows_in):
    return rows_in.reshape(rows_in.shape[0], HEADS, HD)


def score_probs(query_rows, key_rows):
    scores = jnp.einsum(
        "qhd,khd->hqk",
        split_heads(query_rows),
        split_heads(key_rows),
        preferred_element_type=jnp.float32,
    )
    return jax.nn.sigmoid(scores / math.sqrt(HD) - math.log(NT))


def project(rows_in, weight_mat):
    return jnp.dot(rows_in, weight_mat, preferred_element_type=jnp.float32).astype(jnp.bfloat16)


def body(
    gate_feats,
    adjacency,
    gate_count,
    membership,
    tok_count,
    w_msg,
    w_query,
    w_key,
    w_value,
    w_out,
    w_score,
    cotangent,
):
    gate_total = gate_feats.shape[2]
    gate_live = (jnp.arange(gate_total) < gate_count[0, 0]).astype(jnp.float32)
    live_feats = (gate_feats[0, 0].astype(jnp.float32) * gate_live[:, None]).astype(jnp.bfloat16)
    sources = (
        live_feats,
        from_neighbour(live_feats, "row", 1),
        from_neighbour(live_feats, "row", -1),
        from_neighbour(live_feats, "col", 1),
        from_neighbour(live_feats, "col", -1),
    )
    adj_tiles = adjacency[0, 0]
    aggregate = sum(
        jnp.einsum(
            "bij,bjh->bih",
            adj_tiles[:, k].astype(jnp.bfloat16),
            src.reshape(NB, BLK, H),
            preferred_element_type=jnp.float32,
        )
        for k, src in enumerate(sources)
    )
    degree = jnp.sum(adj_tiles, axis=(1, 3)).astype(jnp.float32)
    message = (aggregate / (degree[:, :, None] + 1.0)).astype(jnp.bfloat16).reshape(gate_total, H)
    preact = jnp.dot(message, w_msg, preferred_element_type=jnp.float32)
    hidden = (gate_live[:, None] * (live_feats.astype(jnp.float32) + jax.nn.silu(preact))).astype(
        jnp.bfloat16
    )
    member_rows = membership[0, 0].astype(jnp.bfloat16)
    member_count = jnp.sum(membership[0, 0], axis=1).astype(jnp.float32)[:, None]
    pooled = jnp.dot(member_rows, hidden, preferred_element_type=jnp.float32) / (member_count + 1.0)
    normed, rscale = rms_forward(pooled)
    token_live = (jnp.arange(NT) < tok_count[0, 0]).astype(jnp.float32)[:, None]
    tokens = (token_live * normed).astype(jnp.bfloat16)

    tokens_all = gather_tiles(tokens, "col").reshape(-1, H)
    w_qkv = jnp.concatenate([w_query, w_key, w_value], axis=1)
    qkv_all = project(tokens_all, w_qkv)
    query_all = qkv_all[:, :H]
    key_all = qkv_all[:, H:2 * H]
    value_all = qkv_all[:, 2 * H:]
    qkv_own = project(tokens, w_qkv)
    query_own = qkv_own[:, :H]
    key_own = qkv_own[:, H:2 * H]
    value_own = qkv_own[:, 2 * H:]

    attended = attend_fwd(query_own, key_all, value_all)
    proj = jnp.dot(attended, w_out, preferred_element_type=jnp.float32)
    pnormed, pscale = rms_forward(proj)
    mixed = tokens.astype(jnp.float32) + pnormed
    score_w = w_score.astype(jnp.float32)
    value_out = token_live[:, 0] * jnp.sum(mixed * score_w, axis=1)
    loss_weight = 1.0 / math.sqrt(lax.axis_size("row") * lax.axis_size("col") * NT)
    grad_value = token_live[:, 0] * cotangent[0, 0] * loss_weight
    g_score = jnp.sum(mixed * grad_value[:, None], axis=0)
    grad_mixed = grad_value[:, None] * score_w
    grad_proj = rms_backward(grad_mixed, pnormed, pscale).astype(jnp.bfloat16)
    g_out = jnp.einsum("nh,ne->he", attended, grad_proj, preferred_element_type=jnp.float32)
    grad_attn = jnp.dot(grad_proj, w_out.T, preferred_element_type=jnp.float32).astype(jnp.bfloat16)
    devices = lax.axis_size("row") * lax.axis_size("col")
    early = jnp.concatenate([g_out, g_score[None], jnp.zeros((3 * devices - H - 1, H), jnp.float32)])

    grad_attn_all = gather_tiles(grad_attn, "col").reshape(-1, H)
    early, grad_attn_all = lax.optimization_barrier((early, grad_attn_all))
    early = all_reduce_a2a(early.reshape(devices, -1), ("row", "col")).reshape(-1, H)

    grad_query = attend_gq(query_own, grad_attn, key_all, value_all)
    grad_key, grad_val = attend_gkv(query_all, grad_attn_all, key_own, value_own)

    g_query = jnp.einsum("nh,ne->he", tokens, grad_query, preferred_element_type=jnp.float32)
    g_key = jnp.einsum("nh,ne->he", tokens, grad_key, preferred_element_type=jnp.float32)
    g_value = jnp.einsum("nh,ne->he", tokens, grad_val, preferred_element_type=jnp.float32)
    grad_tokens = grad_mixed + jnp.dot(grad_query, w_query.T, preferred_element_type=jnp.float32)
    grad_tokens = grad_tokens + jnp.dot(grad_key, w_key.T, preferred_element_type=jnp.float32)
    grad_tokens = grad_tokens + jnp.dot(grad_val, w_value.T, preferred_element_type=jnp.float32)
    grad_pooled = rms_backward(token_live * grad_tokens, normed, rscale)
    grad_scaled = (grad_pooled / (member_count + 1.0)).astype(jnp.bfloat16)
    grad_hidden = jnp.einsum(
        "ng,nh->gh", member_rows, grad_scaled, preferred_element_type=jnp.float32
    )
    grad_pre = (gate_live[:, None] * grad_hidden * silu_grad(preact)).astype(jnp.bfloat16)
    g_msg = jnp.einsum("gh,ge->he", message, grad_pre, preferred_element_type=jnp.float32)

    late = jnp.concatenate([g_msg, g_query, g_key, g_value], axis=0)
    early, late = lax.optimization_barrier((early, late))
    late = all_reduce_a2a(late, ("row", "col")).reshape(-1, H)
    outs = [late[i * H:(i + 1) * H] for i in range(4)] + [early[:H]]
    g_score_sum = early[H]
    return (value_out[None, None], *outs, g_score_sum)


def solution(mesh):
    placed = (
        P("row", "col", None, None),
        P("row", "col", None, None, None, None),
        P("row", "col"),
        P("row", "col", None, None),
        P("row", "col"),
        P(),
        P(),
        P(),
        P(),
        P(),
        P(),
        P("row", "col", None),
    )
    return jax.shard_map(
        body,
        mesh=mesh,
        in_specs=placed,
        out_specs=(P("row", "col", None), P(), P(), P(), P(), P(), P()),
        check_vma=False,
    )
```

```python
import math

import jax
import jax.numpy as jnp
from jax import lax
from jax.experimental import pallas as pl
from jax.experimental.pallas import tpu as pltpu
from jax.sharding import PartitionSpec as P

H = 256
HEADS = 2
HD = 128
BLK = 128
NB = 8
NT = 512


EPS = 1e-06
SHIFT = math.log(NT)
KB = 1024

def _nt(a, b):
    return lax.dot_general(a, b, (((1,), (1,)), ((), ())), preferred_element_type=jnp.float32)

def _nn(a, b):
    return jnp.dot(a, b, preferred_element_type=jnp.float32)

def _half_tanh(q, k):
    return jnp.tanh(_nt(q, k) * (0.5 / math.sqrt(HD)) - 0.5 * SHIFT)

def _fwd_kernel(q_ref, k_ref, v_ref, o_ref, acc_ref):
    blocks = k_ref.shape[0] // KB
    acc_ref[...] = jnp.zeros_like(acc_ref)
    def step(j, carry):
        rows = pl.ds(pl.multiple_of(j * KB, KB), KB)
        for h in range(HEADS):
            cols = slice(h * HD, (h + 1) * HD)
            t = _half_tanh(q_ref[:, cols], k_ref[rows, cols])
            w = (0.5 * t + 0.5).astype(jnp.bfloat16)
            acc_ref[:, cols] += _nn(w, v_ref[rows, cols])
        return carry
    lax.fori_loop(0, blocks, step, 0)
    o_ref[...] = acc_ref[...].astype(o_ref.dtype)

def _gq_kernel(q_ref, g_ref, k_ref, v_ref, o_ref, acc_ref):
    blocks = k_ref.shape[0] // KB
    acc_ref[...] = jnp.zeros_like(acc_ref)
    def step(j, carry):
        rows = pl.ds(pl.multiple_of(j * KB, KB), KB)
        for h in range(HEADS):
            cols = slice(h * HD, (h + 1) * HD)
            k = k_ref[rows, cols]
            t = _half_tanh(q_ref[:, cols], k)
            dp = _nt(g_ref[:, cols], v_ref[rows, cols])
            ds = (dp * (1.0 - t * t) * (0.25 / math.sqrt(HD))).astype(jnp.bfloat16)
            acc_ref[:, cols] += _nn(ds, k)
        return carry
    lax.fori_loop(0, blocks, step, 0)
    o_ref[...] = acc_ref[...].astype(o_ref.dtype)

def _gkv_kernel(q_ref, g_ref, k_ref, v_ref, dk_ref, dv_ref, acck_ref, accv_ref):
    blocks = q_ref.shape[0] // KB
    acck_ref[...] = jnp.zeros_like(acck_ref)
    accv_ref[...] = jnp.zeros_like(accv_ref)
    def step(i, carry):
        rows = pl.ds(pl.multiple_of(i * KB, KB), KB)
        for h in range(HEADS):
            cols = slice(h * HD, (h + 1) * HD)
            q = q_ref[rows, cols]
            g = g_ref[rows, cols]
            t = _half_tanh(k_ref[:, cols], q)
            w = (0.5 * t + 0.5).astype(jnp.bfloat16)
            dp = _nt(v_ref[:, cols], g)
            ds = (dp * (1.0 - t * t) * (0.25 / math.sqrt(HD))).astype(jnp.bfloat16)
            acck_ref[:, cols] += _nn(ds, q)
            accv_ref[:, cols] += _nn(w, g)
        return carry
    lax.fori_loop(0, blocks, step, 0)
    dk_ref[...] = acck_ref[...].astype(dk_ref.dtype)
    dv_ref[...] = accv_ref[...].astype(dv_ref.dtype)

def attend_fwd(q, k_all, v_all):
    return pl.pallas_call(_fwd_kernel, out_shape=jax.ShapeDtypeStruct(q.shape, jnp.bfloat16),
        scratch_shapes=[pltpu.VMEM(q.shape, jnp.float32)])(q, k_all, v_all)

def attend_gq(q, g, k_all, v_all):
    return pl.pallas_call(_gq_kernel, out_shape=jax.ShapeDtypeStruct(q.shape, jnp.bfloat16),
        scratch_shapes=[pltpu.VMEM(q.shape, jnp.float32)])(q, g, k_all, v_all)

def attend_gkv(q_all, g_all, k, v):
    sh = jax.ShapeDtypeStruct(k.shape, jnp.bfloat16)
    return pl.pallas_call(_gkv_kernel, out_shape=(sh, sh),
        scratch_shapes=[pltpu.VMEM(k.shape, jnp.float32), pltpu.VMEM(k.shape, jnp.float32)],)(q_all, g_all, k, v)


def from_neighbour(array, axis, step):
    size = lax.axis_size(axis)
    pairs = [(i, i + step) for i in range(size) if 0 <= i + step < size]
    return lax.ppermute(array, axis, pairs)


def gather_tiles(rows_in, axis):
    size = lax.axis_size(axis)
    copies = jnp.broadcast_to(rows_in[None], (size,) + rows_in.shape)
    return lax.all_to_all(copies, axis, 0, 0, tiled=True)


def all_reduce_a2a(rows_in, axes):
    size = 1
    for axis in axes:
        size *= lax.axis_size(axis)
    if rows_in.shape[0] != size:
        rows_in = rows_in.reshape(size, -1, rows_in.shape[-1])
    chunks = lax.all_to_all(rows_in, axes, 0, 0, tiled=True)
    total = jnp.sum(chunks, axis=0, keepdims=True).astype(jnp.bfloat16)
    copies = jnp.broadcast_to(total, chunks.shape)
    return lax.all_to_all(copies, axes, 0, 0, tiled=True).astype(jnp.float32)


def silu_grad(preact):
    sigmoid_val = jax.nn.sigmoid(preact)
    return sigmoid_val * (1.0 + preact * (1.0 - sigmoid_val))


def rms_forward(values_in):
    rscale = lax.rsqrt(jnp.mean(values_in * values_in, axis=-1, keepdims=True) + EPS)
    return (values_in * rscale, rscale)


def rms_backward(grad_in, normed, rscale):
    return rscale * (grad_in - normed * jnp.mean(grad_in * normed, axis=-1, keepdims=True))


def split_heads(rows_in):
    return rows_in.reshape(rows_in.shape[0], HEADS, HD)


def score_probs(query_rows, key_rows):
    scores = jnp.einsum(
        "qhd,khd->hqk",
        split_heads(query_rows),
        split_heads(key_rows),
        preferred_element_type=jnp.float32,
    )
    return jax.nn.sigmoid(scores / math.sqrt(HD) - math.log(NT))


def project(rows_in, weight_mat):
    return jnp.dot(rows_in, weight_mat, preferred_element_type=jnp.float32).astype(jnp.bfloat16)


def body(
    gate_feats,
    adjacency,
    gate_count,
    membership,
    tok_count,
    w_msg,
    w_query,
    w_key,
    w_value,
    w_out,
    w_score,
    cotangent,
):
    gate_total = gate_feats.shape[2]
    gate_live = (jnp.arange(gate_total) < gate_count[0, 0]).astype(jnp.float32)
    live_feats = (gate_feats[0, 0].astype(jnp.float32) * gate_live[:, None]).astype(jnp.bfloat16)
    sources = (
        live_feats,
        from_neighbour(live_feats, "row", 1),
        from_neighbour(live_feats, "row", -1),
        from_neighbour(live_feats, "col", 1),
        from_neighbour(live_feats, "col", -1),
    )
    adj_tiles = adjacency[0, 0]
    aggregate = sum(
        jnp.einsum(
            "bij,bjh->bih",
            adj_tiles[:, k].astype(jnp.bfloat16),
            src.reshape(NB, BLK, H),
            preferred_element_type=jnp.float32,
        )
        for k, src in enumerate(sources)
    )
    degree = jnp.sum(adj_tiles, axis=(1, 3)).astype(jnp.float32)
    message = (aggregate / (degree[:, :, None] + 1.0)).astype(jnp.bfloat16).reshape(gate_total, H)
    preact = jnp.dot(message, w_msg, preferred_element_type=jnp.float32)
    hidden = (gate_live[:, None] * (live_feats.astype(jnp.float32) + jax.nn.silu(preact))).astype(
        jnp.bfloat16
    )
    member_rows = membership[0, 0].astype(jnp.bfloat16)
    member_count = jnp.sum(membership[0, 0], axis=1).astype(jnp.float32)[:, None]
    pooled = jnp.dot(member_rows, hidden, preferred_element_type=jnp.float32) / (member_count + 1.0)
    normed, rscale = rms_forward(pooled)
    token_live = (jnp.arange(NT) < tok_count[0, 0]).astype(jnp.float32)[:, None]
    tokens = (token_live * normed).astype(jnp.bfloat16)

    tokens_all = gather_tiles(tokens, "col").reshape(-1, H)
    w_qkv = jnp.concatenate([w_query, w_key, w_value], axis=1)
    qkv_all = project(tokens_all, w_qkv)
    query_all = qkv_all[:, :H]
    key_all = qkv_all[:, H:2 * H]
    value_all = qkv_all[:, 2 * H:]
    qkv_own = project(tokens, w_qkv)
    query_own = qkv_own[:, :H]
    key_own = qkv_own[:, H:2 * H]
    value_own = qkv_own[:, 2 * H:]

    attended = attend_fwd(query_own, key_all, value_all)
    proj = jnp.dot(attended, w_out, preferred_element_type=jnp.float32)
    pnormed, pscale = rms_forward(proj)
    mixed = tokens.astype(jnp.float32) + pnormed
    score_w = w_score.astype(jnp.float32)
    value_out = token_live[:, 0] * jnp.sum(mixed * score_w, axis=1)
    loss_weight = 1.0 / math.sqrt(lax.axis_size("row") * lax.axis_size("col") * NT)
    grad_value = token_live[:, 0] * cotangent[0, 0] * loss_weight
    g_score = jnp.sum(mixed * grad_value[:, None], axis=0)
    grad_mixed = grad_value[:, None] * score_w
    grad_proj = rms_backward(grad_mixed, pnormed, pscale).astype(jnp.bfloat16)
    g_out = jnp.einsum("nh,ne->he", attended, grad_proj, preferred_element_type=jnp.float32)
    grad_attn = jnp.dot(grad_proj, w_out.T, preferred_element_type=jnp.float32).astype(jnp.bfloat16)

    grad_attn_all = gather_tiles(grad_attn, "col").reshape(-1, H)

    grad_query = attend_gq(query_own, grad_attn, key_all, value_all)
    grad_key, grad_val = attend_gkv(query_all, grad_attn_all, key_own, value_own)

    g_query = jnp.einsum("nh,ne->he", tokens, grad_query, preferred_element_type=jnp.float32)
    g_key = jnp.einsum("nh,ne->he", tokens, grad_key, preferred_element_type=jnp.float32)
    g_value = jnp.einsum("nh,ne->he", tokens, grad_val, preferred_element_type=jnp.float32)
    grad_tokens = grad_mixed + jnp.dot(grad_query, w_query.T, preferred_element_type=jnp.float32)
    grad_tokens = grad_tokens + jnp.dot(grad_key, w_key.T, preferred_element_type=jnp.float32)
    grad_tokens = grad_tokens + jnp.dot(grad_val, w_value.T, preferred_element_type=jnp.float32)
    grad_pooled = rms_backward(token_live * grad_tokens, normed, rscale)
    grad_scaled = (grad_pooled / (member_count + 1.0)).astype(jnp.bfloat16)
    grad_hidden = jnp.einsum(
        "ng,nh->gh", member_rows, grad_scaled, preferred_element_type=jnp.float32
    )
    grad_pre = (gate_live[:, None] * grad_hidden * silu_grad(preact)).astype(jnp.bfloat16)
    g_msg = jnp.einsum("gh,ge->he", message, grad_pre, preferred_element_type=jnp.float32)

    devices = lax.axis_size("row") * lax.axis_size("col")
    used = 5 * H + 1
    per_device = -(-used * H // (devices * 128))
    grads = [g_msg, g_query, g_key, g_value, g_out, g_score[None]]
    grads.append(jnp.zeros((per_device * devices * 128 // H - used, H), jnp.float32))
    buffer = jnp.concatenate(grads, axis=0).reshape(devices, per_device, 128)
    summed = all_reduce_a2a(buffer, ("row", "col")).reshape(-1, H)
    outs = [summed[i * H:(i + 1) * H] for i in range(5)]
    g_score_sum = summed[5 * H]
    return (value_out[None, None], *outs, g_score_sum)


def solution(mesh):
    placed = (
        P("row", "col", None, None),
        P("row", "col", None, None, None, None),
        P("row", "col"),
        P("row", "col", None, None),
        P("row", "col"),
        P(),
        P(),
        P(),
        P(),
        P(),
        P(),
        P("row", "col", None),
    )
    return jax.shard_map(
        body,
        mesh=mesh,
        in_specs=placed,
        out_specs=(P("row", "col", None), P(), P(), P(), P(), P(), P()),
        check_vma=False,
    )
```

```python
import math

import jax
import jax.numpy as jnp
from jax import lax
from jax.experimental import pallas as pl
from jax.experimental.pallas import tpu as pltpu
from jax.sharding import PartitionSpec as P

H = 256
HEADS = 2
HD = 128
BLK = 128
NB = 8
NT = 512


EPS = 1e-06
SHIFT = math.log(NT)
KB = 1024

def _nt(a, b):
    return lax.dot_general(a, b, (((1,), (1,)), ((), ())), preferred_element_type=jnp.float32)

def _nn(a, b):
    return jnp.dot(a, b, preferred_element_type=jnp.float32)

def _half_tanh(q, k):
    return jnp.tanh(_nt(q, k) * (0.5 / math.sqrt(HD)) - 0.5 * SHIFT)

def _fwd_kernel(q_ref, kv_ref, o_ref, acc_ref):
    blocks = kv_ref.shape[0] // KB
    acc_ref[...] = jnp.zeros_like(acc_ref)
    def step(j, carry):
        rows = pl.ds(pl.multiple_of(j * KB, KB), KB)
        for h in range(HEADS):
            cols = slice(h * HD, (h + 1) * HD)
            t = _half_tanh(q_ref[:, cols], kv_ref[rows, pl.ds(H + h * HD, HD)])
            w = (0.5 * t + 0.5).astype(jnp.bfloat16)
            acc_ref[:, cols] += _nn(w, kv_ref[rows, pl.ds(2 * H + h * HD, HD)])
        return carry
    lax.fori_loop(0, blocks, step, 0)
    o_ref[...] = acc_ref[...].astype(o_ref.dtype)

def _gq_kernel(q_ref, g_ref, kv_ref, o_ref, acc_ref):
    blocks = kv_ref.shape[0] // KB
    acc_ref[...] = jnp.zeros_like(acc_ref)
    def step(j, carry):
        rows = pl.ds(pl.multiple_of(j * KB, KB), KB)
        for h in range(HEADS):
            cols = slice(h * HD, (h + 1) * HD)
            k = kv_ref[rows, pl.ds(H + h * HD, HD)]
            t = _half_tanh(q_ref[:, cols], k)
            dp = _nt(g_ref[:, cols], kv_ref[rows, pl.ds(2 * H + h * HD, HD)])
            ds = (dp * (1.0 - t * t) * (0.25 / math.sqrt(HD))).astype(jnp.bfloat16)
            acc_ref[:, cols] += _nn(ds, k)
        return carry
    lax.fori_loop(0, blocks, step, 0)
    o_ref[...] = acc_ref[...].astype(o_ref.dtype)

def _gkv_kernel(q_ref, g_ref, kv_ref, dk_ref, dv_ref, acck_ref, accv_ref):
    blocks = q_ref.shape[0] // KB
    acck_ref[...] = jnp.zeros_like(acck_ref)
    accv_ref[...] = jnp.zeros_like(accv_ref)
    def step(i, carry):
        rows = pl.ds(pl.multiple_of(i * KB, KB), KB)
        for h in range(HEADS):
            cols = slice(h * HD, (h + 1) * HD)
            q = q_ref[rows, cols]
            g = g_ref[rows, cols]
            t = _half_tanh(kv_ref[:, pl.ds(H + h * HD, HD)], q)
            w = (0.5 * t + 0.5).astype(jnp.bfloat16)
            dp = _nt(kv_ref[:, pl.ds(2 * H + h * HD, HD)], g)
            ds = (dp * (1.0 - t * t) * (0.25 / math.sqrt(HD))).astype(jnp.bfloat16)
            acck_ref[:, cols] += _nn(ds, q)
            accv_ref[:, cols] += _nn(w, g)
        return carry
    lax.fori_loop(0, blocks, step, 0)
    dk_ref[...] = acck_ref[...].astype(dk_ref.dtype)
    dv_ref[...] = accv_ref[...].astype(dv_ref.dtype)

def attend_fwd(qkv_own, qkv_all):
    shape = (qkv_own.shape[0], H)
    return pl.pallas_call(_fwd_kernel, out_shape=jax.ShapeDtypeStruct(shape, jnp.bfloat16),
        scratch_shapes=[pltpu.VMEM(shape, jnp.float32)])(qkv_own, qkv_all)

def attend_gq(qkv_own, g, qkv_all):
    shape = (qkv_own.shape[0], H)
    return pl.pallas_call(_gq_kernel, out_shape=jax.ShapeDtypeStruct(shape, jnp.bfloat16),
        scratch_shapes=[pltpu.VMEM(shape, jnp.float32)])(qkv_own, g, qkv_all)

def attend_gkv(qkv_all, g_all, qkv_own):
    shape = (qkv_own.shape[0], H)
    sh = jax.ShapeDtypeStruct(shape, jnp.bfloat16)
    return pl.pallas_call(_gkv_kernel, out_shape=(sh, sh),
        scratch_shapes=[pltpu.VMEM(shape, jnp.float32), pltpu.VMEM(shape, jnp.float32)])(qkv_all, g_all, qkv_own)


def from_neighbour(array, axis, step):
    size = lax.axis_size(axis)
    pairs = [(i, i + step) for i in range(size) if 0 <= i + step < size]
    return lax.ppermute(array, axis, pairs)


def gather_tiles(rows_in, axis):
    size = lax.axis_size(axis)
    copies = jnp.broadcast_to(rows_in[None], (size,) + rows_in.shape)
    return lax.all_to_all(copies, axis, 0, 0, tiled=True)


def all_reduce_a2a(rows_in, axes):
    size = 1
    for axis in axes:
        size *= lax.axis_size(axis)
    if rows_in.shape[0] != size:
        rows_in = rows_in.reshape(size, -1, rows_in.shape[-1])
    chunks = lax.all_to_all(rows_in, axes, 0, 0, tiled=True)
    total = jnp.sum(chunks, axis=0, keepdims=True).astype(jnp.bfloat16)
    copies = jnp.broadcast_to(total, chunks.shape)
    return lax.all_to_all(copies, axes, 0, 0, tiled=True).astype(jnp.float32)


def silu_grad(preact):
    sigmoid_val = jax.nn.sigmoid(preact)
    return sigmoid_val * (1.0 + preact * (1.0 - sigmoid_val))


def rms_forward(values_in):
    rscale = lax.rsqrt(jnp.mean(values_in * values_in, axis=-1, keepdims=True) + EPS)
    return (values_in * rscale, rscale)


def rms_backward(grad_in, normed, rscale):
    return rscale * (grad_in - normed * jnp.mean(grad_in * normed, axis=-1, keepdims=True))


def split_heads(rows_in):
    return rows_in.reshape(rows_in.shape[0], HEADS, HD)


def score_probs(query_rows, key_rows):
    scores = jnp.einsum(
        "qhd,khd->hqk",
        split_heads(query_rows),
        split_heads(key_rows),
        preferred_element_type=jnp.float32,
    )
    return jax.nn.sigmoid(scores / math.sqrt(HD) - math.log(NT))


def project(rows_in, weight_mat):
    return jnp.dot(rows_in, weight_mat, preferred_element_type=jnp.float32).astype(jnp.bfloat16)


def body(
    gate_feats,
    adjacency,
    gate_count,
    membership,
    tok_count,
    w_msg,
    w_query,
    w_key,
    w_value,
    w_out,
    w_score,
    cotangent,
):
    gate_total = gate_feats.shape[2]
    gate_live = (jnp.arange(gate_total) < gate_count[0, 0]).astype(jnp.float32)
    live_feats = (gate_feats[0, 0].astype(jnp.float32) * gate_live[:, None]).astype(jnp.bfloat16)
    sources = (
        live_feats,
        from_neighbour(live_feats, "row", 1),
        from_neighbour(live_feats, "row", -1),
        from_neighbour(live_feats, "col", 1),
        from_neighbour(live_feats, "col", -1),
    )
    adj_tiles = adjacency[0, 0]
    aggregate = sum(
        jnp.einsum(
            "bij,bjh->bih",
            adj_tiles[:, k].astype(jnp.bfloat16),
            src.reshape(NB, BLK, H),
            preferred_element_type=jnp.float32,
        )
        for k, src in enumerate(sources)
    )
    degree = jnp.sum(adj_tiles, axis=(1, 3)).astype(jnp.float32)
    message = (aggregate / (degree[:, :, None] + 1.0)).astype(jnp.bfloat16).reshape(gate_total, H)
    preact = jnp.dot(message, w_msg, preferred_element_type=jnp.float32)
    hidden = (gate_live[:, None] * (live_feats.astype(jnp.float32) + jax.nn.silu(preact))).astype(
        jnp.bfloat16
    )
    member_rows = membership[0, 0].astype(jnp.bfloat16)
    member_count = jnp.sum(membership[0, 0], axis=1).astype(jnp.float32)[:, None]
    pooled = jnp.dot(member_rows, hidden, preferred_element_type=jnp.float32) / (member_count + 1.0)
    normed, rscale = rms_forward(pooled)
    token_live = (jnp.arange(NT) < tok_count[0, 0]).astype(jnp.float32)[:, None]
    tokens = (token_live * normed).astype(jnp.bfloat16)

    tokens_all = gather_tiles(tokens, "col").reshape(-1, H)
    w_qkv = jnp.concatenate([w_query, w_key, w_value], axis=1)
    qkv_all = project(tokens_all, w_qkv)
    qkv_own = project(tokens, w_qkv)

    attended = attend_fwd(qkv_own, qkv_all)
    proj = jnp.dot(attended, w_out, preferred_element_type=jnp.float32)
    pnormed, pscale = rms_forward(proj)
    mixed = tokens.astype(jnp.float32) + pnormed
    score_w = w_score.astype(jnp.float32)
    value_out = token_live[:, 0] * jnp.sum(mixed * score_w, axis=1)
    loss_weight = 1.0 / math.sqrt(lax.axis_size("row") * lax.axis_size("col") * NT)
    grad_value = token_live[:, 0] * cotangent[0, 0] * loss_weight
    g_score = jnp.sum(mixed * grad_value[:, None], axis=0)
    grad_mixed = grad_value[:, None] * score_w
    grad_proj = rms_backward(grad_mixed, pnormed, pscale).astype(jnp.bfloat16)
    g_out = jnp.einsum("nh,ne->he", attended, grad_proj, preferred_element_type=jnp.float32)
    grad_attn = jnp.dot(grad_proj, w_out.T, preferred_element_type=jnp.float32).astype(jnp.bfloat16)

    grad_attn_all = gather_tiles(grad_attn, "col").reshape(-1, H)

    grad_query = attend_gq(qkv_own, grad_attn, qkv_all)
    grad_key, grad_val = attend_gkv(qkv_all, grad_attn_all, qkv_own)

    grad_qkv = jnp.concatenate([grad_query, grad_key, grad_val], axis=1)
    g_qkv = jnp.einsum("nh,ne->he", tokens, grad_qkv, preferred_element_type=jnp.float32)
    grad_tokens = grad_mixed + jnp.dot(grad_qkv, w_qkv.T, preferred_element_type=jnp.float32)
    grad_pooled = rms_backward(token_live * grad_tokens, normed, rscale)
    grad_scaled = (grad_pooled / (member_count + 1.0)).astype(jnp.bfloat16)
    grad_hidden = jnp.einsum(
        "ng,nh->gh", member_rows, grad_scaled, preferred_element_type=jnp.float32
    )
    grad_pre = (gate_live[:, None] * grad_hidden * silu_grad(preact)).astype(jnp.bfloat16)
    g_msg = jnp.einsum("gh,ge->he", message, grad_pre, preferred_element_type=jnp.float32)

    devices = lax.axis_size("row") * lax.axis_size("col")
    pieces = [g_msg.reshape(-1), g_qkv.reshape(-1), g_out.reshape(-1), g_score]
    used = sum(p.shape[0] for p in pieces)
    per_device = -(-used // (devices * 128))
    pieces.append(jnp.zeros((per_device * devices * 128 - used,), jnp.float32))
    buffer = jnp.concatenate(pieces).reshape(devices, per_device, 128)
    summed = all_reduce_a2a(buffer, ("row", "col")).reshape(-1)
    sq = H * H
    g_qkv_sum = summed[sq:4 * sq].reshape(H, 3 * H)
    outs = [summed[:sq].reshape(H, H)] + [g_qkv_sum[:, i * H:(i + 1) * H] for i in range(3)]
    outs.append(summed[4 * sq:5 * sq].reshape(H, H))
    g_score_sum = summed[5 * sq:5 * sq + H]
    return (value_out[None, None], *outs, g_score_sum)


def solution(mesh):
    placed = (
        P("row", "col", None, None),
        P("row", "col", None, None, None, None),
        P("row", "col"),
        P("row", "col", None, None),
        P("row", "col"),
        P(),
        P(),
        P(),
        P(),
        P(),
        P(),
        P("row", "col", None),
    )
    return jax.shard_map(
        body,
        mesh=mesh,
        in_specs=placed,
        out_specs=(P("row", "col", None), P(), P(), P(), P(), P(), P()),
        check_vma=False,
    )
```

```python
import math

import jax
import jax.numpy as jnp
from jax import lax
from jax.experimental import pallas as pl
from jax.experimental.pallas import tpu as pltpu
from jax.sharding import PartitionSpec as P

H = 256
HEADS = 2
HD = 128
BLK = 128
NB = 8
NT = 512


EPS = 1e-06
SHIFT = math.log(NT)
KB = 1024

def _nt(a, b):
    return lax.dot_general(a, b, (((1,), (1,)), ((), ())), preferred_element_type=jnp.float32)

def _nn(a, b):
    return jnp.dot(a, b, preferred_element_type=jnp.float32)

def _half_tanh(q, k):
    return jnp.tanh(_nt(q, k) * (0.5 / math.sqrt(HD)) - 0.5 * SHIFT)

def _fwd_kernel(q_ref, k_ref, v_ref, o_ref, acc_ref):
    blocks = k_ref.shape[0] // KB
    acc_ref[...] = jnp.zeros_like(acc_ref)
    def step(j, carry):
        rows = pl.ds(pl.multiple_of(j * KB, KB), KB)
        for h in range(HEADS):
            cols = slice(h * HD, (h + 1) * HD)
            t = _half_tanh(q_ref[:, cols], k_ref[rows, cols])
            w = (0.5 * t + 0.5).astype(jnp.bfloat16)
            acc_ref[:, cols] += _nn(w, v_ref[rows, cols])
        return carry
    lax.fori_loop(0, blocks, step, 0)
    o_ref[...] = acc_ref[...].astype(o_ref.dtype)

def _gq_kernel(q_ref, g_ref, k_ref, v_ref, o_ref, acc_ref):
    blocks = k_ref.shape[0] // KB
    acc_ref[...] = jnp.zeros_like(acc_ref)
    def step(j, carry):
        rows = pl.ds(pl.multiple_of(j * KB, KB), KB)
        for h in range(HEADS):
            cols = slice(h * HD, (h + 1) * HD)
            k = k_ref[rows, cols]
            t = _half_tanh(q_ref[:, cols], k)
            dp = _nt(g_ref[:, cols], v_ref[rows, cols])
            ds = (dp * (1.0 - t * t) * (0.25 / math.sqrt(HD))).astype(jnp.bfloat16)
            acc_ref[:, cols] += _nn(ds, k)
        return carry
    lax.fori_loop(0, blocks, step, 0)
    o_ref[...] = acc_ref[...].astype(o_ref.dtype)

def _gkv_kernel(q_ref, g_ref, k_ref, v_ref, dk_ref, dv_ref, acck_ref, accv_ref):
    blocks = q_ref.shape[0] // KB
    acck_ref[...] = jnp.zeros_like(acck_ref)
    accv_ref[...] = jnp.zeros_like(accv_ref)
    def step(i, carry):
        rows = pl.ds(pl.multiple_of(i * KB, KB), KB)
        for h in range(HEADS):
            cols = slice(h * HD, (h + 1) * HD)
            q = q_ref[rows, cols]
            g = g_ref[rows, cols]
            t = _half_tanh(k_ref[:, cols], q)
            w = (0.5 * t + 0.5).astype(jnp.bfloat16)
            dp = _nt(v_ref[:, cols], g)
            ds = (dp * (1.0 - t * t) * (0.25 / math.sqrt(HD))).astype(jnp.bfloat16)
            acck_ref[:, cols] += _nn(ds, q)
            accv_ref[:, cols] += _nn(w, g)
        return carry
    lax.fori_loop(0, blocks, step, 0)
    dk_ref[...] = acck_ref[...].astype(dk_ref.dtype)
    dv_ref[...] = accv_ref[...].astype(dv_ref.dtype)

def attend_fwd(q, k_all, v_all):
    return pl.pallas_call(_fwd_kernel, out_shape=jax.ShapeDtypeStruct(q.shape, jnp.bfloat16),
        scratch_shapes=[pltpu.VMEM(q.shape, jnp.float32)])(q, k_all, v_all)

def attend_gq(q, g, k_all, v_all):
    return pl.pallas_call(_gq_kernel, out_shape=jax.ShapeDtypeStruct(q.shape, jnp.bfloat16),
        scratch_shapes=[pltpu.VMEM(q.shape, jnp.float32)])(q, g, k_all, v_all)

def attend_gkv(q_all, g_all, k, v):
    sh = jax.ShapeDtypeStruct(k.shape, jnp.bfloat16)
    return pl.pallas_call(_gkv_kernel, out_shape=(sh, sh),
        scratch_shapes=[pltpu.VMEM(k.shape, jnp.float32), pltpu.VMEM(k.shape, jnp.float32)],)(q_all, g_all, k, v)


def from_neighbour(array, axis, step):
    size = lax.axis_size(axis)
    pairs = [(i, i + step) for i in range(size) if 0 <= i + step < size]
    return lax.ppermute(array, axis, pairs)


def gather_tiles(rows_in, axis):
    size = lax.axis_size(axis)
    copies = jnp.broadcast_to(rows_in[None], (size,) + rows_in.shape)
    return lax.all_to_all(copies, axis, 0, 0, tiled=True)


def reduce_chunks(rows_in, axes):
    chunks = lax.all_to_all(rows_in, axes, 0, 0, tiled=True)
    return jnp.sum(chunks, axis=0, keepdims=True)


def share_chunks(total, axes, size):
    copies = jnp.broadcast_to(total.astype(jnp.bfloat16), (size,) + total.shape[1:])
    return lax.all_to_all(copies, axes, 0, 0, tiled=True).astype(jnp.float32)


def all_reduce_a2a(rows_in, axes):
    size = 1
    for axis in axes:
        size *= lax.axis_size(axis)
    if rows_in.shape[0] != size:
        rows_in = rows_in.reshape(size, -1, rows_in.shape[-1])
    chunks = lax.all_to_all(rows_in, axes, 0, 0, tiled=True)
    total = jnp.sum(chunks, axis=0, keepdims=True).astype(jnp.bfloat16)
    copies = jnp.broadcast_to(total, chunks.shape)
    return lax.all_to_all(copies, axes, 0, 0, tiled=True).astype(jnp.float32)


def silu_grad(preact):
    sigmoid_val = jax.nn.sigmoid(preact)
    return sigmoid_val * (1.0 + preact * (1.0 - sigmoid_val))


def rms_forward(values_in):
    rscale = lax.rsqrt(jnp.mean(values_in * values_in, axis=-1, keepdims=True) + EPS)
    return (values_in * rscale, rscale)


def rms_backward(grad_in, normed, rscale):
    return rscale * (grad_in - normed * jnp.mean(grad_in * normed, axis=-1, keepdims=True))


def split_heads(rows_in):
    return rows_in.reshape(rows_in.shape[0], HEADS, HD)


def score_probs(query_rows, key_rows):
    scores = jnp.einsum(
        "qhd,khd->hqk",
        split_heads(query_rows),
        split_heads(key_rows),
        preferred_element_type=jnp.float32,
    )
    return jax.nn.sigmoid(scores / math.sqrt(HD) - math.log(NT))


def project(rows_in, weight_mat):
    return jnp.dot(rows_in, weight_mat, preferred_element_type=jnp.float32).astype(jnp.bfloat16)


def body(
    gate_feats,
    adjacency,
    gate_count,
    membership,
    tok_count,
    w_msg,
    w_query,
    w_key,
    w_value,
    w_out,
    w_score,
    cotangent,
):
    gate_total = gate_feats.shape[2]
    gate_live = (jnp.arange(gate_total) < gate_count[0, 0]).astype(jnp.float32)
    live_feats = (gate_feats[0, 0].astype(jnp.float32) * gate_live[:, None]).astype(jnp.bfloat16)
    sources = (
        live_feats,
        from_neighbour(live_feats, "row", 1),
        from_neighbour(live_feats, "row", -1),
        from_neighbour(live_feats, "col", 1),
        from_neighbour(live_feats, "col", -1),
    )
    adj_tiles = adjacency[0, 0]
    aggregate = sum(
        jnp.einsum(
            "bij,bjh->bih",
            adj_tiles[:, k].astype(jnp.bfloat16),
            src.reshape(NB, BLK, H),
            preferred_element_type=jnp.float32,
        )
        for k, src in enumerate(sources)
    )
    degree = jnp.sum(adj_tiles, axis=(1, 3)).astype(jnp.float32)
    message = (aggregate / (degree[:, :, None] + 1.0)).astype(jnp.bfloat16).reshape(gate_total, H)
    preact = jnp.dot(message, w_msg, preferred_element_type=jnp.float32)
    hidden = (gate_live[:, None] * (live_feats.astype(jnp.float32) + jax.nn.silu(preact))).astype(
        jnp.bfloat16
    )
    member_rows = membership[0, 0].astype(jnp.bfloat16)
    member_count = jnp.sum(membership[0, 0], axis=1).astype(jnp.float32)[:, None]
    pooled = jnp.dot(member_rows, hidden, preferred_element_type=jnp.float32) / (member_count + 1.0)
    normed, rscale = rms_forward(pooled)
    token_live = (jnp.arange(NT) < tok_count[0, 0]).astype(jnp.float32)[:, None]
    tokens = (token_live * normed).astype(jnp.bfloat16)

    tokens_all = gather_tiles(tokens, "col").reshape(-1, H)
    w_qkv = jnp.concatenate([w_query, w_key, w_value], axis=1)
    qkv_all = project(tokens_all, w_qkv)
    query_all = qkv_all[:, :H]
    key_all = qkv_all[:, H:2 * H]
    value_all = qkv_all[:, 2 * H:]
    qkv_own = project(tokens, w_qkv)
    query_own = qkv_own[:, :H]
    key_own = qkv_own[:, H:2 * H]
    value_own = qkv_own[:, 2 * H:]

    attended = attend_fwd(query_own, key_all, value_all)
    proj = jnp.dot(attended, w_out, preferred_element_type=jnp.float32)
    pnormed, pscale = rms_forward(proj)
    mixed = tokens.astype(jnp.float32) + pnormed
    score_w = w_score.astype(jnp.float32)
    value_out = token_live[:, 0] * jnp.sum(mixed * score_w, axis=1)
    loss_weight = 1.0 / math.sqrt(lax.axis_size("row") * lax.axis_size("col") * NT)
    grad_value = token_live[:, 0] * cotangent[0, 0] * loss_weight
    g_score = jnp.sum(mixed * grad_value[:, None], axis=0)
    grad_mixed = grad_value[:, None] * score_w
    grad_proj = rms_backward(grad_mixed, pnormed, pscale).astype(jnp.bfloat16)
    g_out = jnp.einsum("nh,ne->he", attended, grad_proj, preferred_element_type=jnp.float32)
    grad_attn = jnp.dot(grad_proj, w_out.T, preferred_element_type=jnp.float32).astype(jnp.bfloat16)

    grad_attn_all = gather_tiles(grad_attn, "col").reshape(-1, H)

    grad_query = attend_gq(query_own, grad_attn, key_all, value_all)
    g_query = jnp.einsum("nh,ne->he", tokens, grad_query, preferred_element_type=jnp.float32)
    devices = lax.axis_size("row") * lax.axis_size("col")
    axes = ("row", "col")
    early = jnp.concatenate([g_out, g_query], axis=0)
    early_rows = early.shape[0] * H // (devices * 128)
    early = reduce_chunks(early.reshape(devices, early_rows, 128), axes)
    grad_key, grad_val = attend_gkv(query_all, grad_attn_all, key_own, value_own)

    g_key = jnp.einsum("nh,ne->he", tokens, grad_key, preferred_element_type=jnp.float32)
    g_value = jnp.einsum("nh,ne->he", tokens, grad_val, preferred_element_type=jnp.float32)
    grad_tokens = grad_mixed + jnp.dot(grad_query, w_query.T, preferred_element_type=jnp.float32)
    grad_tokens = grad_tokens + jnp.dot(grad_key, w_key.T, preferred_element_type=jnp.float32)
    grad_tokens = grad_tokens + jnp.dot(grad_val, w_value.T, preferred_element_type=jnp.float32)
    grad_pooled = rms_backward(token_live * grad_tokens, normed, rscale)
    grad_scaled = (grad_pooled / (member_count + 1.0)).astype(jnp.bfloat16)
    grad_hidden = jnp.einsum(
        "ng,nh->gh", member_rows, grad_scaled, preferred_element_type=jnp.float32
    )
    grad_pre = (gate_live[:, None] * grad_hidden * silu_grad(preact)).astype(jnp.bfloat16)
    g_msg = jnp.einsum("gh,ge->he", message, grad_pre, preferred_element_type=jnp.float32)

    used = 3 * H + 1
    late_rows = -(-used * H // (devices * 128))
    late = [g_msg, g_key, g_value, g_score[None]]
    late.append(jnp.zeros((late_rows * devices * 128 // H - used, H), jnp.float32))
    late = reduce_chunks(jnp.concatenate(late, axis=0).reshape(devices, late_rows, 128), axes)
    both = share_chunks(jnp.concatenate([early, late], axis=1), axes, devices)
    early_sum = both[:, :early_rows].reshape(-1, H)
    late_sum = both[:, early_rows:].reshape(-1, H)
    outs = [late_sum[:H], early_sum[H:], late_sum[H:2 * H], late_sum[2 * H:3 * H], early_sum[:H]]
    g_score_sum = late_sum[3 * H]
    return (value_out[None, None], *outs, g_score_sum)


def solution(mesh):
    placed = (
        P("row", "col", None, None),
        P("row", "col", None, None, None, None),
        P("row", "col"),
        P("row", "col", None, None),
        P("row", "col"),
        P(),
        P(),
        P(),
        P(),
        P(),
        P(),
        P("row", "col", None),
    )
    return jax.shard_map(
        body,
        mesh=mesh,
        in_specs=placed,
        out_specs=(P("row", "col", None), P(), P(), P(), P(), P(), P()),
        check_vma=False,
    )
```

```python
import math

import jax
import jax.numpy as jnp
from jax import lax
from jax.experimental import pallas as pl
from jax.experimental.pallas import tpu as pltpu
from jax.sharding import PartitionSpec as P

H = 256
HEADS = 2
HD = 128
BLK = 128
NB = 8
NT = 512


EPS = 1e-06
SHIFT = math.log(NT)
KB = 1024

def _nt(a, b):
    return lax.dot_general(a, b, (((1,), (1,)), ((), ())), preferred_element_type=jnp.float32)

def _nn(a, b):
    return jnp.dot(a, b, preferred_element_type=jnp.float32)

def _half_tanh(q, k):
    return jnp.tanh(_nt(q, k) * (0.5 / math.sqrt(HD)) - 0.5 * SHIFT)

def _fwd_kernel(q_ref, k_ref, v_ref, o_ref, acc_ref):
    blocks = k_ref.shape[0] // KB
    acc_ref[...] = jnp.zeros_like(acc_ref)
    def step(j, carry):
        rows = pl.ds(pl.multiple_of(j * KB, KB), KB)
        for h in range(HEADS):
            cols = slice(h * HD, (h + 1) * HD)
            t = _half_tanh(q_ref[:, cols], k_ref[rows, cols])
            w = (0.5 * t + 0.5).astype(jnp.bfloat16)
            acc_ref[:, cols] += _nn(w, v_ref[rows, cols])
        return carry
    lax.fori_loop(0, blocks, step, 0)
    o_ref[...] = acc_ref[...].astype(o_ref.dtype)

def _gq_kernel(q_ref, g_ref, k_ref, v_ref, tt_ref, wt_ref, gw_ref, gt_ref, acc_ref):
    blocks = k_ref.shape[0] // KB
    acc_ref[...] = jnp.zeros_like(acc_ref)
    def step(j, carry):
        rows = pl.ds(pl.multiple_of(j * KB, KB), KB)
        for h in range(HEADS):
            cols = slice(h * HD, (h + 1) * HD)
            k = k_ref[rows, cols]
            t = _half_tanh(q_ref[:, cols], k)
            dp = _nt(g_ref[:, cols], v_ref[rows, cols])
            ds = (dp * (1.0 - t * t) * (0.25 / math.sqrt(HD))).astype(jnp.bfloat16)
            acc_ref[:, cols] += _nn(ds, k)
        return carry
    lax.fori_loop(0, blocks, step, 0)
    grad_rows = acc_ref[...].astype(jnp.bfloat16)
    gw_ref[...] = _nn(tt_ref[...], grad_rows)
    gt_ref[...] = _nn(grad_rows, wt_ref[...])

def _gkv_kernel(q_ref, g_ref, k_ref, v_ref, tt_ref, wkt_ref, wvt_ref, gk_ref, gv_ref, gt_ref, acck_ref, accv_ref):
    blocks = q_ref.shape[0] // KB
    acck_ref[...] = jnp.zeros_like(acck_ref)
    accv_ref[...] = jnp.zeros_like(accv_ref)
    def step(i, carry):
        rows = pl.ds(pl.multiple_of(i * KB, KB), KB)
        for h in range(HEADS):
            cols = slice(h * HD, (h + 1) * HD)
            q = q_ref[rows, cols]
            g = g_ref[rows, cols]
            t = _half_tanh(k_ref[:, cols], q)
            w = (0.5 * t + 0.5).astype(jnp.bfloat16)
            dp = _nt(v_ref[:, cols], g)
            ds = (dp * (1.0 - t * t) * (0.25 / math.sqrt(HD))).astype(jnp.bfloat16)
            acck_ref[:, cols] += _nn(ds, q)
            accv_ref[:, cols] += _nn(w, g)
        return carry
    lax.fori_loop(0, blocks, step, 0)
    grad_key = acck_ref[...].astype(jnp.bfloat16)
    grad_val = accv_ref[...].astype(jnp.bfloat16)
    gk_ref[...] = _nn(tt_ref[...], grad_key)
    gv_ref[...] = _nn(tt_ref[...], grad_val)
    gt_ref[...] = _nn(grad_key, wkt_ref[...]) + _nn(grad_val, wvt_ref[...])

def attend_fwd(q, k_all, v_all):
    return pl.pallas_call(_fwd_kernel, out_shape=jax.ShapeDtypeStruct(q.shape, jnp.bfloat16),
        scratch_shapes=[pltpu.VMEM(q.shape, jnp.float32)])(q, k_all, v_all)

def attend_gq(q, g, k_all, v_all, tokens_t, w_t):
    f32 = jnp.float32
    outs = (jax.ShapeDtypeStruct((H, H), f32), jax.ShapeDtypeStruct(q.shape, f32))
    return pl.pallas_call(_gq_kernel, out_shape=outs,
        scratch_shapes=[pltpu.VMEM(q.shape, f32)])(q, g, k_all, v_all, tokens_t, w_t)

def attend_gkv(q_all, g_all, k, v, tokens_t, wk_t, wv_t):
    f32 = jnp.float32
    outs = (jax.ShapeDtypeStruct((H, H), f32), jax.ShapeDtypeStruct((H, H), f32),
            jax.ShapeDtypeStruct(k.shape, f32))
    return pl.pallas_call(_gkv_kernel, out_shape=outs,
        scratch_shapes=[pltpu.VMEM(k.shape, f32), pltpu.VMEM(k.shape, f32)],
        )(q_all, g_all, k, v, tokens_t, wk_t, wv_t)


def from_neighbour(array, axis, step):
    size = lax.axis_size(axis)
    pairs = [(i, i + step) for i in range(size) if 0 <= i + step < size]
    return lax.ppermute(array, axis, pairs)


def gather_tiles(rows_in, axis):
    size = lax.axis_size(axis)
    copies = jnp.broadcast_to(rows_in[None], (size,) + rows_in.shape)
    return lax.all_to_all(copies, axis, 0, 0, tiled=True)


def all_reduce_a2a(rows_in, axes):
    size = 1
    for axis in axes:
        size *= lax.axis_size(axis)
    if rows_in.shape[0] != size:
        rows_in = rows_in.reshape(size, -1, rows_in.shape[-1])
    chunks = lax.all_to_all(rows_in, axes, 0, 0, tiled=True)
    total = jnp.sum(chunks, axis=0, keepdims=True).astype(jnp.bfloat16)
    copies = jnp.broadcast_to(total, chunks.shape)
    return lax.all_to_all(copies, axes, 0, 0, tiled=True).astype(jnp.float32)


def silu_grad(preact):
    sigmoid_val = jax.nn.sigmoid(preact)
    return sigmoid_val * (1.0 + preact * (1.0 - sigmoid_val))


def rms_forward(values_in):
    rscale = lax.rsqrt(jnp.mean(values_in * values_in, axis=-1, keepdims=True) + EPS)
    return (values_in * rscale, rscale)


def rms_backward(grad_in, normed, rscale):
    return rscale * (grad_in - normed * jnp.mean(grad_in * normed, axis=-1, keepdims=True))


def split_heads(rows_in):
    return rows_in.reshape(rows_in.shape[0], HEADS, HD)


def score_probs(query_rows, key_rows):
    scores = jnp.einsum(
        "qhd,khd->hqk",
        split_heads(query_rows),
        split_heads(key_rows),
        preferred_element_type=jnp.float32,
    )
    return jax.nn.sigmoid(scores / math.sqrt(HD) - math.log(NT))


def project(rows_in, weight_mat):
    return jnp.dot(rows_in, weight_mat, preferred_element_type=jnp.float32).astype(jnp.bfloat16)


def body(
    gate_feats,
    adjacency,
    gate_count,
    membership,
    tok_count,
    w_msg,
    w_query,
    w_key,
    w_value,
    w_out,
    w_score,
    cotangent,
):
    gate_total = gate_feats.shape[2]
    gate_live = (jnp.arange(gate_total) < gate_count[0, 0]).astype(jnp.float32)
    live_feats = (gate_feats[0, 0].astype(jnp.float32) * gate_live[:, None]).astype(jnp.bfloat16)
    sources = (
        live_feats,
        from_neighbour(live_feats, "row", 1),
        from_neighbour(live_feats, "row", -1),
        from_neighbour(live_feats, "col", 1),
        from_neighbour(live_feats, "col", -1),
    )
    adj_tiles = adjacency[0, 0]
    aggregate = sum(
        jnp.einsum(
            "bij,bjh->bih",
            adj_tiles[:, k].astype(jnp.bfloat16),
            src.reshape(NB, BLK, H),
            preferred_element_type=jnp.float32,
        )
        for k, src in enumerate(sources)
    )
    degree = jnp.sum(adj_tiles, axis=(1, 3)).astype(jnp.float32)
    message = (aggregate / (degree[:, :, None] + 1.0)).astype(jnp.bfloat16).reshape(gate_total, H)
    preact = jnp.dot(message, w_msg, preferred_element_type=jnp.float32)
    hidden = (gate_live[:, None] * (live_feats.astype(jnp.float32) + jax.nn.silu(preact))).astype(
        jnp.bfloat16
    )
    member_rows = membership[0, 0].astype(jnp.bfloat16)
    member_count = jnp.sum(membership[0, 0], axis=1).astype(jnp.float32)[:, None]
    pooled = jnp.dot(member_rows, hidden, preferred_element_type=jnp.float32) / (member_count + 1.0)
    normed, rscale = rms_forward(pooled)
    token_live = (jnp.arange(NT) < tok_count[0, 0]).astype(jnp.float32)[:, None]
    tokens = (token_live * normed).astype(jnp.bfloat16)

    tokens_all = gather_tiles(tokens, "col").reshape(-1, H)
    w_qkv = jnp.concatenate([w_query, w_key, w_value], axis=1)
    qkv_all = project(tokens_all, w_qkv)
    query_all = qkv_all[:, :H]
    key_all = qkv_all[:, H:2 * H]
    value_all = qkv_all[:, 2 * H:]
    qkv_own = project(tokens, w_qkv)
    query_own = qkv_own[:, :H]
    key_own = qkv_own[:, H:2 * H]
    value_own = qkv_own[:, 2 * H:]

    attended = attend_fwd(query_own, key_all, value_all)
    proj = jnp.dot(attended, w_out, preferred_element_type=jnp.float32)
    pnormed, pscale = rms_forward(proj)
    mixed = tokens.astype(jnp.float32) + pnormed
    score_w = w_score.astype(jnp.float32)
    value_out = token_live[:, 0] * jnp.sum(mixed * score_w, axis=1)
    loss_weight = 1.0 / math.sqrt(lax.axis_size("row") * lax.axis_size("col") * NT)
    grad_value = token_live[:, 0] * cotangent[0, 0] * loss_weight
    g_score = jnp.sum(mixed * grad_value[:, None], axis=0)
    grad_mixed = grad_value[:, None] * score_w
    grad_proj = rms_backward(grad_mixed, pnormed, pscale).astype(jnp.bfloat16)
    g_out = jnp.einsum("nh,ne->he", attended, grad_proj, preferred_element_type=jnp.float32)
    grad_attn = jnp.dot(grad_proj, w_out.T, preferred_element_type=jnp.float32).astype(jnp.bfloat16)

    grad_attn_all = gather_tiles(grad_attn, "col").reshape(-1, H)

    tokens_t = tokens.T
    g_query, tokens_grad_q = attend_gq(query_own, grad_attn, key_all, value_all, tokens_t, w_query.T)
    g_key, g_value, tokens_grad_kv = attend_gkv(
        query_all, grad_attn_all, key_own, value_own, tokens_t, w_key.T, w_value.T
    )

    grad_tokens = grad_mixed + tokens_grad_q + tokens_grad_kv
    grad_pooled = rms_backward(token_live * grad_tokens, normed, rscale)
    grad_scaled = (grad_pooled / (member_count + 1.0)).astype(jnp.bfloat16)
    grad_hidden = jnp.einsum(
        "ng,nh->gh", member_rows, grad_scaled, preferred_element_type=jnp.float32
    )
    grad_pre = (gate_live[:, None] * grad_hidden * silu_grad(preact)).astype(jnp.bfloat16)
    g_msg = jnp.einsum("gh,ge->he", message, grad_pre, preferred_element_type=jnp.float32)

    devices = lax.axis_size("row") * lax.axis_size("col")
    used = 5 * H + 1
    per_device = -(-used * H // (devices * 128))
    grads = [g_msg, g_query, g_key, g_value, g_out, g_score[None]]
    grads.append(jnp.zeros((per_device * devices * 128 // H - used, H), jnp.float32))
    buffer = jnp.concatenate(grads, axis=0).reshape(devices, per_device, 128)
    summed = all_reduce_a2a(buffer, ("row", "col")).reshape(-1, H)
    outs = [summed[i * H:(i + 1) * H] for i in range(5)]
    g_score_sum = summed[5 * H]
    return (value_out[None, None], *outs, g_score_sum)


def solution(mesh):
    placed = (
        P("row", "col", None, None),
        P("row", "col", None, None, None, None),
        P("row", "col"),
        P("row", "col", None, None),
        P("row", "col"),
        P(),
        P(),
        P(),
        P(),
        P(),
        P(),
        P("row", "col", None),
    )
    return jax.shard_map(
        body,
        mesh=mesh,
        in_specs=placed,
        out_specs=(P("row", "col", None), P(), P(), P(), P(), P(), P()),
        check_vma=False,
    )
```

```python
import math

import jax
import jax.numpy as jnp
from jax import lax
from jax.experimental import pallas as pl
from jax.experimental.pallas import tpu as pltpu
from jax.sharding import PartitionSpec as P

H = 256
HEADS = 2
HD = 128
BLK = 128
NB = 8
NT = 512


EPS = 1e-06
SHIFT = math.log(NT)
KB = 1024

def _nt(a, b):
    return lax.dot_general(a, b, (((1,), (1,)), ((), ())), preferred_element_type=jnp.float32)

def _nn(a, b):
    return jnp.dot(a, b, preferred_element_type=jnp.float32)

def _half_tanh(q, k):
    return jnp.tanh(_nt(q, k) * (0.5 / math.sqrt(HD)) - 0.5 * SHIFT)

def _fwd_kernel(q_ref, k_ref, v_ref, tok_ref, gval_ref, sw_ref, wo_ref, wot_ref,
                att_ref, mixed_ref, gproj_ref, gattn_ref, acc_ref):
    blocks = k_ref.shape[0] // KB
    acc_ref[...] = jnp.zeros_like(acc_ref)
    def step(j, carry):
        rows = pl.ds(pl.multiple_of(j * KB, KB), KB)
        for h in range(HEADS):
            cols = slice(h * HD, (h + 1) * HD)
            t = _half_tanh(q_ref[:, cols], k_ref[rows, cols])
            w = (0.5 * t + 0.5).astype(jnp.bfloat16)
            acc_ref[:, cols] += _nn(w, v_ref[rows, cols])
        return carry
    lax.fori_loop(0, blocks, step, 0)
    attended = acc_ref[...].astype(jnp.bfloat16)
    att_ref[...] = attended
    proj = _nn(attended, wo_ref[...])
    pscale = lax.rsqrt(jnp.mean(proj * proj, axis=-1, keepdims=True) + EPS)
    pnormed = proj * pscale
    mixed_ref[...] = tok_ref[...].astype(jnp.float32) + pnormed
    grad_mixed = gval_ref[...] * sw_ref[...].astype(jnp.float32)
    grad_proj = pscale * (grad_mixed - pnormed * jnp.mean(grad_mixed * pnormed, axis=-1, keepdims=True))
    grad_proj = grad_proj.astype(jnp.bfloat16)
    gproj_ref[...] = grad_proj
    grad_attn = _nn(grad_proj, wot_ref[...]).astype(jnp.bfloat16)
    for c in range(gattn_ref.shape[0]):
        gattn_ref[c] = grad_attn

def _gq_kernel(q_ref, g_ref, k_ref, v_ref, o_ref, acc_ref):
    blocks = k_ref.shape[0] // KB
    acc_ref[...] = jnp.zeros_like(acc_ref)
    def step(j, carry):
        rows = pl.ds(pl.multiple_of(j * KB, KB), KB)
        for h in range(HEADS):
            cols = slice(h * HD, (h + 1) * HD)
            k = k_ref[rows, cols]
            t = _half_tanh(q_ref[:, cols], k)
            dp = _nt(g_ref[:, cols], v_ref[rows, cols])
            ds = (dp * (1.0 - t * t) * (0.25 / math.sqrt(HD))).astype(jnp.bfloat16)
            acc_ref[:, cols] += _nn(ds, k)
        return carry
    lax.fori_loop(0, blocks, step, 0)
    o_ref[...] = acc_ref[...].astype(o_ref.dtype)

def _gkv_kernel(q_ref, g_ref, k_ref, v_ref, dk_ref, dv_ref, acck_ref, accv_ref):
    blocks = q_ref.shape[0] // KB
    acck_ref[...] = jnp.zeros_like(acck_ref)
    accv_ref[...] = jnp.zeros_like(accv_ref)
    def step(i, carry):
        rows = pl.ds(pl.multiple_of(i * KB, KB), KB)
        for h in range(HEADS):
            cols = slice(h * HD, (h + 1) * HD)
            q = q_ref[rows, cols]
            g = g_ref[rows, cols]
            t = _half_tanh(k_ref[:, cols], q)
            w = (0.5 * t + 0.5).astype(jnp.bfloat16)
            dp = _nt(v_ref[:, cols], g)
            ds = (dp * (1.0 - t * t) * (0.25 / math.sqrt(HD))).astype(jnp.bfloat16)
            acck_ref[:, cols] += _nn(ds, q)
            accv_ref[:, cols] += _nn(w, g)
        return carry
    lax.fori_loop(0, blocks, step, 0)
    dk_ref[...] = acck_ref[...].astype(dk_ref.dtype)
    dv_ref[...] = accv_ref[...].astype(dv_ref.dtype)

def attend_fwd(q, k_all, v_all, tokens, grad_value, w_score, w_out, copies):
    bf16, f32 = jnp.bfloat16, jnp.float32
    outs = (jax.ShapeDtypeStruct(q.shape, bf16), jax.ShapeDtypeStruct(q.shape, f32),
            jax.ShapeDtypeStruct(q.shape, bf16), jax.ShapeDtypeStruct((copies,) + q.shape, bf16))
    return pl.pallas_call(_fwd_kernel, out_shape=outs,
        scratch_shapes=[pltpu.VMEM(q.shape, f32)])(
            q, k_all, v_all, tokens, grad_value, w_score.reshape(1, -1), w_out, w_out.T)

def attend_gq(q, g, k_all, v_all):
    return pl.pallas_call(_gq_kernel, out_shape=jax.ShapeDtypeStruct(q.shape, jnp.bfloat16),
        scratch_shapes=[pltpu.VMEM(q.shape, jnp.float32)])(q, g, k_all, v_all)

def attend_gkv(q_all, g_all, k, v):
    sh = jax.ShapeDtypeStruct(k.shape, jnp.bfloat16)
    return pl.pallas_call(_gkv_kernel, out_shape=(sh, sh),
        scratch_shapes=[pltpu.VMEM(k.shape, jnp.float32), pltpu.VMEM(k.shape, jnp.float32)],)(q_all, g_all, k, v)


def from_neighbour(array, axis, step):
    size = lax.axis_size(axis)
    pairs = [(i, i + step) for i in range(size) if 0 <= i + step < size]
    return lax.ppermute(array, axis, pairs)


def gather_tiles(rows_in, axis):
    size = lax.axis_size(axis)
    copies = jnp.broadcast_to(rows_in[None], (size,) + rows_in.shape)
    return lax.all_to_all(copies, axis, 0, 0, tiled=True)


def all_reduce_a2a(rows_in, axes):
    size = 1
    for axis in axes:
        size *= lax.axis_size(axis)
    if rows_in.shape[0] != size:
        rows_in = rows_in.reshape(size, -1, rows_in.shape[-1])
    chunks = lax.all_to_all(rows_in, axes, 0, 0, tiled=True)
    total = jnp.sum(chunks, axis=0, keepdims=True).astype(jnp.bfloat16)
    copies = jnp.broadcast_to(total, chunks.shape)
    return lax.all_to_all(copies, axes, 0, 0, tiled=True).astype(jnp.float32)


def silu_grad(preact):
    sigmoid_val = jax.nn.sigmoid(preact)
    return sigmoid_val * (1.0 + preact * (1.0 - sigmoid_val))


def rms_forward(values_in):
    rscale = lax.rsqrt(jnp.mean(values_in * values_in, axis=-1, keepdims=True) + EPS)
    return (values_in * rscale, rscale)


def rms_backward(grad_in, normed, rscale):
    return rscale * (grad_in - normed * jnp.mean(grad_in * normed, axis=-1, keepdims=True))


def split_heads(rows_in):
    return rows_in.reshape(rows_in.shape[0], HEADS, HD)


def score_probs(query_rows, key_rows):
    scores = jnp.einsum(
        "qhd,khd->hqk",
        split_heads(query_rows),
        split_heads(key_rows),
        preferred_element_type=jnp.float32,
    )
    return jax.nn.sigmoid(scores / math.sqrt(HD) - math.log(NT))


def project(rows_in, weight_mat):
    return jnp.dot(rows_in, weight_mat, preferred_element_type=jnp.float32).astype(jnp.bfloat16)


def body(
    gate_feats,
    adjacency,
    gate_count,
    membership,
    tok_count,
    w_msg,
    w_query,
    w_key,
    w_value,
    w_out,
    w_score,
    cotangent,
):
    gate_total = gate_feats.shape[2]
    gate_live = (jnp.arange(gate_total) < gate_count[0, 0]).astype(jnp.float32)
    live_feats = (gate_feats[0, 0].astype(jnp.float32) * gate_live[:, None]).astype(jnp.bfloat16)
    sources = (
        live_feats,
        from_neighbour(live_feats, "row", 1),
        from_neighbour(live_feats, "row", -1),
        from_neighbour(live_feats, "col", 1),
        from_neighbour(live_feats, "col", -1),
    )
    adj_tiles = adjacency[0, 0]
    aggregate = sum(
        jnp.einsum(
            "bij,bjh->bih",
            adj_tiles[:, k].astype(jnp.bfloat16),
            src.reshape(NB, BLK, H),
            preferred_element_type=jnp.float32,
        )
        for k, src in enumerate(sources)
    )
    degree = jnp.sum(adj_tiles, axis=(1, 3)).astype(jnp.float32)
    message = (aggregate / (degree[:, :, None] + 1.0)).astype(jnp.bfloat16).reshape(gate_total, H)
    preact = jnp.dot(message, w_msg, preferred_element_type=jnp.float32)
    hidden = (gate_live[:, None] * (live_feats.astype(jnp.float32) + jax.nn.silu(preact))).astype(
        jnp.bfloat16
    )
    member_rows = membership[0, 0].astype(jnp.bfloat16)
    member_count = jnp.sum(membership[0, 0], axis=1).astype(jnp.float32)[:, None]
    pooled = jnp.dot(member_rows, hidden, preferred_element_type=jnp.float32) / (member_count + 1.0)
    normed, rscale = rms_forward(pooled)
    token_live = (jnp.arange(NT) < tok_count[0, 0]).astype(jnp.float32)[:, None]
    tokens = (token_live * normed).astype(jnp.bfloat16)

    tokens_all = gather_tiles(tokens, "col").reshape(-1, H)
    w_qkv = jnp.concatenate([w_query, w_key, w_value], axis=1)
    qkv_all = project(tokens_all, w_qkv)
    query_all = qkv_all[:, :H]
    key_all = qkv_all[:, H:2 * H]
    value_all = qkv_all[:, 2 * H:]
    qkv_own = project(tokens, w_qkv)
    query_own = qkv_own[:, :H]
    key_own = qkv_own[:, H:2 * H]
    value_own = qkv_own[:, 2 * H:]

    score_w = w_score.astype(jnp.float32)
    loss_weight = 1.0 / math.sqrt(lax.axis_size("row") * lax.axis_size("col") * NT)
    grad_value = token_live[:, 0] * cotangent[0, 0] * loss_weight
    attended, mixed, grad_proj, grad_attn_copies = attend_fwd(
        query_own, key_all, value_all, tokens, grad_value[:, None], w_score, w_out,
        lax.axis_size("col"),
    )
    value_out = token_live[:, 0] * jnp.sum(mixed * score_w, axis=1)
    g_score = jnp.sum(mixed * grad_value[:, None], axis=0)
    grad_mixed = grad_value[:, None] * score_w
    g_out = jnp.einsum("nh,ne->he", attended, grad_proj, preferred_element_type=jnp.float32)
    grad_attn = grad_attn_copies[0]

    grad_attn_all = lax.all_to_all(grad_attn_copies, "col", 0, 0, tiled=True).reshape(-1, H)

    grad_query = attend_gq(query_own, grad_attn, key_all, value_all)
    grad_key, grad_val = attend_gkv(query_all, grad_attn_all, key_own, value_own)

    g_query = jnp.einsum("nh,ne->he", tokens, grad_query, preferred_element_type=jnp.float32)
    g_key = jnp.einsum("nh,ne->he", tokens, grad_key, preferred_element_type=jnp.float32)
    g_value = jnp.einsum("nh,ne->he", tokens, grad_val, preferred_element_type=jnp.float32)
    grad_tokens = grad_mixed + jnp.dot(grad_query, w_query.T, preferred_element_type=jnp.float32)
    grad_tokens = grad_tokens + jnp.dot(grad_key, w_key.T, preferred_element_type=jnp.float32)
    grad_tokens = grad_tokens + jnp.dot(grad_val, w_value.T, preferred_element_type=jnp.float32)
    grad_pooled = rms_backward(token_live * grad_tokens, normed, rscale)
    grad_scaled = (grad_pooled / (member_count + 1.0)).astype(jnp.bfloat16)
    grad_hidden = jnp.einsum(
        "ng,nh->gh", member_rows, grad_scaled, preferred_element_type=jnp.float32
    )
    grad_pre = (gate_live[:, None] * grad_hidden * silu_grad(preact)).astype(jnp.bfloat16)
    g_msg = jnp.einsum("gh,ge->he", message, grad_pre, preferred_element_type=jnp.float32)

    devices = lax.axis_size("row") * lax.axis_size("col")
    used = 5 * H + 1
    per_device = -(-used * H // (devices * 128))
    grads = [g_msg, g_query, g_key, g_value, g_out, g_score[None]]
    grads.append(jnp.zeros((per_device * devices * 128 // H - used, H), jnp.float32))
    buffer = jnp.concatenate(grads, axis=0).reshape(devices, per_device, 128)
    summed = all_reduce_a2a(buffer, ("row", "col")).reshape(-1, H)
    outs = [summed[i * H:(i + 1) * H] for i in range(5)]
    g_score_sum = summed[5 * H]
    return (value_out[None, None], *outs, g_score_sum)


def solution(mesh):
    placed = (
        P("row", "col", None, None),
        P("row", "col", None, None, None, None),
        P("row", "col"),
        P("row", "col", None, None),
        P("row", "col"),
        P(),
        P(),
        P(),
        P(),
        P(),
        P(),
        P("row", "col", None),
    )
    return jax.shard_map(
        body,
        mesh=mesh,
        in_specs=placed,
        out_specs=(P("row", "col", None), P(), P(), P(), P(), P(), P()),
        check_vma=False,
    )
```

```python
import math

import jax
import jax.numpy as jnp
from jax import lax
from jax.experimental import pallas as pl
from jax.experimental.pallas import tpu as pltpu
from jax.sharding import PartitionSpec as P

H = 256
HEADS = 2
HD = 128
BLK = 128
NB = 8
NT = 512


EPS = 1e-06
SHIFT = math.log(NT)
KB = 1024

def _nt(a, b):
    return lax.dot_general(a, b, (((1,), (1,)), ((), ())), preferred_element_type=jnp.float32)

def _nn(a, b):
    return jnp.dot(a, b, preferred_element_type=jnp.float32)

def _half_tanh(q, k):
    return jnp.tanh(_nt(q, k) * (0.5 / math.sqrt(HD)) - 0.5 * SHIFT)

def _fwd_kernel(q_ref, k_ref, v_ref, tok_ref, gval_ref, sw_ref, wo_ref, wot_ref,
                att_ref, mixed_ref, gproj_ref, gattn_ref, acc_ref):
    blocks = k_ref.shape[0] // KB
    acc_ref[...] = jnp.zeros_like(acc_ref)
    def step(j, carry):
        rows = pl.ds(pl.multiple_of(j * KB, KB), KB)
        for h in range(HEADS):
            cols = slice(h * HD, (h + 1) * HD)
            t = _half_tanh(q_ref[:, cols], k_ref[rows, cols])
            w = (0.5 * t + 0.5).astype(jnp.bfloat16)
            acc_ref[:, cols] += _nn(w, v_ref[rows, cols])
        return carry
    lax.fori_loop(0, blocks, step, 0)
    attended = acc_ref[...].astype(jnp.bfloat16)
    att_ref[...] = attended
    proj = _nn(attended, wo_ref[...])
    pscale = lax.rsqrt(jnp.mean(proj * proj, axis=-1, keepdims=True) + EPS)
    pnormed = proj * pscale
    mixed_ref[...] = tok_ref[...].astype(jnp.float32) + pnormed
    grad_mixed = gval_ref[...] * sw_ref[...].astype(jnp.float32)
    grad_proj = pscale * (grad_mixed - pnormed * jnp.mean(grad_mixed * pnormed, axis=-1, keepdims=True))
    grad_proj = grad_proj.astype(jnp.bfloat16)
    gproj_ref[...] = grad_proj
    grad_attn = _nn(grad_proj, wot_ref[...]).astype(jnp.bfloat16)
    for c in range(gattn_ref.shape[0]):
        gattn_ref[c] = grad_attn

def _gq_kernel(q_ref, g_ref, k_ref, v_ref, o_ref, acc_ref):
    blocks = k_ref.shape[0] // KB
    acc_ref[...] = jnp.zeros_like(acc_ref)
    def step(j, carry):
        rows = pl.ds(pl.multiple_of(j * KB, KB), KB)
        for h in range(HEADS):
            cols = slice(h * HD, (h + 1) * HD)
            k = k_ref[rows, cols]
            t = _half_tanh(q_ref[:, cols], k)
            dp = _nt(g_ref[0, :, cols], v_ref[rows, cols])
            ds = (dp * (1.0 - t * t) * (0.25 / math.sqrt(HD))).astype(jnp.bfloat16)
            acc_ref[:, cols] += _nn(ds, k)
        return carry
    lax.fori_loop(0, blocks, step, 0)
    o_ref[...] = acc_ref[...].astype(o_ref.dtype)

def _gkv_kernel(q_ref, g_ref, k_ref, v_ref, dk_ref, dv_ref, acck_ref, accv_ref):
    blocks = q_ref.shape[0] // KB
    acck_ref[...] = jnp.zeros_like(acck_ref)
    accv_ref[...] = jnp.zeros_like(accv_ref)
    def step(i, carry):
        rows = pl.ds(pl.multiple_of(i * KB, KB), KB)
        for h in range(HEADS):
            cols = slice(h * HD, (h + 1) * HD)
            q = q_ref[rows, cols]
            g = g_ref[rows, cols]
            t = _half_tanh(k_ref[:, cols], q)
            w = (0.5 * t + 0.5).astype(jnp.bfloat16)
            dp = _nt(v_ref[:, cols], g)
            ds = (dp * (1.0 - t * t) * (0.25 / math.sqrt(HD))).astype(jnp.bfloat16)
            acck_ref[:, cols] += _nn(ds, q)
            accv_ref[:, cols] += _nn(w, g)
        return carry
    lax.fori_loop(0, blocks, step, 0)
    dk_ref[...] = acck_ref[...].astype(dk_ref.dtype)
    dv_ref[...] = accv_ref[...].astype(dv_ref.dtype)

def attend_fwd(q, k_all, v_all, tokens, grad_value, w_score, w_out, copies):
    bf16, f32 = jnp.bfloat16, jnp.float32
    outs = (jax.ShapeDtypeStruct(q.shape, bf16), jax.ShapeDtypeStruct(q.shape, f32),
            jax.ShapeDtypeStruct(q.shape, bf16), jax.ShapeDtypeStruct((copies,) + q.shape, bf16))
    return pl.pallas_call(_fwd_kernel, out_shape=outs,
        scratch_shapes=[pltpu.VMEM(q.shape, f32)])(
            q, k_all, v_all, tokens, grad_value, w_score.reshape(1, -1), w_out, w_out.T)

def attend_gq(q, g, k_all, v_all):
    return pl.pallas_call(_gq_kernel, out_shape=jax.ShapeDtypeStruct(q.shape, jnp.bfloat16),
        scratch_shapes=[pltpu.VMEM(q.shape, jnp.float32)])(q, g, k_all, v_all)

def attend_gkv(q_all, g_all, k, v):
    sh = jax.ShapeDtypeStruct(k.shape, jnp.bfloat16)
    return pl.pallas_call(_gkv_kernel, out_shape=(sh, sh),
        scratch_shapes=[pltpu.VMEM(k.shape, jnp.float32), pltpu.VMEM(k.shape, jnp.float32)],)(q_all, g_all, k, v)


def from_neighbour(array, axis, step):
    size = lax.axis_size(axis)
    pairs = [(i, i + step) for i in range(size) if 0 <= i + step < size]
    return lax.ppermute(array, axis, pairs)


def gather_tiles(rows_in, axis):
    size = lax.axis_size(axis)
    copies = jnp.broadcast_to(rows_in[None], (size,) + rows_in.shape)
    return lax.all_to_all(copies, axis, 0, 0, tiled=True)


def all_reduce_a2a(rows_in, axes):
    size = 1
    for axis in axes:
        size *= lax.axis_size(axis)
    if rows_in.shape[0] != size:
        rows_in = rows_in.reshape(size, -1, rows_in.shape[-1])
    chunks = lax.all_to_all(rows_in, axes, 0, 0, tiled=True)
    total = jnp.sum(chunks, axis=0, keepdims=True).astype(jnp.bfloat16)
    copies = jnp.broadcast_to(total, chunks.shape)
    return lax.all_to_all(copies, axes, 0, 0, tiled=True).astype(jnp.float32)


def silu_grad(preact):
    sigmoid_val = jax.nn.sigmoid(preact)
    return sigmoid_val * (1.0 + preact * (1.0 - sigmoid_val))


def rms_forward(values_in):
    rscale = lax.rsqrt(jnp.mean(values_in * values_in, axis=-1, keepdims=True) + EPS)
    return (values_in * rscale, rscale)


def rms_backward(grad_in, normed, rscale):
    return rscale * (grad_in - normed * jnp.mean(grad_in * normed, axis=-1, keepdims=True))


def split_heads(rows_in):
    return rows_in.reshape(rows_in.shape[0], HEADS, HD)


def score_probs(query_rows, key_rows):
    scores = jnp.einsum(
        "qhd,khd->hqk",
        split_heads(query_rows),
        split_heads(key_rows),
        preferred_element_type=jnp.float32,
    )
    return jax.nn.sigmoid(scores / math.sqrt(HD) - math.log(NT))


def project(rows_in, weight_mat):
    return jnp.dot(rows_in, weight_mat, preferred_element_type=jnp.float32).astype(jnp.bfloat16)


def body(
    gate_feats,
    adjacency,
    gate_count,
    membership,
    tok_count,
    w_msg,
    w_query,
    w_key,
    w_value,
    w_out,
    w_score,
    cotangent,
):
    gate_total = gate_feats.shape[2]
    gate_live = (jnp.arange(gate_total) < gate_count[0, 0]).astype(jnp.float32)
    live_feats = (gate_feats[0, 0].astype(jnp.float32) * gate_live[:, None]).astype(jnp.bfloat16)
    sources = (
        live_feats,
        from_neighbour(live_feats, "row", 1),
        from_neighbour(live_feats, "row", -1),
        from_neighbour(live_feats, "col", 1),
        from_neighbour(live_feats, "col", -1),
    )
    adj_tiles = adjacency[0, 0]
    aggregate = sum(
        jnp.einsum(
            "bij,bjh->bih",
            adj_tiles[:, k].astype(jnp.bfloat16),
            src.reshape(NB, BLK, H),
            preferred_element_type=jnp.float32,
        )
        for k, src in enumerate(sources)
    )
    degree = jnp.sum(adj_tiles, axis=(1, 3)).astype(jnp.float32)
    message = (aggregate / (degree[:, :, None] + 1.0)).astype(jnp.bfloat16).reshape(gate_total, H)
    preact = jnp.dot(message, w_msg, preferred_element_type=jnp.float32)
    hidden = (gate_live[:, None] * (live_feats.astype(jnp.float32) + jax.nn.silu(preact))).astype(
        jnp.bfloat16
    )
    member_rows = membership[0, 0].astype(jnp.bfloat16)
    member_count = jnp.sum(membership[0, 0], axis=1).astype(jnp.float32)[:, None]
    pooled = jnp.dot(member_rows, hidden, preferred_element_type=jnp.float32) / (member_count + 1.0)
    normed, rscale = rms_forward(pooled)
    token_live = (jnp.arange(NT) < tok_count[0, 0]).astype(jnp.float32)[:, None]
    tokens = (token_live * normed).astype(jnp.bfloat16)

    tokens_all = gather_tiles(tokens, "col").reshape(-1, H)
    w_qkv = jnp.concatenate([w_query, w_key, w_value], axis=1)
    qkv_all = project(tokens_all, w_qkv)
    query_all = qkv_all[:, :H]
    key_all = qkv_all[:, H:2 * H]
    value_all = qkv_all[:, 2 * H:]
    qkv_own = project(tokens, w_qkv)
    query_own = qkv_own[:, :H]
    key_own = qkv_own[:, H:2 * H]
    value_own = qkv_own[:, 2 * H:]

    score_w = w_score.astype(jnp.float32)
    loss_weight = 1.0 / math.sqrt(lax.axis_size("row") * lax.axis_size("col") * NT)
    grad_value = token_live[:, 0] * cotangent[0, 0] * loss_weight
    attended, mixed, grad_proj, grad_attn_copies = attend_fwd(
        query_own, key_all, value_all, tokens, grad_value[:, None], w_score, w_out,
        lax.axis_size("col"),
    )
    value_out = token_live[:, 0] * jnp.sum(mixed * score_w, axis=1)
    g_score = jnp.sum(mixed * grad_value[:, None], axis=0)
    grad_mixed = grad_value[:, None] * score_w
    g_out = jnp.einsum("nh,ne->he", attended, grad_proj, preferred_element_type=jnp.float32)

    grad_attn_all = lax.all_to_all(grad_attn_copies, "col", 0, 0, tiled=True).reshape(-1, H)

    grad_query = attend_gq(query_own, grad_attn_copies, key_all, value_all)
    grad_key, grad_val = attend_gkv(query_all, grad_attn_all, key_own, value_own)

    g_query = jnp.einsum("nh,ne->he", tokens, grad_query, preferred_element_type=jnp.float32)
    g_key = jnp.einsum("nh,ne->he", tokens, grad_key, preferred_element_type=jnp.float32)
    g_value = jnp.einsum("nh,ne->he", tokens, grad_val, preferred_element_type=jnp.float32)
    grad_tokens = grad_mixed + jnp.dot(grad_query, w_query.T, preferred_element_type=jnp.float32)
    grad_tokens = grad_tokens + jnp.dot(grad_key, w_key.T, preferred_element_type=jnp.float32)
    grad_tokens = grad_tokens + jnp.dot(grad_val, w_value.T, preferred_element_type=jnp.float32)
    grad_pooled = rms_backward(token_live * grad_tokens, normed, rscale)
    grad_scaled = (grad_pooled / (member_count + 1.0)).astype(jnp.bfloat16)
    grad_hidden = jnp.einsum(
        "ng,nh->gh", member_rows, grad_scaled, preferred_element_type=jnp.float32
    )
    grad_pre = (gate_live[:, None] * grad_hidden * silu_grad(preact)).astype(jnp.bfloat16)
    g_msg = jnp.einsum("gh,ge->he", message, grad_pre, preferred_element_type=jnp.float32)

    devices = lax.axis_size("row") * lax.axis_size("col")
    used = 5 * H + 1
    per_device = -(-used * H // (devices * 128))
    grads = [g_msg, g_query, g_key, g_value, g_out, g_score[None]]
    grads.append(jnp.zeros((per_device * devices * 128 // H - used, H), jnp.float32))
    buffer = jnp.concatenate(grads, axis=0).reshape(devices, per_device, 128)
    summed = all_reduce_a2a(buffer, ("row", "col")).reshape(-1, H)
    outs = [summed[i * H:(i + 1) * H] for i in range(5)]
    g_score_sum = summed[5 * H]
    return (value_out[None, None], *outs, g_score_sum)


def solution(mesh):
    placed = (
        P("row", "col", None, None),
        P("row", "col", None, None, None, None),
        P("row", "col"),
        P("row", "col", None, None),
        P("row", "col"),
        P(),
        P(),
        P(),
        P(),
        P(),
        P(),
        P("row", "col", None),
    )
    return jax.shard_map(
        body,
        mesh=mesh,
        in_specs=placed,
        out_specs=(P("row", "col", None), P(), P(), P(), P(), P(), P()),
        check_vma=False,
    )
```

```python
import math

import jax
import jax.numpy as jnp
from jax import lax
from jax.experimental import pallas as pl
from jax.experimental.pallas import tpu as pltpu
from jax.sharding import PartitionSpec as P

H = 256
HEADS = 2
HD = 128
BLK = 128
NB = 8
NT = 512


EPS = 1e-06
SHIFT = math.log(NT)
KB = 1024

def _nt(a, b):
    return lax.dot_general(a, b, (((1,), (1,)), ((), ())), preferred_element_type=jnp.float32)

def _nn(a, b):
    return jnp.dot(a, b, preferred_element_type=jnp.float32)

def _half_tanh(q, k):
    return jnp.tanh(_nt(q, k) * (0.5 / math.sqrt(HD)) - 0.5 * SHIFT)

def _fwd_kernel(q_ref, kv_ref, tok_ref, gval_ref, sw_ref, wo_ref, wot_ref,
                att_ref, mixed_ref, gproj_ref, gattn_ref, acc_ref):
    blocks = kv_ref.shape[0] // KB
    acc_ref[...] = jnp.zeros_like(acc_ref)
    def step(j, carry):
        rows = pl.ds(pl.multiple_of(j * KB, KB), KB)
        for h in range(HEADS):
            cols = slice(h * HD, (h + 1) * HD)
            t = _half_tanh(q_ref[:, cols], kv_ref[rows, cols])
            w = (0.5 * t + 0.5).astype(jnp.bfloat16)
            acc_ref[:, cols] += _nn(w, kv_ref[rows, pl.ds(H + h * HD, HD)])
        return carry
    lax.fori_loop(0, blocks, step, 0)
    attended = acc_ref[...].astype(jnp.bfloat16)
    att_ref[...] = attended
    proj = _nn(attended, wo_ref[...])
    pscale = lax.rsqrt(jnp.mean(proj * proj, axis=-1, keepdims=True) + EPS)
    pnormed = proj * pscale
    mixed_ref[...] = tok_ref[...].astype(jnp.float32) + pnormed
    grad_mixed = gval_ref[...] * sw_ref[...].astype(jnp.float32)
    grad_proj = pscale * (grad_mixed - pnormed * jnp.mean(grad_mixed * pnormed, axis=-1, keepdims=True))
    grad_proj = grad_proj.astype(jnp.bfloat16)
    gproj_ref[...] = grad_proj
    grad_attn = _nn(grad_proj, wot_ref[...]).astype(jnp.bfloat16)
    for c in range(gattn_ref.shape[0]):
        gattn_ref[c] = grad_attn

def _gq_kernel(q_ref, g_ref, kv_ref, o_ref, acc_ref):
    blocks = kv_ref.shape[0] // KB
    acc_ref[...] = jnp.zeros_like(acc_ref)
    def step(j, carry):
        rows = pl.ds(pl.multiple_of(j * KB, KB), KB)
        for h in range(HEADS):
            cols = slice(h * HD, (h + 1) * HD)
            k = kv_ref[rows, cols]
            t = _half_tanh(q_ref[:, cols], k)
            dp = _nt(g_ref[0, :, cols], kv_ref[rows, pl.ds(H + h * HD, HD)])
            ds = (dp * (1.0 - t * t) * (0.25 / math.sqrt(HD))).astype(jnp.bfloat16)
            acc_ref[:, cols] += _nn(ds, k)
        return carry
    lax.fori_loop(0, blocks, step, 0)
    o_ref[...] = acc_ref[...].astype(o_ref.dtype)

def _gkv_kernel(q_ref, g_ref, k_ref, v_ref, dk_ref, dv_ref, acck_ref, accv_ref):
    blocks = q_ref.shape[0] // KB
    acck_ref[...] = jnp.zeros_like(acck_ref)
    accv_ref[...] = jnp.zeros_like(accv_ref)
    def step(i, carry):
        rows = pl.ds(pl.multiple_of(i * KB, KB), KB)
        for h in range(HEADS):
            cols = slice(h * HD, (h + 1) * HD)
            q = q_ref[rows, cols]
            g = g_ref[rows, cols]
            t = _half_tanh(k_ref[:, cols], q)
            w = (0.5 * t + 0.5).astype(jnp.bfloat16)
            dp = _nt(v_ref[:, cols], g)
            ds = (dp * (1.0 - t * t) * (0.25 / math.sqrt(HD))).astype(jnp.bfloat16)
            acck_ref[:, cols] += _nn(ds, q)
            accv_ref[:, cols] += _nn(w, g)
        return carry
    lax.fori_loop(0, blocks, step, 0)
    dk_ref[...] = acck_ref[...].astype(dk_ref.dtype)
    dv_ref[...] = accv_ref[...].astype(dv_ref.dtype)

def attend_fwd(q, kv_all, tokens, grad_value, w_score, w_out, copies):
    bf16, f32 = jnp.bfloat16, jnp.float32
    outs = (jax.ShapeDtypeStruct(q.shape, bf16), jax.ShapeDtypeStruct(q.shape, f32),
            jax.ShapeDtypeStruct(q.shape, bf16), jax.ShapeDtypeStruct((copies,) + q.shape, bf16))
    return pl.pallas_call(_fwd_kernel, out_shape=outs,
        scratch_shapes=[pltpu.VMEM(q.shape, f32)])(
            q, kv_all, tokens, grad_value, w_score.reshape(1, -1), w_out, w_out.T)

def attend_gq(q, g, kv_all):
    return pl.pallas_call(_gq_kernel, out_shape=jax.ShapeDtypeStruct(q.shape, jnp.bfloat16),
        scratch_shapes=[pltpu.VMEM(q.shape, jnp.float32)])(q, g, kv_all)

def attend_gkv(q_all, g_all, k, v):
    sh = jax.ShapeDtypeStruct(k.shape, jnp.bfloat16)
    return pl.pallas_call(_gkv_kernel, out_shape=(sh, sh),
        scratch_shapes=[pltpu.VMEM(k.shape, jnp.float32), pltpu.VMEM(k.shape, jnp.float32)],)(q_all, g_all, k, v)


def from_neighbour(array, axis, step):
    size = lax.axis_size(axis)
    pairs = [(i, i + step) for i in range(size) if 0 <= i + step < size]
    return lax.ppermute(array, axis, pairs)


def gather_tiles(rows_in, axis):
    size = lax.axis_size(axis)
    copies = jnp.broadcast_to(rows_in[None], (size,) + rows_in.shape)
    return lax.all_to_all(copies, axis, 0, 0, tiled=True)


def all_reduce_a2a(rows_in, axes):
    size = 1
    for axis in axes:
        size *= lax.axis_size(axis)
    if rows_in.shape[0] != size:
        rows_in = rows_in.reshape(size, -1, rows_in.shape[-1])
    chunks = lax.all_to_all(rows_in, axes, 0, 0, tiled=True)
    total = jnp.sum(chunks, axis=0, keepdims=True).astype(jnp.bfloat16)
    copies = jnp.broadcast_to(total, chunks.shape)
    return lax.all_to_all(copies, axes, 0, 0, tiled=True).astype(jnp.float32)


def silu_grad(preact):
    sigmoid_val = jax.nn.sigmoid(preact)
    return sigmoid_val * (1.0 + preact * (1.0 - sigmoid_val))


def rms_forward(values_in):
    rscale = lax.rsqrt(jnp.mean(values_in * values_in, axis=-1, keepdims=True) + EPS)
    return (values_in * rscale, rscale)


def rms_backward(grad_in, normed, rscale):
    return rscale * (grad_in - normed * jnp.mean(grad_in * normed, axis=-1, keepdims=True))


def split_heads(rows_in):
    return rows_in.reshape(rows_in.shape[0], HEADS, HD)


def score_probs(query_rows, key_rows):
    scores = jnp.einsum(
        "qhd,khd->hqk",
        split_heads(query_rows),
        split_heads(key_rows),
        preferred_element_type=jnp.float32,
    )
    return jax.nn.sigmoid(scores / math.sqrt(HD) - math.log(NT))


def project(rows_in, weight_mat):
    return jnp.dot(rows_in, weight_mat, preferred_element_type=jnp.float32).astype(jnp.bfloat16)


def body(
    gate_feats,
    adjacency,
    gate_count,
    membership,
    tok_count,
    w_msg,
    w_query,
    w_key,
    w_value,
    w_out,
    w_score,
    cotangent,
):
    gate_total = gate_feats.shape[2]
    gate_live = (jnp.arange(gate_total) < gate_count[0, 0]).astype(jnp.float32)
    live_feats = (gate_feats[0, 0].astype(jnp.float32) * gate_live[:, None]).astype(jnp.bfloat16)
    sources = (
        live_feats,
        from_neighbour(live_feats, "row", 1),
        from_neighbour(live_feats, "row", -1),
        from_neighbour(live_feats, "col", 1),
        from_neighbour(live_feats, "col", -1),
    )
    adj_tiles = adjacency[0, 0]
    aggregate = sum(
        jnp.einsum(
            "bij,bjh->bih",
            adj_tiles[:, k].astype(jnp.bfloat16),
            src.reshape(NB, BLK, H),
            preferred_element_type=jnp.float32,
        )
        for k, src in enumerate(sources)
    )
    degree = jnp.sum(adj_tiles, axis=(1, 3)).astype(jnp.float32)
    message = (aggregate / (degree[:, :, None] + 1.0)).astype(jnp.bfloat16).reshape(gate_total, H)
    preact = jnp.dot(message, w_msg, preferred_element_type=jnp.float32)
    hidden = (gate_live[:, None] * (live_feats.astype(jnp.float32) + jax.nn.silu(preact))).astype(
        jnp.bfloat16
    )
    member_rows = membership[0, 0].astype(jnp.bfloat16)
    member_count = jnp.sum(membership[0, 0], axis=1).astype(jnp.float32)[:, None]
    pooled = jnp.dot(member_rows, hidden, preferred_element_type=jnp.float32) / (member_count + 1.0)
    normed, rscale = rms_forward(pooled)
    token_live = (jnp.arange(NT) < tok_count[0, 0]).astype(jnp.float32)[:, None]
    tokens = (token_live * normed).astype(jnp.bfloat16)

    tokens_all = gather_tiles(tokens, "col").reshape(-1, H)
    w_kv = jnp.concatenate([w_key, w_value], axis=1)
    kv_all = project(tokens_all, w_kv)
    query_all = project(tokens_all, w_query)
    w_qkv = jnp.concatenate([w_query, w_kv], axis=1)
    qkv_own = project(tokens, w_qkv)
    query_own = qkv_own[:, :H]
    key_own = qkv_own[:, H:2 * H]
    value_own = qkv_own[:, 2 * H:]

    score_w = w_score.astype(jnp.float32)
    loss_weight = 1.0 / math.sqrt(lax.axis_size("row") * lax.axis_size("col") * NT)
    grad_value = token_live[:, 0] * cotangent[0, 0] * loss_weight
    attended, mixed, grad_proj, grad_attn_copies = attend_fwd(
        query_own, kv_all, tokens, grad_value[:, None], w_score, w_out,
        lax.axis_size("col"),
    )
    value_out = token_live[:, 0] * jnp.sum(mixed * score_w, axis=1)
    g_score = jnp.sum(mixed * grad_value[:, None], axis=0)
    grad_mixed = grad_value[:, None] * score_w
    g_out = jnp.einsum("nh,ne->he", attended, grad_proj, preferred_element_type=jnp.float32)

    grad_attn_all = lax.all_to_all(grad_attn_copies, "col", 0, 0, tiled=True).reshape(-1, H)

    grad_query = attend_gq(query_own, grad_attn_copies, kv_all)
    grad_key, grad_val = attend_gkv(query_all, grad_attn_all, key_own, value_own)

    g_query = jnp.einsum("nh,ne->he", tokens, grad_query, preferred_element_type=jnp.float32)
    g_key = jnp.einsum("nh,ne->he", tokens, grad_key, preferred_element_type=jnp.float32)
    g_value = jnp.einsum("nh,ne->he", tokens, grad_val, preferred_element_type=jnp.float32)
    grad_tokens = grad_mixed + jnp.dot(grad_query, w_query.T, preferred_element_type=jnp.float32)
    grad_tokens = grad_tokens + jnp.dot(grad_key, w_key.T, preferred_element_type=jnp.float32)
    grad_tokens = grad_tokens + jnp.dot(grad_val, w_value.T, preferred_element_type=jnp.float32)
    grad_pooled = rms_backward(token_live * grad_tokens, normed, rscale)
    grad_scaled = (grad_pooled / (member_count + 1.0)).astype(jnp.bfloat16)
    grad_hidden = jnp.einsum(
        "ng,nh->gh", member_rows, grad_scaled, preferred_element_type=jnp.float32
    )
    grad_pre = (gate_live[:, None] * grad_hidden * silu_grad(preact)).astype(jnp.bfloat16)
    g_msg = jnp.einsum("gh,ge->he", message, grad_pre, preferred_element_type=jnp.float32)

    devices = lax.axis_size("row") * lax.axis_size("col")
    used = 5 * H + 1
    per_device = -(-used * H // (devices * 128))
    grads = [g_msg, g_query, g_key, g_value, g_out, g_score[None]]
    grads.append(jnp.zeros((per_device * devices * 128 // H - used, H), jnp.float32))
    buffer = jnp.concatenate(grads, axis=0).reshape(devices, per_device, 128)
    summed = all_reduce_a2a(buffer, ("row", "col")).reshape(-1, H)
    outs = [summed[i * H:(i + 1) * H] for i in range(5)]
    g_score_sum = summed[5 * H]
    return (value_out[None, None], *outs, g_score_sum)


def solution(mesh):
    placed = (
        P("row", "col", None, None),
        P("row", "col", None, None, None, None),
        P("row", "col"),
        P("row", "col", None, None),
        P("row", "col"),
        P(),
        P(),
        P(),
        P(),
        P(),
        P(),
        P("row", "col", None),
    )
    return jax.shard_map(
        body,
        mesh=mesh,
        in_specs=placed,
        out_specs=(P("row", "col", None), P(), P(), P(), P(), P(), P()),
        check_vma=False,
    )
```

```python
import math

import jax
import jax.numpy as jnp
from jax import lax
from jax.experimental import pallas as pl
from jax.experimental.pallas import tpu as pltpu
from jax.sharding import PartitionSpec as P

H = 256
HEADS = 2
HD = 128
BLK = 128
NB = 8
NT = 512


EPS = 1e-06
SHIFT = math.log(NT)
KB = 2048

def _nt(a, b):
    return lax.dot_general(a, b, (((1,), (1,)), ((), ())), preferred_element_type=jnp.float32)

def _nn(a, b):
    return jnp.dot(a, b, preferred_element_type=jnp.float32)

def _half_tanh(q, k):
    return jnp.tanh(_nt(q, k) * (0.5 / math.sqrt(HD)) - 0.5 * SHIFT)

def _fwd_kernel(q_ref, kv_ref, tok_ref, gval_ref, sw_ref, wo_ref, wot_ref,
                att_ref, mixed_ref, gproj_ref, gattn_ref, acc_ref):
    blocks = kv_ref.shape[0] // KB
    acc_ref[...] = jnp.zeros_like(acc_ref)
    def step(j, carry):
        rows = pl.ds(pl.multiple_of(j * KB, KB), KB)
        for h in range(HEADS):
            cols = slice(h * HD, (h + 1) * HD)
            t = _half_tanh(q_ref[:, cols], kv_ref[rows, cols])
            w = (0.5 * t + 0.5).astype(jnp.bfloat16)
            acc_ref[:, cols] += _nn(w, kv_ref[rows, pl.ds(H + h * HD, HD)])
        return carry
    lax.fori_loop(0, blocks, step, 0)
    attended = acc_ref[...].astype(jnp.bfloat16)
    att_ref[...] = attended
    proj = _nn(attended, wo_ref[...])
    pscale = lax.rsqrt(jnp.mean(proj * proj, axis=-1, keepdims=True) + EPS)
    pnormed = proj * pscale
    mixed_ref[...] = tok_ref[...].astype(jnp.float32) + pnormed
    grad_mixed = gval_ref[...] * sw_ref[...].astype(jnp.float32)
    grad_proj = pscale * (grad_mixed - pnormed * jnp.mean(grad_mixed * pnormed, axis=-1, keepdims=True))
    grad_proj = grad_proj.astype(jnp.bfloat16)
    gproj_ref[...] = grad_proj
    grad_attn = _nn(grad_proj, wot_ref[...]).astype(jnp.bfloat16)
    for c in range(gattn_ref.shape[0]):
        gattn_ref[c] = grad_attn

def _gq_kernel(q_ref, g_ref, kv_ref, o_ref, acc_ref):
    blocks = kv_ref.shape[0] // KB
    acc_ref[...] = jnp.zeros_like(acc_ref)
    def step(j, carry):
        rows = pl.ds(pl.multiple_of(j * KB, KB), KB)
        for h in range(HEADS):
            cols = slice(h * HD, (h + 1) * HD)
            k = kv_ref[rows, cols]
            t = _half_tanh(q_ref[:, cols], k)
            dp = _nt(g_ref[0, :, cols], kv_ref[rows, pl.ds(H + h * HD, HD)])
            ds = (dp * (1.0 - t * t) * (0.25 / math.sqrt(HD))).astype(jnp.bfloat16)
            acc_ref[:, cols] += _nn(ds, k)
        return carry
    lax.fori_loop(0, blocks, step, 0)
    o_ref[...] = acc_ref[...].astype(o_ref.dtype)

def _gkv_kernel(q_ref, g_ref, k_ref, v_ref, dk_ref, dv_ref, acck_ref, accv_ref):
    blocks = q_ref.shape[0] // KB
    acck_ref[...] = jnp.zeros_like(acck_ref)
    accv_ref[...] = jnp.zeros_like(accv_ref)
    def step(i, carry):
        rows = pl.ds(pl.multiple_of(i * KB, KB), KB)
        for h in range(HEADS):
            cols = slice(h * HD, (h + 1) * HD)
            q = q_ref[rows, cols]
            g = g_ref[rows, cols]
            t = _half_tanh(k_ref[:, cols], q)
            w = (0.5 * t + 0.5).astype(jnp.bfloat16)
            dp = _nt(v_ref[:, cols], g)
            ds = (dp * (1.0 - t * t) * (0.25 / math.sqrt(HD))).astype(jnp.bfloat16)
            acck_ref[:, cols] += _nn(ds, q)
            accv_ref[:, cols] += _nn(w, g)
        return carry
    lax.fori_loop(0, blocks, step, 0)
    dk_ref[...] = acck_ref[...].astype(dk_ref.dtype)
    dv_ref[...] = accv_ref[...].astype(dv_ref.dtype)

def attend_fwd(q, kv_all, tokens, grad_value, w_score, w_out, copies):
    bf16, f32 = jnp.bfloat16, jnp.float32
    outs = (jax.ShapeDtypeStruct(q.shape, bf16), jax.ShapeDtypeStruct(q.shape, f32),
            jax.ShapeDtypeStruct(q.shape, bf16), jax.ShapeDtypeStruct((copies,) + q.shape, bf16))
    return pl.pallas_call(_fwd_kernel, out_shape=outs,
        scratch_shapes=[pltpu.VMEM(q.shape, f32)])(
            q, kv_all, tokens, grad_value, w_score.reshape(1, -1), w_out, w_out.T)

def attend_gq(q, g, kv_all):
    return pl.pallas_call(_gq_kernel, out_shape=jax.ShapeDtypeStruct(q.shape, jnp.bfloat16),
        scratch_shapes=[pltpu.VMEM(q.shape, jnp.float32)])(q, g, kv_all)

def attend_gkv(q_all, g_all, k, v):
    sh = jax.ShapeDtypeStruct(k.shape, jnp.bfloat16)
    return pl.pallas_call(_gkv_kernel, out_shape=(sh, sh),
        scratch_shapes=[pltpu.VMEM(k.shape, jnp.float32), pltpu.VMEM(k.shape, jnp.float32)],)(q_all, g_all, k, v)


def from_neighbour(array, axis, step):
    size = lax.axis_size(axis)
    pairs = [(i, i + step) for i in range(size) if 0 <= i + step < size]
    return lax.ppermute(array, axis, pairs)


def gather_tiles(rows_in, axis):
    size = lax.axis_size(axis)
    copies = jnp.broadcast_to(rows_in[None], (size,) + rows_in.shape)
    return lax.all_to_all(copies, axis, 0, 0, tiled=True)


def all_reduce_a2a(rows_in, axes):
    size = 1
    for axis in axes:
        size *= lax.axis_size(axis)
    if rows_in.shape[0] != size:
        rows_in = rows_in.reshape(size, -1, rows_in.shape[-1])
    chunks = lax.all_to_all(rows_in, axes, 0, 0, tiled=True)
    total = jnp.sum(chunks, axis=0, keepdims=True).astype(jnp.bfloat16)
    copies = jnp.broadcast_to(total, chunks.shape)
    return lax.all_to_all(copies, axes, 0, 0, tiled=True).astype(jnp.float32)


def silu_grad(preact):
    sigmoid_val = jax.nn.sigmoid(preact)
    return sigmoid_val * (1.0 + preact * (1.0 - sigmoid_val))


def rms_forward(values_in):
    rscale = lax.rsqrt(jnp.mean(values_in * values_in, axis=-1, keepdims=True) + EPS)
    return (values_in * rscale, rscale)


def rms_backward(grad_in, normed, rscale):
    return rscale * (grad_in - normed * jnp.mean(grad_in * normed, axis=-1, keepdims=True))


def split_heads(rows_in):
    return rows_in.reshape(rows_in.shape[0], HEADS, HD)


def score_probs(query_rows, key_rows):
    scores = jnp.einsum(
        "qhd,khd->hqk",
        split_heads(query_rows),
        split_heads(key_rows),
        preferred_element_type=jnp.float32,
    )
    return jax.nn.sigmoid(scores / math.sqrt(HD) - math.log(NT))


def project(rows_in, weight_mat):
    return jnp.dot(rows_in, weight_mat, preferred_element_type=jnp.float32).astype(jnp.bfloat16)


def body(
    gate_feats,
    adjacency,
    gate_count,
    membership,
    tok_count,
    w_msg,
    w_query,
    w_key,
    w_value,
    w_out,
    w_score,
    cotangent,
):
    gate_total = gate_feats.shape[2]
    gate_live = (jnp.arange(gate_total) < gate_count[0, 0]).astype(jnp.float32)
    live_feats = (gate_feats[0, 0].astype(jnp.float32) * gate_live[:, None]).astype(jnp.bfloat16)
    sources = (
        live_feats,
        from_neighbour(live_feats, "row", 1),
        from_neighbour(live_feats, "row", -1),
        from_neighbour(live_feats, "col", 1),
        from_neighbour(live_feats, "col", -1),
    )
    adj_tiles = adjacency[0, 0]
    aggregate = sum(
        jnp.einsum(
            "bij,bjh->bih",
            adj_tiles[:, k].astype(jnp.bfloat16),
            src.reshape(NB, BLK, H),
            preferred_element_type=jnp.float32,
        )
        for k, src in enumerate(sources)
    )
    degree = jnp.sum(adj_tiles, axis=(1, 3)).astype(jnp.float32)
    message = (aggregate / (degree[:, :, None] + 1.0)).astype(jnp.bfloat16).reshape(gate_total, H)
    preact = jnp.dot(message, w_msg, preferred_element_type=jnp.float32)
    hidden = (gate_live[:, None] * (live_feats.astype(jnp.float32) + jax.nn.silu(preact))).astype(
        jnp.bfloat16
    )
    member_rows = membership[0, 0].astype(jnp.bfloat16)
    member_count = jnp.sum(membership[0, 0], axis=1).astype(jnp.float32)[:, None]
    pooled = jnp.dot(member_rows, hidden, preferred_element_type=jnp.float32) / (member_count + 1.0)
    normed, rscale = rms_forward(pooled)
    token_live = (jnp.arange(NT) < tok_count[0, 0]).astype(jnp.float32)[:, None]
    tokens = (token_live * normed).astype(jnp.bfloat16)

    tokens_all = gather_tiles(tokens, "col").reshape(-1, H)
    w_kv = jnp.concatenate([w_key, w_value], axis=1)
    kv_all = project(tokens_all, w_kv)
    query_all = project(tokens_all, w_query)
    w_qkv = jnp.concatenate([w_query, w_kv], axis=1)
    qkv_own = project(tokens, w_qkv)
    query_own = qkv_own[:, :H]
    key_own = qkv_own[:, H:2 * H]
    value_own = qkv_own[:, 2 * H:]

    score_w = w_score.astype(jnp.float32)
    loss_weight = 1.0 / math.sqrt(lax.axis_size("row") * lax.axis_size("col") * NT)
    grad_value = token_live[:, 0] * cotangent[0, 0] * loss_weight
    attended, mixed, grad_proj, grad_attn_copies = attend_fwd(
        query_own, kv_all, tokens, grad_value[:, None], w_score, w_out,
        lax.axis_size("col"),
    )
    value_out = token_live[:, 0] * jnp.sum(mixed * score_w, axis=1)
    g_score = jnp.sum(mixed * grad_value[:, None], axis=0)
    grad_mixed = grad_value[:, None] * score_w
    g_out = jnp.einsum("nh,ne->he", attended, grad_proj, preferred_element_type=jnp.float32)

    grad_attn_all = lax.all_to_all(grad_attn_copies, "col", 0, 0, tiled=True).reshape(-1, H)

    grad_query = attend_gq(query_own, grad_attn_copies, kv_all)
    grad_key, grad_val = attend_gkv(query_all, grad_attn_all, key_own, value_own)

    g_query = jnp.einsum("nh,ne->he", tokens, grad_query, preferred_element_type=jnp.float32)
    g_key = jnp.einsum("nh,ne->he", tokens, grad_key, preferred_element_type=jnp.float32)
    g_value = jnp.einsum("nh,ne->he", tokens, grad_val, preferred_element_type=jnp.float32)
    grad_tokens = grad_mixed + jnp.dot(grad_query, w_query.T, preferred_element_type=jnp.float32)
    grad_tokens = grad_tokens + jnp.dot(grad_key, w_key.T, preferred_element_type=jnp.float32)
    grad_tokens = grad_tokens + jnp.dot(grad_val, w_value.T, preferred_element_type=jnp.float32)
    grad_pooled = rms_backward(token_live * grad_tokens, normed, rscale)
    grad_scaled = (grad_pooled / (member_count + 1.0)).astype(jnp.bfloat16)
    grad_hidden = jnp.einsum(
        "ng,nh->gh", member_rows, grad_scaled, preferred_element_type=jnp.float32
    )
    grad_pre = (gate_live[:, None] * grad_hidden * silu_grad(preact)).astype(jnp.bfloat16)
    g_msg = jnp.einsum("gh,ge->he", message, grad_pre, preferred_element_type=jnp.float32)

    devices = lax.axis_size("row") * lax.axis_size("col")
    used = 5 * H + 1
    per_device = -(-used * H // (devices * 128))
    grads = [g_msg, g_query, g_key, g_value, g_out, g_score[None]]
    grads.append(jnp.zeros((per_device * devices * 128 // H - used, H), jnp.float32))
    buffer = jnp.concatenate(grads, axis=0).reshape(devices, per_device, 128)
    summed = all_reduce_a2a(buffer, ("row", "col")).reshape(-1, H)
    outs = [summed[i * H:(i + 1) * H] for i in range(5)]
    g_score_sum = summed[5 * H]
    return (value_out[None, None], *outs, g_score_sum)


def solution(mesh):
    placed = (
        P("row", "col", None, None),
        P("row", "col", None, None, None, None),
        P("row", "col"),
        P("row", "col", None, None),
        P("row", "col"),
        P(),
        P(),
        P(),
        P(),
        P(),
        P(),
        P("row", "col", None),
    )
    return jax.shard_map(
        body,
        mesh=mesh,
        in_specs=placed,
        out_specs=(P("row", "col", None), P(), P(), P(), P(), P(), P()),
        check_vma=False,
    )
```

```python
import math

import jax
import jax.numpy as jnp
from jax import lax
from jax.experimental import pallas as pl
from jax.experimental.pallas import tpu as pltpu
from jax.sharding import PartitionSpec as P

H = 256
HEADS = 2
HD = 128
BLK = 128
NB = 8
NT = 512


EPS = 1e-06
SHIFT = math.log(NT)
KB = 1024

def _nt(a, b):
    return lax.dot_general(a, b, (((1,), (1,)), ((), ())), preferred_element_type=jnp.float32)

def _nn(a, b):
    return jnp.dot(a, b, preferred_element_type=jnp.float32)

def _half_tanh(q, k):
    return jnp.tanh(_nt(q, k) * (0.5 / math.sqrt(HD)) - 0.5 * SHIFT)

def _fwd_kernel(q_ref, kv_ref, tok_ref, gval_ref, sw_ref, wo_ref, wot_ref,
                att_ref, mixed_ref, gproj_ref, gattn_ref, acc_ref):
    blocks = kv_ref.shape[0] // KB
    acc_ref[...] = jnp.zeros_like(acc_ref)
    def step(j, carry):
        rows = pl.ds(pl.multiple_of(j * KB, KB), KB)
        for h in range(HEADS):
            cols = slice(h * HD, (h + 1) * HD)
            t = _half_tanh(q_ref[:, cols], kv_ref[rows, cols])
            w = (0.5 * t + 0.5).astype(jnp.bfloat16)
            acc_ref[:, cols] += _nn(w, kv_ref[rows, pl.ds(H + h * HD, HD)])
        return carry
    lax.fori_loop(0, blocks, step, 0)
    attended = acc_ref[...].astype(jnp.bfloat16)
    att_ref[...] = attended
    proj = _nn(attended, wo_ref[...])
    pscale = lax.rsqrt(jnp.mean(proj * proj, axis=-1, keepdims=True) + EPS)
    pnormed = proj * pscale
    mixed_ref[...] = tok_ref[...].astype(jnp.float32) + pnormed
    grad_mixed = gval_ref[...] * sw_ref[...].astype(jnp.float32)
    grad_proj = pscale * (grad_mixed - pnormed * jnp.mean(grad_mixed * pnormed, axis=-1, keepdims=True))
    grad_proj = grad_proj.astype(jnp.bfloat16)
    gproj_ref[...] = grad_proj
    grad_attn = _nn(grad_proj, wot_ref[...]).astype(jnp.bfloat16)
    for c in range(gattn_ref.shape[0]):
        gattn_ref[c] = grad_attn

def _gq_kernel(q_ref, g_ref, kv_ref, o_ref, acc_ref):
    blocks = kv_ref.shape[0] // KB
    acc_ref[...] = jnp.zeros_like(acc_ref)
    def step(j, carry):
        rows = pl.ds(pl.multiple_of(j * KB, KB), KB)
        for h in range(HEADS):
            cols = slice(h * HD, (h + 1) * HD)
            k = kv_ref[rows, cols]
            t = _half_tanh(q_ref[:, cols], k)
            dp = _nt(g_ref[0, :, cols], kv_ref[rows, pl.ds(H + h * HD, HD)])
            ds = (dp * (1.0 - t * t) * (0.25 / math.sqrt(HD))).astype(jnp.bfloat16)
            acc_ref[:, cols] += _nn(ds, k)
        return carry
    lax.fori_loop(0, blocks, step, 0)
    o_ref[...] = acc_ref[...].astype(o_ref.dtype)

def _gkv_kernel(q_ref, g_ref, k_ref, v_ref, tt_ref, dk_ref, dv_ref, gk_ref, gv_ref, acck_ref, accv_ref):
    blocks = q_ref.shape[0] // KB
    acck_ref[...] = jnp.zeros_like(acck_ref)
    accv_ref[...] = jnp.zeros_like(accv_ref)
    def step(i, carry):
        rows = pl.ds(pl.multiple_of(i * KB, KB), KB)
        for h in range(HEADS):
            cols = slice(h * HD, (h + 1) * HD)
            q = q_ref[rows, cols]
            g = g_ref[rows, cols]
            t = _half_tanh(k_ref[:, cols], q)
            w = (0.5 * t + 0.5).astype(jnp.bfloat16)
            dp = _nt(v_ref[:, cols], g)
            ds = (dp * (1.0 - t * t) * (0.25 / math.sqrt(HD))).astype(jnp.bfloat16)
            acck_ref[:, cols] += _nn(ds, q)
            accv_ref[:, cols] += _nn(w, g)
        return carry
    lax.fori_loop(0, blocks, step, 0)
    grad_key = acck_ref[...].astype(jnp.bfloat16)
    grad_val = accv_ref[...].astype(jnp.bfloat16)
    dk_ref[...] = grad_key
    dv_ref[...] = grad_val
    gk_ref[...] = _nn(tt_ref[...], grad_key)
    gv_ref[...] = _nn(tt_ref[...], grad_val)

def attend_fwd(q, kv_all, tokens, grad_value, w_score, w_out, copies):
    bf16, f32 = jnp.bfloat16, jnp.float32
    outs = (jax.ShapeDtypeStruct(q.shape, bf16), jax.ShapeDtypeStruct(q.shape, f32),
            jax.ShapeDtypeStruct(q.shape, bf16), jax.ShapeDtypeStruct((copies,) + q.shape, bf16))
    return pl.pallas_call(_fwd_kernel, out_shape=outs,
        scratch_shapes=[pltpu.VMEM(q.shape, f32)])(
            q, kv_all, tokens, grad_value, w_score.reshape(1, -1), w_out, w_out.T)

def attend_gq(q, g, kv_all):
    return pl.pallas_call(_gq_kernel, out_shape=jax.ShapeDtypeStruct(q.shape, jnp.bfloat16),
        scratch_shapes=[pltpu.VMEM(q.shape, jnp.float32)])(q, g, kv_all)

def attend_gkv(q_all, g_all, k, v, tokens_t):
    sh = jax.ShapeDtypeStruct(k.shape, jnp.bfloat16)
    gw = jax.ShapeDtypeStruct((H, H), jnp.float32)
    return pl.pallas_call(_gkv_kernel, out_shape=(sh, sh, gw, gw),
        scratch_shapes=[pltpu.VMEM(k.shape, jnp.float32), pltpu.VMEM(k.shape, jnp.float32)],
        )(q_all, g_all, k, v, tokens_t)


def from_neighbour(array, axis, step):
    size = lax.axis_size(axis)
    pairs = [(i, i + step) for i in range(size) if 0 <= i + step < size]
    return lax.ppermute(array, axis, pairs)


def gather_tiles(rows_in, axis):
    size = lax.axis_size(axis)
    copies = jnp.broadcast_to(rows_in[None], (size,) + rows_in.shape)
    return lax.all_to_all(copies, axis, 0, 0, tiled=True)


def all_reduce_a2a(rows_in, axes):
    size = 1
    for axis in axes:
        size *= lax.axis_size(axis)
    if rows_in.shape[0] != size:
        rows_in = rows_in.reshape(size, -1, rows_in.shape[-1])
    chunks = lax.all_to_all(rows_in, axes, 0, 0, tiled=True)
    total = jnp.sum(chunks, axis=0, keepdims=True).astype(jnp.bfloat16)
    copies = jnp.broadcast_to(total, chunks.shape)
    return lax.all_to_all(copies, axes, 0, 0, tiled=True).astype(jnp.float32)


def silu_grad(preact):
    sigmoid_val = jax.nn.sigmoid(preact)
    return sigmoid_val * (1.0 + preact * (1.0 - sigmoid_val))


def rms_forward(values_in):
    rscale = lax.rsqrt(jnp.mean(values_in * values_in, axis=-1, keepdims=True) + EPS)
    return (values_in * rscale, rscale)


def rms_backward(grad_in, normed, rscale):
    return rscale * (grad_in - normed * jnp.mean(grad_in * normed, axis=-1, keepdims=True))


def split_heads(rows_in):
    return rows_in.reshape(rows_in.shape[0], HEADS, HD)


def score_probs(query_rows, key_rows):
    scores = jnp.einsum(
        "qhd,khd->hqk",
        split_heads(query_rows),
        split_heads(key_rows),
        preferred_element_type=jnp.float32,
    )
    return jax.nn.sigmoid(scores / math.sqrt(HD) - math.log(NT))


def project(rows_in, weight_mat):
    return jnp.dot(rows_in, weight_mat, preferred_element_type=jnp.float32).astype(jnp.bfloat16)


def body(
    gate_feats,
    adjacency,
    gate_count,
    membership,
    tok_count,
    w_msg,
    w_query,
    w_key,
    w_value,
    w_out,
    w_score,
    cotangent,
):
    gate_total = gate_feats.shape[2]
    gate_live = (jnp.arange(gate_total) < gate_count[0, 0]).astype(jnp.float32)
    live_feats = (gate_feats[0, 0].astype(jnp.float32) * gate_live[:, None]).astype(jnp.bfloat16)
    sources = (
        live_feats,
        from_neighbour(live_feats, "row", 1),
        from_neighbour(live_feats, "row", -1),
        from_neighbour(live_feats, "col", 1),
        from_neighbour(live_feats, "col", -1),
    )
    adj_tiles = adjacency[0, 0]
    aggregate = sum(
        jnp.einsum(
            "bij,bjh->bih",
            adj_tiles[:, k].astype(jnp.bfloat16),
            src.reshape(NB, BLK, H),
            preferred_element_type=jnp.float32,
        )
        for k, src in enumerate(sources)
    )
    degree = jnp.sum(adj_tiles, axis=(1, 3)).astype(jnp.float32)
    message = (aggregate / (degree[:, :, None] + 1.0)).astype(jnp.bfloat16).reshape(gate_total, H)
    preact = jnp.dot(message, w_msg, preferred_element_type=jnp.float32)
    hidden = (gate_live[:, None] * (live_feats.astype(jnp.float32) + jax.nn.silu(preact))).astype(
        jnp.bfloat16
    )
    member_rows = membership[0, 0].astype(jnp.bfloat16)
    member_count = jnp.sum(membership[0, 0], axis=1).astype(jnp.float32)[:, None]
    pooled = jnp.dot(member_rows, hidden, preferred_element_type=jnp.float32) / (member_count + 1.0)
    normed, rscale = rms_forward(pooled)
    token_live = (jnp.arange(NT) < tok_count[0, 0]).astype(jnp.float32)[:, None]
    tokens = (token_live * normed).astype(jnp.bfloat16)

    tokens_all = gather_tiles(tokens, "col").reshape(-1, H)
    w_kv = jnp.concatenate([w_key, w_value], axis=1)
    kv_all = project(tokens_all, w_kv)
    query_all = project(tokens_all, w_query)
    w_qkv = jnp.concatenate([w_query, w_kv], axis=1)
    qkv_own = project(tokens, w_qkv)
    query_own = qkv_own[:, :H]
    key_own = qkv_own[:, H:2 * H]
    value_own = qkv_own[:, 2 * H:]

    score_w = w_score.astype(jnp.float32)
    loss_weight = 1.0 / math.sqrt(lax.axis_size("row") * lax.axis_size("col") * NT)
    grad_value = token_live[:, 0] * cotangent[0, 0] * loss_weight
    attended, mixed, grad_proj, grad_attn_copies = attend_fwd(
        query_own, kv_all, tokens, grad_value[:, None], w_score, w_out,
        lax.axis_size("col"),
    )
    value_out = token_live[:, 0] * jnp.sum(mixed * score_w, axis=1)
    g_score = jnp.sum(mixed * grad_value[:, None], axis=0)
    grad_mixed = grad_value[:, None] * score_w
    g_out = jnp.einsum("nh,ne->he", attended, grad_proj, preferred_element_type=jnp.float32)

    grad_attn_all = lax.all_to_all(grad_attn_copies, "col", 0, 0, tiled=True).reshape(-1, H)

    grad_query = attend_gq(query_own, grad_attn_copies, kv_all)
    grad_key, grad_val, g_key, g_value = attend_gkv(
        query_all, grad_attn_all, key_own, value_own, tokens.T
    )

    g_query = jnp.einsum("nh,ne->he", tokens, grad_query, preferred_element_type=jnp.float32)
    grad_tokens = grad_mixed + jnp.dot(grad_query, w_query.T, preferred_element_type=jnp.float32)
    grad_tokens = grad_tokens + jnp.dot(grad_key, w_key.T, preferred_element_type=jnp.float32)
    grad_tokens = grad_tokens + jnp.dot(grad_val, w_value.T, preferred_element_type=jnp.float32)
    grad_pooled = rms_backward(token_live * grad_tokens, normed, rscale)
    grad_scaled = (grad_pooled / (member_count + 1.0)).astype(jnp.bfloat16)
    grad_hidden = jnp.einsum(
        "ng,nh->gh", member_rows, grad_scaled, preferred_element_type=jnp.float32
    )
    grad_pre = (gate_live[:, None] * grad_hidden * silu_grad(preact)).astype(jnp.bfloat16)
    g_msg = jnp.einsum("gh,ge->he", message, grad_pre, preferred_element_type=jnp.float32)

    devices = lax.axis_size("row") * lax.axis_size("col")
    used = 5 * H + 1
    per_device = -(-used * H // (devices * 128))
    grads = [g_msg, g_query, g_key, g_value, g_out, g_score[None]]
    grads.append(jnp.zeros((per_device * devices * 128 // H - used, H), jnp.float32))
    buffer = jnp.concatenate(grads, axis=0).reshape(devices, per_device, 128)
    summed = all_reduce_a2a(buffer, ("row", "col")).reshape(-1, H)
    outs = [summed[i * H:(i + 1) * H] for i in range(5)]
    g_score_sum = summed[5 * H]
    return (value_out[None, None], *outs, g_score_sum)


def solution(mesh):
    placed = (
        P("row", "col", None, None),
        P("row", "col", None, None, None, None),
        P("row", "col"),
        P("row", "col", None, None),
        P("row", "col"),
        P(),
        P(),
        P(),
        P(),
        P(),
        P(),
        P("row", "col", None),
    )
    return jax.shard_map(
        body,
        mesh=mesh,
        in_specs=placed,
        out_specs=(P("row", "col", None), P(), P(), P(), P(), P(), P()),
        check_vma=False,
    )
```
